128 devices in a mesh: seq: 32 (over y, x, core), head: 4 (over z).
Axes of the slice: x: 4, y: 4, z: 4, core: 2. Of those that a mesh axis runs over, the one named last changes fastest.
Arguments:
- queries: bfloat16 [8192, 4096], P(('seq', 'head')), may hold values from -8 to 8
- keys: bfloat16 [8192, 1024], P(('seq', 'head')), may hold values from -8 to 8
- values: bfloat16 [8192, 1024], P(('seq', 'head')), may hold values from -6 to 6
- slash: int32 [8, 4], replicated, may hold values from 0 to 3, all different within a row
- vertical: int32 [8, 32], replicated, may hold values from 0 to 127, as said below
Outputs:
- attended: bfloat16 [8192, 4096], P('seq', 'head')
The draws below stay inside these ranges and needn't reach their ends.
Inputs may be any that keep to these rules, and one draw needn't show every extreme that they name: `slash`: each row holds 4 different values. `vertical`: each row names 32 different blocks; at most 2 of them lie in one range of 4 blocks k * 4 to (k + 1) * 4 - 1, and every row has exactly 2 in some such range.
All inputs are finite; a program needn't handle non-finite values.
Results may differ from the reference program's by a relative error of at most 0.0045.
Values may be sent and summed in bfloat16 or wider, within the bound.
No kernel may reach another device: no remote copies, remote signals or barrier semaphores. Data moves between devices by JAX's collectives and lax.ppermute only.
A program may use at most 128 MiB of HBM per device.

```python
import jax
import jax.numpy as jnp
from jax import lax

QUERY_HEADS = 32
KEY_VALUE_HEADS = 8
HEAD_WIDTH = 128
BLOCK_TOKENS = 64
EXTRA_DIAGONALS = 4
VOWN = 2
BLOCKS_PER_INDEX = 4
PROMPT_TOKENS = 8192
PROMPT_BLOCKS = 128
NV = 32


def draw_queries(key, part):
    base_value = jax.random.truncated_normal(jax.random.fold_in(key, 1), -8.0, 8.0, (PROMPT_TOKENS, QUERY_HEADS, HEAD_WIDTH), jnp.float32)
    return base_value.reshape(PROMPT_TOKENS, QUERY_HEADS * HEAD_WIDTH).astype(jnp.bfloat16)


def draw_keys(key, part):
    base_value = jax.random.truncated_normal(jax.random.fold_in(key, 2), -8.0, 8.0, (PROMPT_TOKENS, KEY_VALUE_HEADS, HEAD_WIDTH), jnp.float32)
    return base_value.reshape(PROMPT_TOKENS, KEY_VALUE_HEADS * HEAD_WIDTH).astype(jnp.bfloat16)


def draw_vertical(key, part):
    shards = PROMPT_BLOCKS // BLOCKS_PER_INDEX
    listing = []
    for group_member in range(KEY_VALUE_HEADS):
        sub = jax.random.fold_in(key, 100 + group_member)
        order = jax.random.permutation(jax.random.fold_in(sub, 1), shards * VOWN)
        forced = jax.random.randint(jax.random.fold_in(sub, 2), (), 0, shards)
        candidate = jnp.arange(shards * VOWN)
        ranking = jnp.where(candidate // VOWN == forced, -1 - candidate % VOWN, order)
        chosen = jnp.argsort(ranking, stable=True)[:NV]
        owner = chosen // VOWN
        place = chosen % VOWN
        start = jax.random.randint(jax.random.fold_in(sub, 3), (shards,), 0, BLOCKS_PER_INDEX)
        inner = (start[owner] + place * (BLOCKS_PER_INDEX // VOWN)) % BLOCKS_PER_INDEX
        listing.append(owner * BLOCKS_PER_INDEX + inner)
    return jnp.stack(listing, 0).astype(jnp.int32)


def block_levels(stream_key, shape, cuts, low, top_value):
    def one(dim, parts):
        steps = jax.random.uniform(jax.random.fold_in(jax.random.fold_in(stream_key, 6), dim), (parts,), jnp.float32, low / len(cuts), top_value / len(cuts))
        return jnp.repeat(jnp.exp(steps), shape[dim] // parts).reshape((-1,) + (1,) * (len(shape) - dim - 1))

    factor_of = one(*cuts[0])
    for cut in cuts[1:]:
        factor_of = factor_of * one(*cut)
    return factor_of


def distinct(rng, rows, number_of, top, lift):
    sequence = jax.random.permutation(jax.random.fold_in(rng, 1), number_of)
    favour = sequence
    for power in range(3):
        favour = favour * favour // number_of
    favour = favour * lift // number_of
    tickets = jax.random.randint(jax.random.fold_in(rng, 2), (rows, number_of), 0, 4096) + favour
    sure = jax.random.permutation(jax.random.fold_in(rng, 3), rows)[jnp.arange(number_of) % rows]
    tickets = jnp.where(jnp.arange(rows)[:, None] == sure[None, :], 1 << 14, tickets)
    merit = tickets * number_of + jnp.arange(number_of)
    return lax.top_k(merit.astype(jnp.int32), top)[1].astype(jnp.int32)


def centred(stream_key, extent, scale, reach, cuts=(), kind=jnp.bfloat16):
    entries = scale * jax.random.normal(stream_key, extent, jnp.float32)
    if cuts:
        entries = entries * block_levels(stream_key, extent, cuts, -0.22, 0.18)
    return jnp.clip(entries, -reach, reach).astype(kind)


def setup_inputs(seed: int = 0) -> dict:
    streams_of = jax.random.split(jax.random.key(seed), 6)
    return {
        "queries": draw_queries(jax.random.fold_in(streams_of[5], 71), 0),
        "keys": draw_keys(jax.random.fold_in(streams_of[5], 71), 0),
        "values": centred(streams_of[2], (PROMPT_TOKENS, KEY_VALUE_HEADS * HEAD_WIDTH), 1.0, 6.0, ((0, 128),)),
        "slash": distinct(streams_of[3], KEY_VALUE_HEADS, BLOCKS_PER_INDEX, EXTRA_DIAGONALS, 0),
        "vertical": draw_vertical(jax.random.fold_in(streams_of[5], 71), 0),
    }


def reference(queries, keys, values, slash, vertical):
    softmax_scale = HEAD_WIDTH ** -0.5
    query_group = QUERY_HEADS // KEY_VALUE_HEADS
    qs = queries.reshape(PROMPT_BLOCKS, BLOCK_TOKENS, QUERY_HEADS, HEAD_WIDTH).transpose(2, 0, 1, 3)
    key_split = keys.reshape(PROMPT_BLOCKS, BLOCK_TOKENS, KEY_VALUE_HEADS, HEAD_WIDTH).transpose(2, 0, 1, 3)
    vertical_slash = values.reshape(PROMPT_BLOCKS, BLOCK_TOKENS, KEY_VALUE_HEADS, HEAD_WIDTH).transpose(2, 0, 1, 3)
    diagonal_offsets = jnp.concatenate([jnp.zeros((KEY_VALUE_HEADS, 1), jnp.int32), slash.astype(jnp.int32) + 1], 1)
    blocks = jnp.arange(PROMPT_BLOCKS, dtype=jnp.int32)
    spots = jnp.arange(BLOCK_TOKENS, dtype=jnp.int32)
    causal = spots[None, :] <= spots[:, None]
    later = jnp.arange(EXTRA_DIAGONALS + 1, dtype=jnp.int32) > 0

    def one_head(head):
        kvh = head // query_group
        query_rows = qs[head].astype(jnp.float32)
        key_all = key_split[kvh]
        val_all = vertical_slash[kvh]
        offset = diagonal_offsets[kvh]
        listed = vertical[kvh].astype(jnp.int32)
        slash_blocks = blocks[:, None] - offset[None, :]
        slash_ok = slash_blocks >= 0
        index = jnp.maximum(slash_blocks, 0)
        slash_keys_picked = key_all[index].astype(jnp.float32)
        slash_values_picked = val_all[index].astype(jnp.float32)
        slash_score = jnp.einsum("gxh,gvih->gxvi", query_rows, slash_keys_picked) * softmax_scale
        mask_s = slash_ok[:, None, :, None] & (later[None, None, :, None] | causal[None, :, None, :])
        slash_score = jnp.where(mask_s, slash_score, -jnp.inf)
        vertical_key_rows = key_all[listed].astype(jnp.float32)
        vertical_value_rows = val_all[listed].astype(jnp.float32)
        dist = blocks[:, None] - listed[None, :]
        hit = jnp.any(dist[:, :, None] == offset[None, None, :], axis=2)
        vert_ok = (dist > 0) & jnp.logical_not(hit)
        vertical_score = jnp.einsum("ulo,ezo->ulez", query_rows, vertical_key_rows) * softmax_scale
        vertical_score = jnp.where(vert_ok[:, None, :, None], vertical_score, -jnp.inf)
        top = jnp.maximum(jnp.max(slash_score, axis=(2, 3)), jnp.max(vertical_score, axis=(2, 3)))
        slash_weight = jnp.exp(slash_score - top[:, :, None, None])
        vertical_weight = jnp.exp(vertical_score - top[:, :, None, None])
        total = jnp.sum(slash_weight, axis=(2, 3)) + jnp.sum(vertical_weight, axis=(2, 3))
        slash_rounded = lax.optimization_barrier(slash_weight.astype(jnp.bfloat16)).astype(jnp.float32)
        vertical_rounded = lax.optimization_barrier(vertical_weight.astype(jnp.bfloat16)).astype(jnp.float32)
        summed_scores = jnp.einsum("zirc,zrcp->zip", slash_rounded, slash_values_picked) + jnp.einsum("wenc,ncp->wep", vertical_rounded, vertical_value_rows)
        return (summed_scores / total[:, :, None]).astype(jnp.bfloat16)

    result = lax.map(one_head, jnp.arange(QUERY_HEADS, dtype=jnp.int32))
    return result.transpose(1, 2, 0, 3).reshape(PROMPT_TOKENS, QUERY_HEADS * HEAD_WIDTH)
```

```python
import jax
import jax.numpy as jnp
from jax import lax
from jax.sharding import PartitionSpec as P

HEAD_WIDTH = 128
BLOCK_TOKENS = 64
EXTRA_DIAGONALS = 4


def shifted(value, axis, by):
    size = lax.axis_size(axis)
    pairs = [(i, i + by) for i in range(size) if 0 <= i + by < size]
    return lax.ppermute(value, axis, pairs)


def attend_head(
    query_rows,
    slash_keys_picked,
    slash_values_picked,
    mask_s,
    vertical_key_rows,
    vertical_value_rows,
    vert_ok,
    softmax_scale,
):
    slash_score = (
        jnp.einsum(
            "gxh,gvih->gxvi", query_rows, slash_keys_picked, preferred_element_type=jnp.float32
        )
        * softmax_scale
    )
    slash_score = jnp.where(mask_s, slash_score, -jnp.inf)
    vertical_score = (
        jnp.einsum(
            "ulo,ezo->ulez", query_rows, vertical_key_rows, preferred_element_type=jnp.float32
        )
        * softmax_scale
    )
    vertical_score = jnp.where(vert_ok[:, None, :, None], vertical_score, -jnp.inf)
    top = jnp.maximum(jnp.max(slash_score, axis=(2, 3)), jnp.max(vertical_score, axis=(2, 3)))
    slash_weight = jnp.exp(slash_score - top[:, :, None, None])
    vertical_weight = jnp.exp(vertical_score - top[:, :, None, None])
    total = jnp.sum(slash_weight, axis=(2, 3)) + jnp.sum(vertical_weight, axis=(2, 3))
    summed_scores = jnp.einsum(
        "zirc,zrcp->zip",
        slash_weight.astype(jnp.bfloat16),
        slash_values_picked,
        preferred_element_type=jnp.float32,
    )
    summed_scores = summed_scores + jnp.einsum(
        "wenc,ncp->wep",
        vertical_weight.astype(jnp.bfloat16),
        vertical_value_rows,
        preferred_element_type=jnp.float32,
    )
    result = (summed_scores / total[:, :, None]).astype(jnp.bfloat16)
    return result.reshape(-1, result.shape[2])


def local(queries, keys, values, slash, vertical):
    softmax_scale = HEAD_WIDTH ** (-0.5)
    seq_index = lax.axis_index("seq")
    head_index = lax.axis_index("head")
    q_all, k_all, v_all = (
        lax.all_to_all(queries, "head", split_axis=1, concat_axis=0, tiled=True),
        lax.all_to_all(keys, "head", split_axis=1, concat_axis=0, tiled=True),
        lax.all_to_all(values, "head", split_axis=1, concat_axis=0, tiled=True),
    )
    rows = q_all.shape[0]
    nbd = rows // BLOCK_TOKENS
    kv_local = k_all.shape[1] // HEAD_WIDTH
    query_group = q_all.shape[1] // HEAD_WIDTH // kv_local
    width = EXTRA_DIAGONALS + 1
    prev_k, prev_v = shifted((k_all, v_all), "seq", 1)
    window_k = jnp.concatenate([prev_k, k_all], 0).reshape(
        2 * nbd, BLOCK_TOKENS, kv_local, HEAD_WIDTH
    )
    window_v = jnp.concatenate([prev_v, v_all], 0).reshape(
        2 * nbd, BLOCK_TOKENS, kv_local, HEAD_WIDTH
    )
    own_k = k_all.reshape(nbd, BLOCK_TOKENS, kv_local, HEAD_WIDTH)
    own_v = v_all.reshape(nbd, BLOCK_TOKENS, kv_local, HEAD_WIDTH)
    first_head = head_index * kv_local
    local_slash = lax.dynamic_slice_in_dim(slash, first_head, kv_local, 0) + 1
    diagonal_offsets = jnp.concatenate([jnp.zeros((kv_local, 1), jnp.int32), local_slash], 1)
    local_vert = lax.dynamic_slice_in_dim(vertical, first_head, kv_local, 0)
    owner = local_vert // nbd
    inner = local_vert % nbd
    listed = local_vert.shape[1]
    earlier = jnp.arange(listed)[None, :] < jnp.arange(listed)[:, None]
    same_owner = owner[:, :, None] == owner[:, None, :]
    rank = jnp.sum(same_owner & earlier[None], axis=2)
    slots = 2
    mine = (owner == seq_index)[:, None, :] & (rank[:, None, :] == jnp.arange(slots)[None, :, None])
    pick = jnp.sum(jnp.where(mine, inner[:, None, :], 0), axis=2)
    pieces = []
    for group_member in range(kv_local):
        pieces.append(
            jnp.stack(
                [
                    own_k[:, :, group_member][pick[group_member]],
                    own_v[:, :, group_member][pick[group_member]],
                ],
                1,
            )
        )
    gathered = lax.all_gather(jnp.stack(pieces, 0), "seq", axis=0, tiled=False)
    heads_idx = jnp.arange(kv_local)[:, None]
    fetched = gathered[owner, heads_idx, rank]
    fetched = jnp.moveaxis(fetched, 2, 1)
    vert_keys = fetched[:, 0]
    vert_vals = fetched[:, 1]
    qblocks = seq_index * nbd + jnp.arange(nbd, dtype=jnp.int32)
    spots = jnp.arange(BLOCK_TOKENS)
    causal = spots[None, :] <= spots[:, None]
    beyond = jnp.arange(width) > 0
    outputs = []
    for group_member in range(kv_local):
        offset = diagonal_offsets[group_member]
        slab_k = window_k[:, :, group_member]
        slab_v = window_v[:, :, group_member]
        slash_keys_picked = jnp.stack(
            [lax.dynamic_slice_in_dim(slab_k, nbd - offset[j], nbd, 0) for j in range(width)], 1
        )
        slash_values_picked = jnp.stack(
            [lax.dynamic_slice_in_dim(slab_v, nbd - offset[j], nbd, 0) for j in range(width)], 1
        )
        slash_ok = qblocks[:, None] - offset[None, :] >= 0
        mask_s = slash_ok[:, None, :, None] & (
            beyond[None, None, :, None] | causal[None, :, None, :]
        )
        dist = qblocks[:, None] - local_vert[group_member][None, :]
        hit = jnp.any(dist[:, :, None] == offset[None, None, :], axis=2)
        vert_ok = (dist > 0) & jnp.logical_not(hit)
        for inside in range(query_group):
            head = group_member * query_group + inside
            query_rows = q_all[:, head * HEAD_WIDTH : (head + 1) * HEAD_WIDTH].reshape(
                nbd, BLOCK_TOKENS, HEAD_WIDTH
            )
            outputs.append(
                attend_head(
                    query_rows,
                    slash_keys_picked,
                    slash_values_picked,
                    mask_s,
                    vert_keys[group_member],
                    vert_vals[group_member],
                    vert_ok,
                    softmax_scale,
                )
            )
    return jnp.concatenate(outputs, 1)


def solution(mesh):
    return jax.shard_map(
        local,
        mesh=mesh,
        in_specs=(
            P(("seq", "head"), None),
            P(("seq", "head"), None),
            P(("seq", "head"), None),
            P(),
            P(),
        ),
        out_specs=P("seq", "head"),
        check_vma=False,
    )
```

```python
import jax
import jax.numpy as jnp
from jax import lax
from jax.experimental import pallas as pl
from jax.sharding import PartitionSpec as P

HEAD_WIDTH = 128
BLOCK_TOKENS = 64
EXTRA_DIAGONALS = 4
SLASH_SLOTS = 6
INTERPRET = False


def shifted(value, axis, by):
    size = lax.axis_size(axis)
    pairs = [(i, i + by) for i in range(size) if 0 <= i + by < size]
    return lax.ppermute(value, axis, pairs)


def attend_kernel(q_ref, ks_ref, vs_ref, kv_ref, vv_ref, ms_ref, mv_ref, o_ref, *, group, scale):
    rows = BLOCK_TOKENS * group
    q = q_ref[...]
    q_stack = jnp.concatenate(
        [q[:, h * HEAD_WIDTH : (h + 1) * HEAD_WIDTH] for h in range(group)], axis=0
    )
    nt = (((1,), (1,)), ((), ()))
    s_slash = (
        lax.dot_general(q_stack, ks_ref[0, 0], nt, preferred_element_type=jnp.float32) * scale
    )
    s_vert = lax.dot_general(q_stack, kv_ref[0], nt, preferred_element_type=jnp.float32) * scale
    width = s_slash.shape[1]
    row = jnp.bitwise_and(lax.broadcasted_iota(jnp.int32, (rows, width), 0), BLOCK_TOKENS - 1)
    col = lax.broadcasted_iota(jnp.int32, (rows, width), 1)
    ok_slash = (ms_ref[0, 0] > 0) & ((col >= BLOCK_TOKENS) | (col <= row))
    s_slash = jnp.where(ok_slash, s_slash, -jnp.inf)
    s_vert = jnp.where(mv_ref[0, 0] > 0, s_vert, -jnp.inf)
    top = jnp.maximum(
        jnp.max(s_slash, axis=1, keepdims=True), jnp.max(s_vert, axis=1, keepdims=True)
    )
    w_slash = jnp.exp(s_slash - top)
    w_vert = jnp.exp(s_vert - top)
    total = jnp.sum(w_slash, axis=1, keepdims=True) + jnp.sum(w_vert, axis=1, keepdims=True)
    acc = jnp.dot(w_slash.astype(jnp.bfloat16), vs_ref[0, 0], preferred_element_type=jnp.float32)
    acc = acc + jnp.dot(
        w_vert.astype(jnp.bfloat16), vv_ref[0], preferred_element_type=jnp.float32
    )
    res = (acc / total).astype(o_ref.dtype)
    for h in range(group):
        o_ref[:, h * HEAD_WIDTH : (h + 1) * HEAD_WIDTH] = res[
            h * BLOCK_TOKENS : (h + 1) * BLOCK_TOKENS
        ]


def attend(q_all, ks, vs, kv, vv, ms, mv, group, scale):
    kv_local, nbd = ks.shape[0], ks.shape[1]
    slash_rows = ks.shape[2]
    vert_rows = kv.shape[1]
    cols = group * HEAD_WIDTH
    rows = BLOCK_TOKENS * group
    steps = kv_local * nbd
    flops = steps * 4 * rows * (slash_rows + vert_rows) * HEAD_WIDTH
    cost = pl.CostEstimate(
        flops=flops,
        transcendentals=steps * rows * (slash_rows + vert_rows),
        bytes_accessed=2 * (2 * q_all.size + ks.size + vs.size + kv.size + vv.size),
    )
    kernel = lambda *refs: attend_kernel(*refs, group=group, scale=scale)
    return pl.pallas_call(
        kernel,
        grid=(kv_local, nbd),
        in_specs=[
            pl.BlockSpec((BLOCK_TOKENS, cols), lambda g, i: (i, g)),
            pl.BlockSpec((1, 1, slash_rows, HEAD_WIDTH), lambda g, i: (g, i, 0, 0)),
            pl.BlockSpec((1, 1, slash_rows, HEAD_WIDTH), lambda g, i: (g, i, 0, 0)),
            pl.BlockSpec((1, vert_rows, HEAD_WIDTH), lambda g, i: (g, 0, 0)),
            pl.BlockSpec((1, vert_rows, HEAD_WIDTH), lambda g, i: (g, 0, 0)),
            pl.BlockSpec((1, 1, 1, slash_rows), lambda g, i: (g, i, 0, 0)),
            pl.BlockSpec((1, 1, 1, vert_rows), lambda g, i: (g, i, 0, 0)),
        ],
        out_specs=pl.BlockSpec((BLOCK_TOKENS, cols), lambda g, i: (i, g)),
        out_shape=jax.ShapeDtypeStruct(q_all.shape, q_all.dtype),
        cost_estimate=cost,
        interpret=INTERPRET,
    )(q_all, ks, vs, kv, vv, ms, mv)


def local(queries, keys, values, slash, vertical):
    softmax_scale = HEAD_WIDTH ** (-0.5)
    seq_index = lax.axis_index("seq")
    head_index = lax.axis_index("head")
    q_all, k_all, v_all = (
        lax.all_to_all(queries, "head", split_axis=1, concat_axis=0, tiled=True),
        lax.all_to_all(keys, "head", split_axis=1, concat_axis=0, tiled=True),
        lax.all_to_all(values, "head", split_axis=1, concat_axis=0, tiled=True),
    )
    rows = q_all.shape[0]
    nbd = rows // BLOCK_TOKENS
    kv_local = k_all.shape[1] // HEAD_WIDTH
    query_group = q_all.shape[1] // HEAD_WIDTH // kv_local
    width = EXTRA_DIAGONALS + 1
    prev_k, prev_v = shifted((k_all, v_all), "seq", 1)
    window_k = jnp.concatenate([prev_k, k_all], 0).reshape(
        2 * nbd, BLOCK_TOKENS, kv_local, HEAD_WIDTH
    )
    window_v = jnp.concatenate([prev_v, v_all], 0).reshape(
        2 * nbd, BLOCK_TOKENS, kv_local, HEAD_WIDTH
    )
    own_k = k_all.reshape(nbd, BLOCK_TOKENS, kv_local, HEAD_WIDTH)
    own_v = v_all.reshape(nbd, BLOCK_TOKENS, kv_local, HEAD_WIDTH)
    first_head = head_index * kv_local
    local_slash = lax.dynamic_slice_in_dim(slash, first_head, kv_local, 0) + 1
    diagonal_offsets = jnp.concatenate([jnp.zeros((kv_local, 1), jnp.int32), local_slash], 1)
    local_vert = lax.dynamic_slice_in_dim(vertical, first_head, kv_local, 0)
    owner = local_vert // nbd
    inner = local_vert % nbd
    listed = local_vert.shape[1]
    earlier = jnp.arange(listed)[None, :] < jnp.arange(listed)[:, None]
    same_owner = owner[:, :, None] == owner[:, None, :]
    rank = jnp.sum(same_owner & earlier[None], axis=2)
    slots = 2
    mine = (owner == seq_index)[:, None, :] & (rank[:, None, :] == jnp.arange(slots)[None, :, None])
    pick = jnp.sum(jnp.where(mine, inner[:, None, :], 0), axis=2)
    pieces = []
    for group_member in range(kv_local):
        pieces.append(
            jnp.stack(
                [
                    own_k[:, :, group_member][pick[group_member]],
                    own_v[:, :, group_member][pick[group_member]],
                ],
                1,
            )
        )
    gathered = lax.all_gather(jnp.stack(pieces, 0), "seq", axis=0, tiled=False)
    heads_idx = jnp.arange(kv_local)[:, None]
    fetched = gathered[owner, heads_idx, rank]
    vert_keys = fetched[:, :, 0].reshape(kv_local, listed * BLOCK_TOKENS, HEAD_WIDTH)
    vert_vals = fetched[:, :, 1].reshape(kv_local, listed * BLOCK_TOKENS, HEAD_WIDTH)
    qblocks = seq_index * nbd + jnp.arange(nbd, dtype=jnp.int32)
    pad = jnp.zeros((nbd, SLASH_SLOTS - width, BLOCK_TOKENS, HEAD_WIDTH), k_all.dtype)
    slash_k, slash_v, slash_ok, vert_ok = [], [], [], []
    for group_member in range(kv_local):
        offset = diagonal_offsets[group_member]
        slab_k = window_k[:, :, group_member]
        slab_v = window_v[:, :, group_member]
        picked_k = jnp.stack(
            [lax.dynamic_slice_in_dim(slab_k, nbd - offset[j], nbd, 0) for j in range(width)], 1
        )
        picked_v = jnp.stack(
            [lax.dynamic_slice_in_dim(slab_v, nbd - offset[j], nbd, 0) for j in range(width)], 1
        )
        slash_k.append(jnp.concatenate([picked_k, pad], 1))
        slash_v.append(jnp.concatenate([picked_v, pad], 1))
        block_ok = qblocks[:, None] - offset[None, :] >= 0
        block_ok = jnp.concatenate(
            [block_ok, jnp.zeros((nbd, SLASH_SLOTS - width), jnp.bool_)], 1
        )
        slash_ok.append(jnp.repeat(block_ok, BLOCK_TOKENS, axis=1))
        dist = qblocks[:, None] - local_vert[group_member][None, :]
        hit = jnp.any(dist[:, :, None] == offset[None, None, :], axis=2)
        ok = (dist > 0) & jnp.logical_not(hit)
        vert_ok.append(jnp.repeat(ok, BLOCK_TOKENS, axis=1))
    ks = jnp.stack(slash_k, 0).reshape(kv_local, nbd, SLASH_SLOTS * BLOCK_TOKENS, HEAD_WIDTH)
    vs = jnp.stack(slash_v, 0).reshape(kv_local, nbd, SLASH_SLOTS * BLOCK_TOKENS, HEAD_WIDTH)
    ms = jnp.stack(slash_ok, 0).astype(jnp.int32)[:, :, None, :]
    mv = jnp.stack(vert_ok, 0).astype(jnp.int32)[:, :, None, :]
    return attend(q_all, ks, vs, vert_keys, vert_vals, ms, mv, query_group, softmax_scale)


def solution(mesh):
    return jax.shard_map(
        local,
        mesh=mesh,
        in_specs=(
            P(("seq", "head"), None),
            P(("seq", "head"), None),
            P(("seq", "head"), None),
            P(),
            P(),
        ),
        out_specs=P("seq", "head"),
        check_vma=False,
    )
```

```python
import jax
import jax.numpy as jnp
from jax import lax
from jax.experimental import pallas as pl
from jax.sharding import Mesh, PartitionSpec as P

HEAD_WIDTH = 128
BLOCK_TOKENS = 64
EXTRA_DIAGONALS = 4
SLASH_SLOTS = 6
INTERPRET = False


def shifted(value, axis, by):
    size = lax.axis_size(axis)
    pairs = [(i, i + by) for i in range(size) if 0 <= i + by < size]
    return lax.ppermute(value, axis, pairs)


def attend_kernel(q_ref, ks_ref, vs_ref, kv_ref, vv_ref, ms_ref, mv_ref, o_ref, *, group, scale):
    rows = BLOCK_TOKENS * group
    q = q_ref[...]
    q_stack = jnp.concatenate(
        [q[:, h * HEAD_WIDTH : (h + 1) * HEAD_WIDTH] for h in range(group)], axis=0
    )
    nt = (((1,), (1,)), ((), ()))
    s_slash = (
        lax.dot_general(q_stack, ks_ref[0, 0], nt, preferred_element_type=jnp.float32) * scale
    )
    s_vert = lax.dot_general(q_stack, kv_ref[0], nt, preferred_element_type=jnp.float32) * scale
    width = s_slash.shape[1]
    row = jnp.bitwise_and(lax.broadcasted_iota(jnp.int32, (rows, width), 0), BLOCK_TOKENS - 1)
    col = lax.broadcasted_iota(jnp.int32, (rows, width), 1)
    ok_slash = (ms_ref[0, 0] > 0) & ((col >= BLOCK_TOKENS) | (col <= row))
    s_slash = jnp.where(ok_slash, s_slash, -jnp.inf)
    s_vert = jnp.where(mv_ref[0, 0] > 0, s_vert, -jnp.inf)
    top = jnp.maximum(
        jnp.max(s_slash, axis=1, keepdims=True), jnp.max(s_vert, axis=1, keepdims=True)
    )
    w_slash = jnp.exp(s_slash - top)
    w_vert = jnp.exp(s_vert - top)
    total = jnp.sum(w_slash, axis=1, keepdims=True) + jnp.sum(w_vert, axis=1, keepdims=True)
    acc = jnp.dot(w_slash.astype(jnp.bfloat16), vs_ref[0, 0], preferred_element_type=jnp.float32)
    acc = acc + jnp.dot(
        w_vert.astype(jnp.bfloat16), vv_ref[0], preferred_element_type=jnp.float32
    )
    res = (acc / total).astype(o_ref.dtype)
    for h in range(group):
        o_ref[:, h * HEAD_WIDTH : (h + 1) * HEAD_WIDTH] = res[
            h * BLOCK_TOKENS : (h + 1) * BLOCK_TOKENS
        ]


def attend(q_all, ks, vs, kv, vv, ms, mv, group, scale):
    kv_local, nbd = ks.shape[0], ks.shape[1]
    slash_rows = ks.shape[2]
    vert_rows = kv.shape[1]
    cols = group * HEAD_WIDTH
    rows = BLOCK_TOKENS * group
    steps = kv_local * nbd
    flops = steps * 4 * rows * (slash_rows + vert_rows) * HEAD_WIDTH
    cost = pl.CostEstimate(
        flops=flops,
        transcendentals=steps * rows * (slash_rows + vert_rows),
        bytes_accessed=2 * (2 * q_all.size + ks.size + vs.size + kv.size + vv.size),
    )
    kernel = lambda *refs: attend_kernel(*refs, group=group, scale=scale)
    return pl.pallas_call(
        kernel,
        grid=(kv_local, nbd),
        in_specs=[
            pl.BlockSpec((BLOCK_TOKENS, cols), lambda g, i: (i, g)),
            pl.BlockSpec((1, 1, slash_rows, HEAD_WIDTH), lambda g, i: (g, i, 0, 0)),
            pl.BlockSpec((1, 1, slash_rows, HEAD_WIDTH), lambda g, i: (g, i, 0, 0)),
            pl.BlockSpec((1, vert_rows, HEAD_WIDTH), lambda g, i: (g, 0, 0)),
            pl.BlockSpec((1, vert_rows, HEAD_WIDTH), lambda g, i: (g, 0, 0)),
            pl.BlockSpec((1, 1, 1, slash_rows), lambda g, i: (g, i, 0, 0)),
            pl.BlockSpec((1, 1, 1, vert_rows), lambda g, i: (g, i, 0, 0)),
        ],
        out_specs=pl.BlockSpec((BLOCK_TOKENS, cols), lambda g, i: (i, g)),
        out_shape=jax.ShapeDtypeStruct(q_all.shape, q_all.dtype),
        cost_estimate=cost,
        interpret=INTERPRET,
    )(q_all, ks, vs, kv, vv, ms, mv)


def local(queries, keys, values, slash, vertical):
    softmax_scale = HEAD_WIDTH ** (-0.5)
    core_index = lax.axis_index("core")
    seq_index = lax.axis_index("chip") * lax.axis_size("core") + core_index
    head_index = lax.axis_index("head")
    both = jnp.stack([keys, values], 1).reshape(keys.shape[0], 2, lax.axis_size("head"), -1)
    both = lax.all_to_all(both, "head", split_axis=2, concat_axis=0, tiled=True)
    k_all = both[:, 0].reshape(both.shape[0], -1)
    v_all = both[:, 1].reshape(both.shape[0], -1)
    q_all = lax.all_to_all(queries, "head", split_axis=1, concat_axis=0, tiled=True)
    rows = q_all.shape[0]
    nbd = rows // BLOCK_TOKENS
    kv_local = k_all.shape[1] // HEAD_WIDTH
    query_group = q_all.shape[1] // HEAD_WIDTH // kv_local
    width = EXTRA_DIAGONALS + 1
    prev_k, prev_v = shifted((k_all, v_all), ("chip", "core"), 1)
    window_k = jnp.concatenate([prev_k, k_all], 0).reshape(
        2 * nbd, BLOCK_TOKENS, kv_local, HEAD_WIDTH
    )
    window_v = jnp.concatenate([prev_v, v_all], 0).reshape(
        2 * nbd, BLOCK_TOKENS, kv_local, HEAD_WIDTH
    )
    own_k = k_all.reshape(nbd, BLOCK_TOKENS, kv_local, HEAD_WIDTH)
    own_v = v_all.reshape(nbd, BLOCK_TOKENS, kv_local, HEAD_WIDTH)
    first_head = head_index * kv_local
    local_slash = lax.dynamic_slice_in_dim(slash, first_head, kv_local, 0) + 1
    diagonal_offsets = jnp.concatenate([jnp.zeros((kv_local, 1), jnp.int32), local_slash], 1)
    local_vert = lax.dynamic_slice_in_dim(vertical, first_head, kv_local, 0)
    owner = local_vert // nbd
    inner = local_vert % nbd
    listed = local_vert.shape[1]
    earlier = jnp.arange(listed)[None, :] < jnp.arange(listed)[:, None]
    same_owner = owner[:, :, None] == owner[:, None, :]
    rank = jnp.sum(same_owner & earlier[None], axis=2)
    slots = 2
    mine = (owner == seq_index)[:, None, :] & (rank[:, None, :] == jnp.arange(slots)[None, :, None])
    pick = jnp.sum(jnp.where(mine, inner[:, None, :], 0), axis=2)
    pieces = []
    for group_member in range(kv_local):
        pieces.append(
            jnp.stack(
                [
                    own_k[:, :, group_member][pick[group_member]],
                    own_v[:, :, group_member][pick[group_member]],
                ],
                1,
            )
        )
    half = lax.all_gather(jnp.stack(pieces, 0), "chip", axis=0, tiled=False)
    cores = lax.axis_size("core")
    other = lax.ppermute(half, "core", [(c, cores - 1 - c) for c in range(cores)])
    gathered = jnp.concatenate([half, other], 0)
    chips = half.shape[0]
    source = jnp.where(owner % cores == core_index, owner // cores, chips + owner // cores)
    heads_idx = jnp.arange(kv_local)[:, None]
    fetched = gathered[source, heads_idx, rank]
    vert_keys = fetched[:, :, 0].reshape(kv_local, listed * BLOCK_TOKENS, HEAD_WIDTH)
    vert_vals = fetched[:, :, 1].reshape(kv_local, listed * BLOCK_TOKENS, HEAD_WIDTH)
    qblocks = seq_index * nbd + jnp.arange(nbd, dtype=jnp.int32)
    pad = jnp.zeros((nbd, SLASH_SLOTS - width, BLOCK_TOKENS, HEAD_WIDTH), k_all.dtype)
    slash_k, slash_v, slash_ok, vert_ok = [], [], [], []
    for group_member in range(kv_local):
        offset = diagonal_offsets[group_member]
        slab_k = window_k[:, :, group_member]
        slab_v = window_v[:, :, group_member]
        picked_k = jnp.stack(
            [lax.dynamic_slice_in_dim(slab_k, nbd - offset[j], nbd, 0) for j in range(width)], 1
        )
        picked_v = jnp.stack(
            [lax.dynamic_slice_in_dim(slab_v, nbd - offset[j], nbd, 0) for j in range(width)], 1
        )
        slash_k.append(jnp.concatenate([picked_k, pad], 1))
        slash_v.append(jnp.concatenate([picked_v, pad], 1))
        block_ok = qblocks[:, None] - offset[None, :] >= 0
        block_ok = jnp.concatenate(
            [block_ok, jnp.zeros((nbd, SLASH_SLOTS - width), jnp.bool_)], 1
        )
        slash_ok.append(jnp.repeat(block_ok, BLOCK_TOKENS, axis=1))
        dist = qblocks[:, None] - local_vert[group_member][None, :]
        hit = jnp.any(dist[:, :, None] == offset[None, None, :], axis=2)
        ok = (dist > 0) & jnp.logical_not(hit)
        vert_ok.append(jnp.repeat(ok, BLOCK_TOKENS, axis=1))
    ks = jnp.stack(slash_k, 0).reshape(kv_local, nbd, SLASH_SLOTS * BLOCK_TOKENS, HEAD_WIDTH)
    vs = jnp.stack(slash_v, 0).reshape(kv_local, nbd, SLASH_SLOTS * BLOCK_TOKENS, HEAD_WIDTH)
    ms = jnp.stack(slash_ok, 0).astype(jnp.int32)[:, :, None, :]
    mv = jnp.stack(vert_ok, 0).astype(jnp.int32)[:, :, None, :]
    return attend(q_all, ks, vs, vert_keys, vert_vals, ms, mv, query_group, softmax_scale)


def solution(mesh):
    cores = 2
    devices = mesh.devices.reshape(mesh.shape["seq"] // cores, cores, mesh.shape["head"])
    split = Mesh(devices, ("chip", "core", "head"))
    return jax.shard_map(
        local,
        mesh=split,
        in_specs=(
            P(("chip", "core", "head"), None),
            P(("chip", "core", "head"), None),
            P(("chip", "core", "head"), None),
            P(),
            P(),
        ),
        out_specs=P(("chip", "core"), "head"),
        check_vma=False,
    )
```

```python
import jax
import jax.numpy as jnp
from jax import lax
from jax.experimental import pallas as pl
from jax.sharding import Mesh, PartitionSpec as P

HEAD_WIDTH = 128
BLOCK_TOKENS = 64
EXTRA_DIAGONALS = 4
SLASH_SLOTS = 6
INTERPRET = False


def shifted(value, axis, by):
    size = lax.axis_size(axis)
    pairs = [(i, i + by) for i in range(size) if 0 <= i + by < size]
    return lax.ppermute(value, axis, pairs)


def attend_kernel(q_ref, ks_ref, vs_ref, kv_ref, vv_ref, ms_ref, mv_ref, o_ref, *, group, scale):
    rows = BLOCK_TOKENS * group
    q = q_ref[...]
    q_stack = jnp.concatenate(
        [q[:, h * HEAD_WIDTH : (h + 1) * HEAD_WIDTH] for h in range(group)], axis=0
    )
    nt = (((1,), (1,)), ((), ()))
    s_slash = (
        lax.dot_general(q_stack, ks_ref[0, 0], nt, preferred_element_type=jnp.float32) * scale
    )
    s_vert = lax.dot_general(q_stack, kv_ref[0], nt, preferred_element_type=jnp.float32) * scale
    width = s_slash.shape[1]
    row = jnp.bitwise_and(lax.broadcasted_iota(jnp.int32, (rows, width), 0), BLOCK_TOKENS - 1)
    col = lax.broadcasted_iota(jnp.int32, (rows, width), 1)
    ok_slash = (ms_ref[0, 0] > 0) & ((col >= BLOCK_TOKENS) | (col <= row))
    s_slash = jnp.where(ok_slash, s_slash, -jnp.inf)
    s_vert = jnp.where(mv_ref[0, 0] > 0, s_vert, -jnp.inf)
    top = jnp.maximum(
        jnp.max(s_slash, axis=1, keepdims=True), jnp.max(s_vert, axis=1, keepdims=True)
    )
    w_slash = jnp.exp(s_slash - top)
    w_vert = jnp.exp(s_vert - top)
    total = jnp.sum(w_slash, axis=1, keepdims=True) + jnp.sum(w_vert, axis=1, keepdims=True)
    acc = jnp.dot(w_slash.astype(jnp.bfloat16), vs_ref[0, 0], preferred_element_type=jnp.float32)
    acc = acc + jnp.dot(
        w_vert.astype(jnp.bfloat16), vv_ref[0], preferred_element_type=jnp.float32
    )
    res = (acc / total).astype(o_ref.dtype)
    for h in range(group):
        o_ref[:, h * HEAD_WIDTH : (h + 1) * HEAD_WIDTH] = res[
            h * BLOCK_TOKENS : (h + 1) * BLOCK_TOKENS
        ]


def attend(q_all, ks, vs, kv, vv, ms, mv, group, scale):
    kv_local, nbd = ks.shape[0], ks.shape[1]
    slash_rows = ks.shape[2]
    vert_rows = kv.shape[1]
    cols = group * HEAD_WIDTH
    rows = BLOCK_TOKENS * group
    steps = kv_local * nbd
    flops = steps * 4 * rows * (slash_rows + vert_rows) * HEAD_WIDTH
    cost = pl.CostEstimate(
        flops=flops,
        transcendentals=steps * rows * (slash_rows + vert_rows),
        bytes_accessed=2 * (2 * q_all.size + ks.size + vs.size + kv.size + vv.size),
    )
    kernel = lambda *refs: attend_kernel(*refs, group=group, scale=scale)
    return pl.pallas_call(
        kernel,
        grid=(kv_local, nbd),
        in_specs=[
            pl.BlockSpec((BLOCK_TOKENS, cols), lambda g, i: (i, g)),
            pl.BlockSpec((1, 1, slash_rows, HEAD_WIDTH), lambda g, i: (g, i, 0, 0)),
            pl.BlockSpec((1, 1, slash_rows, HEAD_WIDTH), lambda g, i: (g, i, 0, 0)),
            pl.BlockSpec((1, vert_rows, HEAD_WIDTH), lambda g, i: (g, 0, 0)),
            pl.BlockSpec((1, vert_rows, HEAD_WIDTH), lambda g, i: (g, 0, 0)),
            pl.BlockSpec((1, 1, 1, slash_rows), lambda g, i: (g, i, 0, 0)),
            pl.BlockSpec((1, 1, 1, vert_rows), lambda g, i: (g, i, 0, 0)),
        ],
        out_specs=pl.BlockSpec((BLOCK_TOKENS, cols), lambda g, i: (i, g)),
        out_shape=jax.ShapeDtypeStruct(q_all.shape, q_all.dtype),
        cost_estimate=cost,
        interpret=INTERPRET,
    )(q_all, ks, vs, kv, vv, ms, mv)


def local(queries, keys, values, slash, vertical):
    softmax_scale = HEAD_WIDTH ** (-0.5)
    core_index = lax.axis_index("core")
    seq_index = lax.axis_index("chip") * lax.axis_size("core") + core_index
    head_index = lax.axis_index("head")
    heads = lax.axis_size("head")
    tokens = queries.shape[0]
    joined = jnp.concatenate(
        [
            queries.reshape(tokens, heads, -1),
            keys.reshape(tokens, heads, -1),
            values.reshape(tokens, heads, -1),
        ],
        2,
    )
    joined = lax.all_to_all(joined, "head", split_axis=1, concat_axis=0, tiled=True)
    q_cols = queries.shape[1] // heads
    k_cols = keys.shape[1] // heads
    q_all = joined[:, 0, :q_cols]
    k_all = joined[:, 0, q_cols : q_cols + k_cols]
    v_all = joined[:, 0, q_cols + k_cols :]
    rows = q_all.shape[0]
    nbd = rows // BLOCK_TOKENS
    kv_local = k_all.shape[1] // HEAD_WIDTH
    query_group = q_all.shape[1] // HEAD_WIDTH // kv_local
    width = EXTRA_DIAGONALS + 1
    prev_k, prev_v = shifted((k_all, v_all), ("chip", "core"), 1)
    window_k = jnp.concatenate([prev_k, k_all], 0).reshape(
        2 * nbd, BLOCK_TOKENS, kv_local, HEAD_WIDTH
    )
    window_v = jnp.concatenate([prev_v, v_all], 0).reshape(
        2 * nbd, BLOCK_TOKENS, kv_local, HEAD_WIDTH
    )
    own_k = k_all.reshape(nbd, BLOCK_TOKENS, kv_local, HEAD_WIDTH)
    own_v = v_all.reshape(nbd, BLOCK_TOKENS, kv_local, HEAD_WIDTH)
    first_head = head_index * kv_local
    local_slash = lax.dynamic_slice_in_dim(slash, first_head, kv_local, 0) + 1
    diagonal_offsets = jnp.concatenate([jnp.zeros((kv_local, 1), jnp.int32), local_slash], 1)
    local_vert = lax.dynamic_slice_in_dim(vertical, first_head, kv_local, 0)
    owner = local_vert // nbd
    inner = local_vert % nbd
    listed = local_vert.shape[1]
    earlier = jnp.arange(listed)[None, :] < jnp.arange(listed)[:, None]
    same_owner = owner[:, :, None] == owner[:, None, :]
    rank = jnp.sum(same_owner & earlier[None], axis=2)
    slots = 2
    mine = (owner == seq_index)[:, None, :] & (rank[:, None, :] == jnp.arange(slots)[None, :, None])
    pick = jnp.sum(jnp.where(mine, inner[:, None, :], 0), axis=2)
    pieces = []
    for group_member in range(kv_local):
        pieces.append(
            jnp.stack(
                [
                    own_k[:, :, group_member][pick[group_member]],
                    own_v[:, :, group_member][pick[group_member]],
                ],
                1,
            )
        )
    gathered = lax.all_gather(jnp.stack(pieces, 0), ("chip", "core"), axis=0, tiled=False)
    heads_idx = jnp.arange(kv_local)[:, None]
    fetched = gathered[owner, heads_idx, rank]
    vert_keys = fetched[:, :, 0].reshape(kv_local, listed * BLOCK_TOKENS, HEAD_WIDTH)
    vert_vals = fetched[:, :, 1].reshape(kv_local, listed * BLOCK_TOKENS, HEAD_WIDTH)
    qblocks = seq_index * nbd + jnp.arange(nbd, dtype=jnp.int32)
    pad = jnp.zeros((nbd, SLASH_SLOTS - width, BLOCK_TOKENS, HEAD_WIDTH), k_all.dtype)
    slash_k, slash_v, slash_ok, vert_ok = [], [], [], []
    for group_member in range(kv_local):
        offset = diagonal_offsets[group_member]
        slab_k = window_k[:, :, group_member]
        slab_v = window_v[:, :, group_member]
        picked_k = jnp.stack(
            [lax.dynamic_slice_in_dim(slab_k, nbd - offset[j], nbd, 0) for j in range(width)], 1
        )
        picked_v = jnp.stack(
            [lax.dynamic_slice_in_dim(slab_v, nbd - offset[j], nbd, 0) for j in range(width)], 1
        )
        slash_k.append(jnp.concatenate([picked_k, pad], 1))
        slash_v.append(jnp.concatenate([picked_v, pad], 1))
        block_ok = qblocks[:, None] - offset[None, :] >= 0
        block_ok = jnp.concatenate(
            [block_ok, jnp.zeros((nbd, SLASH_SLOTS - width), jnp.bool_)], 1
        )
        slash_ok.append(jnp.repeat(block_ok, BLOCK_TOKENS, axis=1))
        dist = qblocks[:, None] - local_vert[group_member][None, :]
        hit = jnp.any(dist[:, :, None] == offset[None, None, :], axis=2)
        ok = (dist > 0) & jnp.logical_not(hit)
        vert_ok.append(jnp.repeat(ok, BLOCK_TOKENS, axis=1))
    ks = jnp.stack(slash_k, 0).reshape(kv_local, nbd, SLASH_SLOTS * BLOCK_TOKENS, HEAD_WIDTH)
    vs = jnp.stack(slash_v, 0).reshape(kv_local, nbd, SLASH_SLOTS * BLOCK_TOKENS, HEAD_WIDTH)
    ms = jnp.stack(slash_ok, 0).astype(jnp.int32)[:, :, None, :]
    mv = jnp.stack(vert_ok, 0).astype(jnp.int32)[:, :, None, :]
    return attend(q_all, ks, vs, vert_keys, vert_vals, ms, mv, query_group, softmax_scale)


def solution(mesh):
    cores = 2
    devices = mesh.devices.reshape(mesh.shape["seq"] // cores, cores, mesh.shape["head"])
    split = Mesh(devices, ("chip", "core", "head"))
    return jax.shard_map(
        local,
        mesh=split,
        in_specs=(
            P(("chip", "core", "head"), None),
            P(("chip", "core", "head"), None),
            P(("chip", "core", "head"), None),
            P(),
            P(),
        ),
        out_specs=P(("chip", "core"), "head"),
        check_vma=False,
    )
```

```python
import jax
import jax.numpy as jnp
from jax import lax
from jax.experimental import pallas as pl
from jax.sharding import Mesh, PartitionSpec as P

HEAD_WIDTH = 128
BLOCK_TOKENS = 64
EXTRA_DIAGONALS = 4
SLASH_SLOTS = 6
INTERPRET = False


def shifted(value, axis, by):
    size = lax.axis_size(axis)
    pairs = [(i, i + by) for i in range(size) if 0 <= i + by < size]
    return lax.ppermute(value, axis, pairs)


def attend_kernel(q_ref, ks_ref, vs_ref, kv_ref, vv_ref, ms_ref, mv_ref, o_ref, *, group, scale):
    rows = BLOCK_TOKENS * group
    q = q_ref[...]
    q_stack = jnp.concatenate(
        [q[:, h * HEAD_WIDTH : (h + 1) * HEAD_WIDTH] for h in range(group)], axis=0
    )
    nt = (((1,), (1,)), ((), ()))
    s_slash = (
        lax.dot_general(q_stack, ks_ref[0, 0], nt, preferred_element_type=jnp.float32) * scale
    )
    s_vert = lax.dot_general(q_stack, kv_ref[0], nt, preferred_element_type=jnp.float32) * scale
    width = s_slash.shape[1]
    row = jnp.bitwise_and(lax.broadcasted_iota(jnp.int32, (rows, width), 0), BLOCK_TOKENS - 1)
    col = lax.broadcasted_iota(jnp.int32, (rows, width), 1)
    ok_slash = (ms_ref[0, 0] > 0) & ((col >= BLOCK_TOKENS) | (col <= row))
    s_slash = jnp.where(ok_slash, s_slash, -jnp.inf)
    s_vert = jnp.where(mv_ref[0, 0] > 0, s_vert, -jnp.inf)
    top = jnp.maximum(
        jnp.max(s_slash, axis=1, keepdims=True), jnp.max(s_vert, axis=1, keepdims=True)
    )
    w_slash = jnp.exp(s_slash - top)
    w_vert = jnp.exp(s_vert - top)
    total = jnp.sum(w_slash, axis=1, keepdims=True) + jnp.sum(w_vert, axis=1, keepdims=True)
    acc = jnp.dot(w_slash.astype(jnp.bfloat16), vs_ref[0, 0], preferred_element_type=jnp.float32)
    acc = acc + jnp.dot(
        w_vert.astype(jnp.bfloat16), vv_ref[0], preferred_element_type=jnp.float32
    )
    res = (acc / total).astype(o_ref.dtype)
    for h in range(group):
        o_ref[:, h * HEAD_WIDTH : (h + 1) * HEAD_WIDTH] = res[
            h * BLOCK_TOKENS : (h + 1) * BLOCK_TOKENS
        ]


def attend(q_all, ks, vs, kv, vv, ms, mv, group, scale):
    kv_local, nbd = ks.shape[0], ks.shape[1]
    slash_rows = ks.shape[2]
    vert_rows = kv.shape[1]
    cols = group * HEAD_WIDTH
    rows = BLOCK_TOKENS * group
    steps = kv_local * nbd
    flops = steps * 4 * rows * (slash_rows + vert_rows) * HEAD_WIDTH
    cost = pl.CostEstimate(
        flops=flops,
        transcendentals=steps * rows * (slash_rows + vert_rows),
        bytes_accessed=2 * (2 * q_all.size + ks.size + vs.size + kv.size + vv.size),
    )
    kernel = lambda *refs: attend_kernel(*refs, group=group, scale=scale)
    return pl.pallas_call(
        kernel,
        grid=(kv_local, nbd),
        in_specs=[
            pl.BlockSpec((BLOCK_TOKENS, cols), lambda g, i: (i, g)),
            pl.BlockSpec((1, 1, slash_rows, HEAD_WIDTH), lambda g, i: (g, i, 0, 0)),
            pl.BlockSpec((1, 1, slash_rows, HEAD_WIDTH), lambda g, i: (g, i, 0, 0)),
            pl.BlockSpec((1, vert_rows, HEAD_WIDTH), lambda g, i: (g, 0, 0)),
            pl.BlockSpec((1, vert_rows, HEAD_WIDTH), lambda g, i: (g, 0, 0)),
            pl.BlockSpec((1, 1, 1, slash_rows), lambda g, i: (g, i, 0, 0)),
            pl.BlockSpec((1, 1, 1, vert_rows), lambda g, i: (g, i, 0, 0)),
        ],
        out_specs=pl.BlockSpec((BLOCK_TOKENS, cols), lambda g, i: (i, g)),
        out_shape=jax.ShapeDtypeStruct(q_all.shape, q_all.dtype),
        cost_estimate=cost,
        interpret=INTERPRET,
    )(q_all, ks, vs, kv, vv, ms, mv)


def local(queries, keys, values, slash, vertical):
    softmax_scale = HEAD_WIDTH ** (-0.5)
    core_index = lax.axis_index("core")
    seq_index = lax.axis_index("chip") * lax.axis_size("core") + core_index
    head_index = lax.axis_index("head")
    heads = lax.axis_size("head")
    tokens = keys.shape[0]
    joined = jnp.concatenate(
        [keys.reshape(tokens, heads, -1), values.reshape(tokens, heads, -1)], 2
    )
    joined = lax.all_to_all(joined, "head", split_axis=1, concat_axis=0, tiled=True)
    k_cols = keys.shape[1] // heads
    k_all = joined[:, 0, :k_cols]
    v_all = joined[:, 0, k_cols:]
    rows = k_all.shape[0]
    nbd = rows // BLOCK_TOKENS
    kv_local = k_all.shape[1] // HEAD_WIDTH
    query_group = queries.shape[1] // heads // HEAD_WIDTH // kv_local
    width = EXTRA_DIAGONALS + 1
    prev_k, prev_v = shifted((k_all, v_all), ("chip", "core"), 1)
    window_k = jnp.concatenate([prev_k, k_all], 0).reshape(
        2 * nbd, BLOCK_TOKENS, kv_local, HEAD_WIDTH
    )
    window_v = jnp.concatenate([prev_v, v_all], 0).reshape(
        2 * nbd, BLOCK_TOKENS, kv_local, HEAD_WIDTH
    )
    own_k = k_all.reshape(nbd, BLOCK_TOKENS, kv_local, HEAD_WIDTH)
    own_v = v_all.reshape(nbd, BLOCK_TOKENS, kv_local, HEAD_WIDTH)
    first_head = head_index * kv_local
    local_slash = lax.dynamic_slice_in_dim(slash, first_head, kv_local, 0) + 1
    diagonal_offsets = jnp.concatenate([jnp.zeros((kv_local, 1), jnp.int32), local_slash], 1)
    local_vert = lax.dynamic_slice_in_dim(vertical, first_head, kv_local, 0)
    owner = local_vert // nbd
    inner = local_vert % nbd
    listed = local_vert.shape[1]
    earlier = jnp.arange(listed)[None, :] < jnp.arange(listed)[:, None]
    same_owner = owner[:, :, None] == owner[:, None, :]
    rank = jnp.sum(same_owner & earlier[None], axis=2)
    slots = 2
    mine = (owner == seq_index)[:, None, :] & (rank[:, None, :] == jnp.arange(slots)[None, :, None])
    pick = jnp.sum(jnp.where(mine, inner[:, None, :], 0), axis=2)
    pieces = []
    for group_member in range(kv_local):
        pieces.append(
            jnp.stack(
                [
                    own_k[:, :, group_member][pick[group_member]],
                    own_v[:, :, group_member][pick[group_member]],
                ],
                1,
            )
        )
    pieces, queries = lax.optimization_barrier((jnp.stack(pieces, 0), queries))
    gathered = lax.all_gather(pieces, ("chip", "core"), axis=0, tiled=False)
    q_all = lax.all_to_all(queries, "head", split_axis=1, concat_axis=0, tiled=True)
    heads_idx = jnp.arange(kv_local)[:, None]
    fetched = gathered[owner, heads_idx, rank]
    vert_keys = fetched[:, :, 0].reshape(kv_local, listed * BLOCK_TOKENS, HEAD_WIDTH)
    vert_vals = fetched[:, :, 1].reshape(kv_local, listed * BLOCK_TOKENS, HEAD_WIDTH)
    qblocks = seq_index * nbd + jnp.arange(nbd, dtype=jnp.int32)
    pad = jnp.zeros((nbd, SLASH_SLOTS - width, BLOCK_TOKENS, HEAD_WIDTH), k_all.dtype)
    slash_k, slash_v, slash_ok, vert_ok = [], [], [], []
    for group_member in range(kv_local):
        offset = diagonal_offsets[group_member]
        slab_k = window_k[:, :, group_member]
        slab_v = window_v[:, :, group_member]
        picked_k = jnp.stack(
            [lax.dynamic_slice_in_dim(slab_k, nbd - offset[j], nbd, 0) for j in range(width)], 1
        )
        picked_v = jnp.stack(
            [lax.dynamic_slice_in_dim(slab_v, nbd - offset[j], nbd, 0) for j in range(width)], 1
        )
        slash_k.append(jnp.concatenate([picked_k, pad], 1))
        slash_v.append(jnp.concatenate([picked_v, pad], 1))
        block_ok = qblocks[:, None] - offset[None, :] >= 0
        block_ok = jnp.concatenate(
            [block_ok, jnp.zeros((nbd, SLASH_SLOTS - width), jnp.bool_)], 1
        )
        slash_ok.append(jnp.repeat(block_ok, BLOCK_TOKENS, axis=1))
        dist = qblocks[:, None] - local_vert[group_member][None, :]
        hit = jnp.any(dist[:, :, None] == offset[None, None, :], axis=2)
        ok = (dist > 0) & jnp.logical_not(hit)
        vert_ok.append(jnp.repeat(ok, BLOCK_TOKENS, axis=1))
    ks = jnp.stack(slash_k, 0).reshape(kv_local, nbd, SLASH_SLOTS * BLOCK_TOKENS, HEAD_WIDTH)
    vs = jnp.stack(slash_v, 0).reshape(kv_local, nbd, SLASH_SLOTS * BLOCK_TOKENS, HEAD_WIDTH)
    ms = jnp.stack(slash_ok, 0).astype(jnp.int32)[:, :, None, :]
    mv = jnp.stack(vert_ok, 0).astype(jnp.int32)[:, :, None, :]
    return attend(q_all, ks, vs, vert_keys, vert_vals, ms, mv, query_group, softmax_scale)


def solution(mesh):
    cores = 2
    devices = mesh.devices.reshape(mesh.shape["seq"] // cores, cores, mesh.shape["head"])
    split = Mesh(devices, ("chip", "core", "head"))
    return jax.shard_map(
        local,
        mesh=split,
        in_specs=(
            P(("chip", "core", "head"), None),
            P(("chip", "core", "head"), None),
            P(("chip", "core", "head"), None),
            P(),
            P(),
        ),
        out_specs=P(("chip", "core"), "head"),
        check_vma=False,
    )
```

```python
import jax
import jax.numpy as jnp
from jax import lax
from jax.experimental import pallas as pl
from jax.sharding import Mesh, PartitionSpec as P

HEAD_WIDTH = 128
BLOCK_TOKENS = 64
EXTRA_DIAGONALS = 4
SLASH_SLOTS = 6
INTERPRET = False


def shifted(value, axis, by):
    size = lax.axis_size(axis)
    pairs = [(i, i + by) for i in range(size) if 0 <= i + by < size]
    return lax.ppermute(value, axis, pairs)


def attend_kernel(q_ref, ks_ref, vs_ref, kv_ref, vv_ref, ms_ref, mv_ref, o_ref, *, group, scale):
    rows = BLOCK_TOKENS * group
    q = q_ref[...]
    q_stack = jnp.concatenate(
        [q[:, h * HEAD_WIDTH : (h + 1) * HEAD_WIDTH] for h in range(group)], axis=0
    )
    nt = (((1,), (1,)), ((), ()))
    s_slash = (
        lax.dot_general(q_stack, ks_ref[0, 0], nt, preferred_element_type=jnp.float32) * scale
    )
    s_vert = lax.dot_general(q_stack, kv_ref[0], nt, preferred_element_type=jnp.float32) * scale
    width = s_slash.shape[1]
    row = jnp.bitwise_and(lax.broadcasted_iota(jnp.int32, (rows, width), 0), BLOCK_TOKENS - 1)
    col = lax.broadcasted_iota(jnp.int32, (rows, width), 1)
    ok_slash = (ms_ref[0, 0] > 0) & ((col >= BLOCK_TOKENS) | (col <= row))
    s_slash = jnp.where(ok_slash, s_slash, -jnp.inf)
    s_vert = jnp.where(mv_ref[0, 0] > 0, s_vert, -jnp.inf)
    top = jnp.maximum(
        jnp.max(s_slash, axis=1, keepdims=True), jnp.max(s_vert, axis=1, keepdims=True)
    )
    w_slash = jnp.exp(s_slash - top)
    w_vert = jnp.exp(s_vert - top)
    total = jnp.sum(w_slash, axis=1, keepdims=True) + jnp.sum(w_vert, axis=1, keepdims=True)
    acc = jnp.dot(w_slash.astype(jnp.bfloat16), vs_ref[0, 0], preferred_element_type=jnp.float32)
    acc = acc + jnp.dot(
        w_vert.astype(jnp.bfloat16), vv_ref[0], preferred_element_type=jnp.float32
    )
    res = (acc / total).astype(o_ref.dtype)
    for h in range(group):
        o_ref[:, h * HEAD_WIDTH : (h + 1) * HEAD_WIDTH] = res[
            h * BLOCK_TOKENS : (h + 1) * BLOCK_TOKENS
        ]


def attend(q_all, ks, vs, kv, vv, ms, mv, group, scale):
    kv_local, nbd = ks.shape[0], ks.shape[1]
    slash_rows = ks.shape[2]
    vert_rows = kv.shape[1]
    cols = group * HEAD_WIDTH
    rows = BLOCK_TOKENS * group
    steps = kv_local * nbd
    flops = steps * 4 * rows * (slash_rows + vert_rows) * HEAD_WIDTH
    cost = pl.CostEstimate(
        flops=flops,
        transcendentals=steps * rows * (slash_rows + vert_rows),
        bytes_accessed=2 * (2 * q_all.size + ks.size + vs.size + kv.size + vv.size),
    )
    kernel = lambda *refs: attend_kernel(*refs, group=group, scale=scale)
    return pl.pallas_call(
        kernel,
        grid=(kv_local, nbd),
        in_specs=[
            pl.BlockSpec((BLOCK_TOKENS, cols), lambda g, i: (i, g)),
            pl.BlockSpec((1, 1, slash_rows, HEAD_WIDTH), lambda g, i: (g, i, 0, 0)),
            pl.BlockSpec((1, 1, slash_rows, HEAD_WIDTH), lambda g, i: (g, i, 0, 0)),
            pl.BlockSpec((1, vert_rows, HEAD_WIDTH), lambda g, i: (g, 0, 0)),
            pl.BlockSpec((1, vert_rows, HEAD_WIDTH), lambda g, i: (g, 0, 0)),
            pl.BlockSpec((1, 1, 1, slash_rows), lambda g, i: (g, i, 0, 0)),
            pl.BlockSpec((1, 1, 1, vert_rows), lambda g, i: (g, i, 0, 0)),
        ],
        out_specs=pl.BlockSpec((BLOCK_TOKENS, cols), lambda g, i: (i, g)),
        out_shape=jax.ShapeDtypeStruct(q_all.shape, q_all.dtype),
        cost_estimate=cost,
        interpret=INTERPRET,
    )(q_all, ks, vs, kv, vv, ms, mv)


def local(queries, keys, values, slash, vertical):
    softmax_scale = HEAD_WIDTH ** (-0.5)
    core_index = lax.axis_index("core")
    seq_index = lax.axis_index("chip") * lax.axis_size("core") + core_index
    head_index = lax.axis_index("head")
    heads = lax.axis_size("head")
    tokens = keys.shape[0]
    joined = jnp.concatenate(
        [keys.reshape(tokens, heads, -1), values.reshape(tokens, heads, -1)], 2
    )
    joined = lax.all_to_all(joined, "head", split_axis=1, concat_axis=0, tiled=True)
    k_cols = keys.shape[1] // heads
    k_all = joined[:, 0, :k_cols]
    v_all = joined[:, 0, k_cols:]
    rows = k_all.shape[0]
    nbd = rows // BLOCK_TOKENS
    kv_local = k_all.shape[1] // HEAD_WIDTH
    query_group = queries.shape[1] // heads // HEAD_WIDTH // kv_local
    width = EXTRA_DIAGONALS + 1
    prev_k, prev_v = shifted((k_all, v_all), ("chip", "core"), 1)
    window_k = jnp.concatenate([prev_k, k_all], 0).reshape(
        2 * nbd, BLOCK_TOKENS, kv_local, HEAD_WIDTH
    )
    window_v = jnp.concatenate([prev_v, v_all], 0).reshape(
        2 * nbd, BLOCK_TOKENS, kv_local, HEAD_WIDTH
    )
    own_k = k_all.reshape(nbd, BLOCK_TOKENS, kv_local, HEAD_WIDTH)
    own_v = v_all.reshape(nbd, BLOCK_TOKENS, kv_local, HEAD_WIDTH)
    first_head = head_index * kv_local
    local_slash = lax.dynamic_slice_in_dim(slash, first_head, kv_local, 0) + 1
    diagonal_offsets = jnp.concatenate([jnp.zeros((kv_local, 1), jnp.int32), local_slash], 1)
    local_vert = lax.dynamic_slice_in_dim(vertical, first_head, kv_local, 0)
    owner = local_vert // nbd
    inner = local_vert % nbd
    listed = local_vert.shape[1]
    earlier = jnp.arange(listed)[None, :] < jnp.arange(listed)[:, None]
    same_owner = owner[:, :, None] == owner[:, None, :]
    rank = jnp.sum(same_owner & earlier[None], axis=2)
    slots = 2
    mine = (owner == seq_index)[:, None, :] & (rank[:, None, :] == jnp.arange(slots)[None, :, None])
    pick = jnp.sum(jnp.where(mine, inner[:, None, :], 0), axis=2)
    pieces = []
    for group_member in range(kv_local):
        pieces.append(
            jnp.stack(
                [
                    own_k[:, :, group_member][pick[group_member]],
                    own_v[:, :, group_member][pick[group_member]],
                ],
                1,
            )
        )
    pieces, queries = lax.optimization_barrier((jnp.stack(pieces, 0), queries))
    chips = lax.axis_size("chip")
    cores = lax.axis_size("core")
    spread = jnp.broadcast_to(pieces[None], (chips,) + pieces.shape)
    half = lax.all_to_all(spread, "chip", split_axis=0, concat_axis=0, tiled=True)
    other = lax.ppermute(half, "core", [(c, cores - 1 - c) for c in range(cores)])
    gathered = jnp.concatenate([half, other], 0)
    owner = jnp.where(owner % cores == core_index, owner // cores, chips + owner // cores)
    q_all = lax.all_to_all(queries, "head", split_axis=1, concat_axis=0, tiled=True)
    heads_idx = jnp.arange(kv_local)[:, None]
    fetched = gathered[owner, heads_idx, rank]
    vert_keys = fetched[:, :, 0].reshape(kv_local, listed * BLOCK_TOKENS, HEAD_WIDTH)
    vert_vals = fetched[:, :, 1].reshape(kv_local, listed * BLOCK_TOKENS, HEAD_WIDTH)
    qblocks = seq_index * nbd + jnp.arange(nbd, dtype=jnp.int32)
    pad = jnp.zeros((nbd, SLASH_SLOTS - width, BLOCK_TOKENS, HEAD_WIDTH), k_all.dtype)
    slash_k, slash_v, slash_ok, vert_ok = [], [], [], []
    for group_member in range(kv_local):
        offset = diagonal_offsets[group_member]
        slab_k = window_k[:, :, group_member]
        slab_v = window_v[:, :, group_member]
        picked_k = jnp.stack(
            [lax.dynamic_slice_in_dim(slab_k, nbd - offset[j], nbd, 0) for j in range(width)], 1
        )
        picked_v = jnp.stack(
            [lax.dynamic_slice_in_dim(slab_v, nbd - offset[j], nbd, 0) for j in range(width)], 1
        )
        slash_k.append(jnp.concatenate([picked_k, pad], 1))
        slash_v.append(jnp.concatenate([picked_v, pad], 1))
        block_ok = qblocks[:, None] - offset[None, :] >= 0
        block_ok = jnp.concatenate(
            [block_ok, jnp.zeros((nbd, SLASH_SLOTS - width), jnp.bool_)], 1
        )
        slash_ok.append(jnp.repeat(block_ok, BLOCK_TOKENS, axis=1))
        dist = qblocks[:, None] - local_vert[group_member][None, :]
        hit = jnp.any(dist[:, :, None] == offset[None, None, :], axis=2)
        ok = (dist > 0) & jnp.logical_not(hit)
        vert_ok.append(jnp.repeat(ok, BLOCK_TOKENS, axis=1))
    ks = jnp.stack(slash_k, 0).reshape(kv_local, nbd, SLASH_SLOTS * BLOCK_TOKENS, HEAD_WIDTH)
    vs = jnp.stack(slash_v, 0).reshape(kv_local, nbd, SLASH_SLOTS * BLOCK_TOKENS, HEAD_WIDTH)
    ms = jnp.stack(slash_ok, 0).astype(jnp.int32)[:, :, None, :]
    mv = jnp.stack(vert_ok, 0).astype(jnp.int32)[:, :, None, :]
    return attend(q_all, ks, vs, vert_keys, vert_vals, ms, mv, query_group, softmax_scale)


def solution(mesh):
    cores = 2
    devices = mesh.devices.reshape(mesh.shape["seq"] // cores, cores, mesh.shape["head"])
    split = Mesh(devices, ("chip", "core", "head"))
    return jax.shard_map(
        local,
        mesh=split,
        in_specs=(
            P(("chip", "core", "head"), None),
            P(("chip", "core", "head"), None),
            P(("chip", "core", "head"), None),
            P(),
            P(),
        ),
        out_specs=P(("chip", "core"), "head"),
        check_vma=False,
    )
```

```python
import jax
import jax.numpy as jnp
from jax import lax
from jax.experimental import pallas as pl
from jax.sharding import Mesh, PartitionSpec as P

HEAD_WIDTH = 128
BLOCK_TOKENS = 64
EXTRA_DIAGONALS = 4
SLASH_SLOTS = 6
INTERPRET = False


def shifted(value, axis, by):
    size = lax.axis_size(axis)
    pairs = [(i, i + by) for i in range(size) if 0 <= i + by < size]
    return lax.ppermute(value, axis, pairs)


def attend_kernel(q_ref, ks_ref, vs_ref, kv_ref, vv_ref, ms_ref, mv_ref, o_ref, *, group, scale):
    rows = BLOCK_TOKENS * group
    q = q_ref[...]
    q_stack = jnp.concatenate(
        [q[:, h * HEAD_WIDTH : (h + 1) * HEAD_WIDTH] for h in range(group)], axis=0
    )
    nt = (((1,), (1,)), ((), ()))
    s_slash = (
        lax.dot_general(q_stack, ks_ref[0, 0], nt, preferred_element_type=jnp.float32) * scale
    )
    s_vert = lax.dot_general(q_stack, kv_ref[0], nt, preferred_element_type=jnp.float32) * scale
    width = s_slash.shape[1]
    row = jnp.bitwise_and(lax.broadcasted_iota(jnp.int32, (rows, width), 0), BLOCK_TOKENS - 1)
    col = lax.broadcasted_iota(jnp.int32, (rows, width), 1)
    ok_slash = (ms_ref[0, 0] > 0) & ((col >= BLOCK_TOKENS) | (col <= row))
    s_slash = jnp.where(ok_slash, s_slash, -jnp.inf)
    s_vert = jnp.where(mv_ref[0, 0] > 0, s_vert, -jnp.inf)
    top = jnp.maximum(
        jnp.max(s_slash, axis=1, keepdims=True), jnp.max(s_vert, axis=1, keepdims=True)
    )
    w_slash = jnp.exp(s_slash - top)
    w_vert = jnp.exp(s_vert - top)
    total = jnp.sum(w_slash, axis=1, keepdims=True) + jnp.sum(w_vert, axis=1, keepdims=True)
    acc = jnp.dot(w_slash.astype(jnp.bfloat16), vs_ref[0, 0], preferred_element_type=jnp.float32)
    acc = acc + jnp.dot(
        w_vert.astype(jnp.bfloat16), vv_ref[0], preferred_element_type=jnp.float32
    )
    res = (acc / total).astype(o_ref.dtype)
    for h in range(group):
        o_ref[:, h * HEAD_WIDTH : (h + 1) * HEAD_WIDTH] = res[
            h * BLOCK_TOKENS : (h + 1) * BLOCK_TOKENS
        ]


def attend(q_all, ks, vs, kv, vv, ms, mv, group, scale):
    kv_local, nbd = ks.shape[0], ks.shape[1]
    slash_rows = ks.shape[2]
    vert_rows = kv.shape[1]
    cols = group * HEAD_WIDTH
    rows = BLOCK_TOKENS * group
    steps = kv_local * nbd
    flops = steps * 4 * rows * (slash_rows + vert_rows) * HEAD_WIDTH
    cost = pl.CostEstimate(
        flops=flops,
        transcendentals=steps * rows * (slash_rows + vert_rows),
        bytes_accessed=2 * (2 * q_all.size + ks.size + vs.size + kv.size + vv.size),
    )
    kernel = lambda *refs: attend_kernel(*refs, group=group, scale=scale)
    return pl.pallas_call(
        kernel,
        grid=(kv_local, nbd),
        in_specs=[
            pl.BlockSpec((BLOCK_TOKENS, cols), lambda g, i: (i, g)),
            pl.BlockSpec((1, 1, slash_rows, HEAD_WIDTH), lambda g, i: (g, i, 0, 0)),
            pl.BlockSpec((1, 1, slash_rows, HEAD_WIDTH), lambda g, i: (g, i, 0, 0)),
            pl.BlockSpec((1, vert_rows, HEAD_WIDTH), lambda g, i: (g, 0, 0)),
            pl.BlockSpec((1, vert_rows, HEAD_WIDTH), lambda g, i: (g, 0, 0)),
            pl.BlockSpec((1, 1, 1, slash_rows), lambda g, i: (g, i, 0, 0)),
            pl.BlockSpec((1, 1, 1, vert_rows), lambda g, i: (g, i, 0, 0)),
        ],
        out_specs=pl.BlockSpec((BLOCK_TOKENS, cols), lambda g, i: (i, g)),
        out_shape=jax.ShapeDtypeStruct(q_all.shape, q_all.dtype),
        cost_estimate=cost,
        interpret=INTERPRET,
    )(q_all, ks, vs, kv, vv, ms, mv)


def local(queries, keys, values, slash, vertical):
    softmax_scale = HEAD_WIDTH ** (-0.5)
    core_index = lax.axis_index("core")
    seq_index = lax.axis_index("chip") * lax.axis_size("core") + core_index
    head_index = lax.axis_index("head")
    heads = lax.axis_size("head")
    tokens = keys.shape[0]
    joined = jnp.concatenate(
        [keys.reshape(tokens, heads, -1), values.reshape(tokens, heads, -1)], 2
    )
    joined = lax.all_to_all(joined, "head", split_axis=1, concat_axis=0, tiled=True)
    k_cols = keys.shape[1] // heads
    k_all = joined[:, 0, :k_cols]
    v_all = joined[:, 0, k_cols:]
    rows = k_all.shape[0]
    nbd = rows // BLOCK_TOKENS
    kv_local = k_all.shape[1] // HEAD_WIDTH
    query_group = queries.shape[1] // heads // HEAD_WIDTH // kv_local
    width = EXTRA_DIAGONALS + 1
    prev_k, prev_v = shifted((k_all, v_all), ("chip", "core"), 1)
    window_k = jnp.concatenate([prev_k, k_all], 0).reshape(
        2 * nbd, BLOCK_TOKENS, kv_local, HEAD_WIDTH
    )
    window_v = jnp.concatenate([prev_v, v_all], 0).reshape(
        2 * nbd, BLOCK_TOKENS, kv_local, HEAD_WIDTH
    )
    own_k = k_all.reshape(nbd, BLOCK_TOKENS, kv_local, HEAD_WIDTH)
    own_v = v_all.reshape(nbd, BLOCK_TOKENS, kv_local, HEAD_WIDTH)
    first_head = head_index * kv_local
    local_slash = lax.dynamic_slice_in_dim(slash, first_head, kv_local, 0) + 1
    diagonal_offsets = jnp.concatenate([jnp.zeros((kv_local, 1), jnp.int32), local_slash], 1)
    local_vert = lax.dynamic_slice_in_dim(vertical, first_head, kv_local, 0)
    owner = local_vert // nbd
    inner = local_vert % nbd
    listed = local_vert.shape[1]
    earlier = jnp.arange(listed)[None, :] < jnp.arange(listed)[:, None]
    same_owner = owner[:, :, None] == owner[:, None, :]
    rank = jnp.sum(same_owner & earlier[None], axis=2)
    slots = 2
    mine = (owner == seq_index)[:, None, :] & (rank[:, None, :] == jnp.arange(slots)[None, :, None])
    pick = jnp.sum(jnp.where(mine, inner[:, None, :], 0), axis=2)
    pieces = []
    for group_member in range(kv_local):
        pieces.append(
            jnp.stack(
                [
                    own_k[:, :, group_member][pick[group_member]],
                    own_v[:, :, group_member][pick[group_member]],
                ],
                1,
            )
        )
    pieces, queries = lax.optimization_barrier((jnp.stack(pieces, 0), queries))
    chips = lax.axis_size("chip")
    cores = lax.axis_size("core")
    side = int(round(chips ** 0.5))
    chip_index = lax.axis_index("chip")
    swap = [(c, cores - 1 - c) for c in range(cores)]
    mine = lax.dynamic_index_in_dim(pieces, core_index, 2, keepdims=False)
    sent = lax.dynamic_index_in_dim(pieces, cores - 1 - core_index, 2, keepdims=False)
    stage = jnp.stack([mine, lax.ppermute(sent, "core", swap)], 0)
    q_all = lax.all_to_all(queries, "head", split_axis=1, concat_axis=0, tiled=True)
    for stride in (1, side):
        moved = [stage]
        for step in range(1, side):
            pairs = []
            for chip in range(chips):
                row, col = chip // side, chip % side
                if stride == 1:
                    pairs.append((chip, row * side + (col + step) % side))
                else:
                    pairs.append((chip, ((row + step) % side) * side + col))
            moved.append(lax.ppermute(stage, "chip", pairs))
        stage = jnp.stack(moved, 0)
    partner = lax.ppermute(stage, "core", swap)
    keys_src = jnp.where(core_index == 0, stage, partner)
    vals_src = jnp.where(core_index == 0, partner, stage)
    owner_chip = owner // cores
    owner_core = owner % cores
    dy = (chip_index // side - owner_chip // side) % side
    dx = (chip_index % side - owner_chip % side) % side
    heads_idx = jnp.arange(kv_local)[:, None]
    vert_keys = keys_src[dy, dx, owner_core, heads_idx, rank]
    vert_vals = vals_src[dy, dx, cores - 1 - owner_core, heads_idx, rank]
    vert_keys = vert_keys.reshape(kv_local, listed * BLOCK_TOKENS, HEAD_WIDTH)
    vert_vals = vert_vals.reshape(kv_local, listed * BLOCK_TOKENS, HEAD_WIDTH)
    qblocks = seq_index * nbd + jnp.arange(nbd, dtype=jnp.int32)
    pad = jnp.zeros((nbd, SLASH_SLOTS - width, BLOCK_TOKENS, HEAD_WIDTH), k_all.dtype)
    slash_k, slash_v, slash_ok, vert_ok = [], [], [], []
    for group_member in range(kv_local):
        offset = diagonal_offsets[group_member]
        slab_k = window_k[:, :, group_member]
        slab_v = window_v[:, :, group_member]
        picked_k = jnp.stack(
            [lax.dynamic_slice_in_dim(slab_k, nbd - offset[j], nbd, 0) for j in range(width)], 1
        )
        picked_v = jnp.stack(
            [lax.dynamic_slice_in_dim(slab_v, nbd - offset[j], nbd, 0) for j in range(width)], 1
        )
        slash_k.append(jnp.concatenate([picked_k, pad], 1))
        slash_v.append(jnp.concatenate([picked_v, pad], 1))
        block_ok = qblocks[:, None] - offset[None, :] >= 0
        block_ok = jnp.concatenate(
            [block_ok, jnp.zeros((nbd, SLASH_SLOTS - width), jnp.bool_)], 1
        )
        slash_ok.append(jnp.repeat(block_ok, BLOCK_TOKENS, axis=1))
        dist = qblocks[:, None] - local_vert[group_member][None, :]
        hit = jnp.any(dist[:, :, None] == offset[None, None, :], axis=2)
        ok = (dist > 0) & jnp.logical_not(hit)
        vert_ok.append(jnp.repeat(ok, BLOCK_TOKENS, axis=1))
    ks = jnp.stack(slash_k, 0).reshape(kv_local, nbd, SLASH_SLOTS * BLOCK_TOKENS, HEAD_WIDTH)
    vs = jnp.stack(slash_v, 0).reshape(kv_local, nbd, SLASH_SLOTS * BLOCK_TOKENS, HEAD_WIDTH)
    ms = jnp.stack(slash_ok, 0).astype(jnp.int32)[:, :, None, :]
    mv = jnp.stack(vert_ok, 0).astype(jnp.int32)[:, :, None, :]
    return attend(q_all, ks, vs, vert_keys, vert_vals, ms, mv, query_group, softmax_scale)


def solution(mesh):
    cores = 2
    devices = mesh.devices.reshape(mesh.shape["seq"] // cores, cores, mesh.shape["head"])
    split = Mesh(devices, ("chip", "core", "head"))
    return jax.shard_map(
        local,
        mesh=split,
        in_specs=(
            P(("chip", "core", "head"), None),
            P(("chip", "core", "head"), None),
            P(("chip", "core", "head"), None),
            P(),
            P(),
        ),
        out_specs=P(("chip", "core"), "head"),
        check_vma=False,
    )
```

```python
import jax
import jax.numpy as jnp
from jax import lax
from jax.experimental import pallas as pl
from jax.experimental.pallas import tpu as pltpu
from jax.sharding import Mesh, PartitionSpec as P

HEAD_WIDTH = 128
BLOCK_TOKENS = 64
EXTRA_DIAGONALS = 4
SLASH_SLOTS = 6
INTERPRET = False


def shifted(value, axis, by):
    size = lax.axis_size(axis)
    pairs = [(i, i + by) for i in range(size) if 0 <= i + by < size]
    return lax.ppermute(value, axis, pairs)


def attend_kernel(
    off_ref, q_ref, wk_ref, wv_ref, kv_ref, vv_ref, ms_ref, mv_ref, o_ref, *, group, scale, nbd
):
    g = pl.program_id(0)
    i = pl.program_id(1)
    rows = BLOCK_TOKENS * group
    picked_k, picked_v = [], []
    for j in range(EXTRA_DIAGONALS + 1):
        block = jnp.clip(nbd + i - off_ref[g, j], 0, 2 * nbd - 1)
        start = pl.multiple_of(block * BLOCK_TOKENS, BLOCK_TOKENS)
        picked_k.append(wk_ref[pl.ds(start, BLOCK_TOKENS), :])
        picked_v.append(wv_ref[pl.ds(start, BLOCK_TOKENS), :])
    pad = jnp.zeros(
        ((SLASH_SLOTS - EXTRA_DIAGONALS - 1) * BLOCK_TOKENS, HEAD_WIDTH), wk_ref.dtype
    )
    ks = jnp.concatenate(picked_k + [pad], 0)
    vs = jnp.concatenate(picked_v + [pad], 0)
    q = q_ref[...]
    q_stack = jnp.concatenate(
        [q[:, h * HEAD_WIDTH : (h + 1) * HEAD_WIDTH] for h in range(group)], axis=0
    )
    nt = (((1,), (1,)), ((), ()))
    s_slash = lax.dot_general(q_stack, ks, nt, preferred_element_type=jnp.float32) * scale
    s_vert = lax.dot_general(q_stack, kv_ref[0], nt, preferred_element_type=jnp.float32) * scale
    width = s_slash.shape[1]
    row = jnp.bitwise_and(lax.broadcasted_iota(jnp.int32, (rows, width), 0), BLOCK_TOKENS - 1)
    col = lax.broadcasted_iota(jnp.int32, (rows, width), 1)
    ok_slash = (ms_ref[0, 0] > 0) & ((col >= BLOCK_TOKENS) | (col <= row))
    s_slash = jnp.where(ok_slash, s_slash, -jnp.inf)
    s_vert = jnp.where(mv_ref[0, 0] > 0, s_vert, -jnp.inf)
    top = jnp.maximum(
        jnp.max(s_slash, axis=1, keepdims=True), jnp.max(s_vert, axis=1, keepdims=True)
    )
    w_slash = jnp.exp(s_slash - top)
    w_vert = jnp.exp(s_vert - top)
    total = jnp.sum(w_slash, axis=1, keepdims=True) + jnp.sum(w_vert, axis=1, keepdims=True)
    acc = jnp.dot(w_slash.astype(jnp.bfloat16), vs, preferred_element_type=jnp.float32)
    acc = acc + jnp.dot(
        w_vert.astype(jnp.bfloat16), vv_ref[0], preferred_element_type=jnp.float32
    )
    res = (acc / total).astype(o_ref.dtype)
    for h in range(group):
        o_ref[:, h * HEAD_WIDTH : (h + 1) * HEAD_WIDTH] = res[
            h * BLOCK_TOKENS : (h + 1) * BLOCK_TOKENS
        ]


def attend(offsets, q_all, win_k, win_v, kv, vv, ms, mv, group, scale):
    kv_local, nbd = ms.shape[0], ms.shape[1]
    slash_rows = ms.shape[3]
    vert_rows = kv.shape[1]
    window_rows = win_k.shape[0]
    cols = group * HEAD_WIDTH
    rows = BLOCK_TOKENS * group
    steps = kv_local * nbd
    flops = steps * 4 * rows * (slash_rows + vert_rows) * HEAD_WIDTH
    cost = pl.CostEstimate(
        flops=flops,
        transcendentals=steps * rows * (slash_rows + vert_rows),
        bytes_accessed=2 * (2 * q_all.size + win_k.size + win_v.size + kv.size + vv.size),
    )
    kernel = lambda *refs: attend_kernel(*refs, group=group, scale=scale, nbd=nbd)
    grid_spec = pltpu.PrefetchScalarGridSpec(
        num_scalar_prefetch=1,
        grid=(kv_local, nbd),
        in_specs=[
            pl.BlockSpec((BLOCK_TOKENS, cols), lambda g, i, off: (i, g)),
            pl.BlockSpec((window_rows, HEAD_WIDTH), lambda g, i, off: (0, g)),
            pl.BlockSpec((window_rows, HEAD_WIDTH), lambda g, i, off: (0, g)),
            pl.BlockSpec((1, vert_rows, HEAD_WIDTH), lambda g, i, off: (g, 0, 0)),
            pl.BlockSpec((1, vert_rows, HEAD_WIDTH), lambda g, i, off: (g, 0, 0)),
            pl.BlockSpec((1, 1, 1, slash_rows), lambda g, i, off: (g, i, 0, 0)),
            pl.BlockSpec((1, 1, 1, vert_rows), lambda g, i, off: (g, i, 0, 0)),
        ],
        out_specs=pl.BlockSpec((BLOCK_TOKENS, cols), lambda g, i, off: (i, g)),
    )
    return pl.pallas_call(
        kernel,
        grid_spec=grid_spec,
        out_shape=jax.ShapeDtypeStruct(q_all.shape, q_all.dtype),
        cost_estimate=cost,
        interpret=INTERPRET,
    )(offsets, q_all, win_k, win_v, kv, vv, ms, mv)


def local(queries, keys, values, slash, vertical):
    softmax_scale = HEAD_WIDTH ** (-0.5)
    core_index = lax.axis_index("core")
    seq_index = lax.axis_index("chip") * lax.axis_size("core") + core_index
    head_index = lax.axis_index("head")
    heads = lax.axis_size("head")
    tokens = keys.shape[0]
    joined = jnp.concatenate(
        [keys.reshape(tokens, heads, -1), values.reshape(tokens, heads, -1)], 2
    )
    joined = lax.all_to_all(joined, "head", split_axis=1, concat_axis=0, tiled=True)
    k_cols = keys.shape[1] // heads
    k_all = joined[:, 0, :k_cols]
    v_all = joined[:, 0, k_cols:]
    rows = k_all.shape[0]
    nbd = rows // BLOCK_TOKENS
    kv_local = k_all.shape[1] // HEAD_WIDTH
    query_group = queries.shape[1] // heads // HEAD_WIDTH // kv_local
    width = EXTRA_DIAGONALS + 1
    prev_k, prev_v = shifted((k_all, v_all), ("chip", "core"), 1)
    window_k = jnp.concatenate([prev_k, k_all], 0)
    window_v = jnp.concatenate([prev_v, v_all], 0)
    own_k = k_all.reshape(nbd, BLOCK_TOKENS, kv_local, HEAD_WIDTH)
    own_v = v_all.reshape(nbd, BLOCK_TOKENS, kv_local, HEAD_WIDTH)
    first_head = head_index * kv_local
    local_slash = lax.dynamic_slice_in_dim(slash, first_head, kv_local, 0) + 1
    diagonal_offsets = jnp.concatenate([jnp.zeros((kv_local, 1), jnp.int32), local_slash], 1)
    local_vert = lax.dynamic_slice_in_dim(vertical, first_head, kv_local, 0)
    owner = local_vert // nbd
    inner = local_vert % nbd
    listed = local_vert.shape[1]
    earlier = jnp.arange(listed)[None, :] < jnp.arange(listed)[:, None]
    same_owner = owner[:, :, None] == owner[:, None, :]
    rank = jnp.sum(same_owner & earlier[None], axis=2)
    slots = 2
    mine = (owner == seq_index)[:, None, :] & (rank[:, None, :] == jnp.arange(slots)[None, :, None])
    pick = jnp.sum(jnp.where(mine, inner[:, None, :], 0), axis=2)
    pieces = []
    for group_member in range(kv_local):
        pieces.append(
            jnp.stack(
                [
                    own_k[:, :, group_member][pick[group_member]],
                    own_v[:, :, group_member][pick[group_member]],
                ],
                1,
            )
        )
    pieces, queries = lax.optimization_barrier((jnp.stack(pieces, 0), queries))
    chips = lax.axis_size("chip")
    cores = lax.axis_size("core")
    side = int(round(chips ** 0.5))
    chip_index = lax.axis_index("chip")
    swap = [(c, cores - 1 - c) for c in range(cores)]
    mine = lax.dynamic_index_in_dim(pieces, core_index, 2, keepdims=False)
    sent = lax.dynamic_index_in_dim(pieces, cores - 1 - core_index, 2, keepdims=False)
    stage = jnp.stack([mine, lax.ppermute(sent, "core", swap)], 0)
    q_all = lax.all_to_all(queries, "head", split_axis=1, concat_axis=0, tiled=True)
    for stride in (1, side):
        moved = [stage]
        for step in range(1, side):
            pairs = []
            for chip in range(chips):
                row, col = chip // side, chip % side
                if stride == 1:
                    pairs.append((chip, row * side + (col + step) % side))
                else:
                    pairs.append((chip, ((row + step) % side) * side + col))
            moved.append(lax.ppermute(stage, "chip", pairs))
        stage = jnp.stack(moved, 0)
    owner_chip = owner // cores
    owner_core = owner % cores
    dy = (chip_index // side - owner_chip // side) % side
    dx = (chip_index % side - owner_chip % side) % side
    heads_idx = jnp.arange(kv_local)[:, None]
    part = stage[dy, dx, (owner_core + core_index) % cores, heads_idx, rank]
    part = part.reshape(kv_local, listed * BLOCK_TOKENS, HEAD_WIDTH)
    other = lax.ppermute(part, "core", swap)
    vert_keys = jnp.where(core_index == 0, part, other)
    vert_vals = jnp.where(core_index == 0, other, part)
    qblocks = seq_index * nbd + jnp.arange(nbd, dtype=jnp.int32)
    slash_ok, vert_ok = [], []
    for group_member in range(kv_local):
        offset = diagonal_offsets[group_member]
        block_ok = qblocks[:, None] - offset[None, :] >= 0
        block_ok = jnp.concatenate(
            [block_ok, jnp.zeros((nbd, SLASH_SLOTS - width), jnp.bool_)], 1
        )
        slash_ok.append(jnp.repeat(block_ok, BLOCK_TOKENS, axis=1))
        dist = qblocks[:, None] - local_vert[group_member][None, :]
        hit = jnp.any(dist[:, :, None] == offset[None, None, :], axis=2)
        ok = (dist > 0) & jnp.logical_not(hit)
        vert_ok.append(jnp.repeat(ok, BLOCK_TOKENS, axis=1))
    ms = jnp.stack(slash_ok, 0).astype(jnp.int32)[:, :, None, :]
    mv = jnp.stack(vert_ok, 0).astype(jnp.int32)[:, :, None, :]
    return attend(
        diagonal_offsets, q_all, window_k, window_v, vert_keys, vert_vals, ms, mv,
        query_group, softmax_scale,
    )


def solution(mesh):
    cores = 2
    devices = mesh.devices.reshape(mesh.shape["seq"] // cores, cores, mesh.shape["head"])
    split = Mesh(devices, ("chip", "core", "head"))
    return jax.shard_map(
        local,
        mesh=split,
        in_specs=(
            P(("chip", "core", "head"), None),
            P(("chip", "core", "head"), None),
            P(("chip", "core", "head"), None),
            P(),
            P(),
        ),
        out_specs=P(("chip", "core"), "head"),
        check_vma=False,
    )
```

```python
import jax
import jax.numpy as jnp
from jax import lax
from jax.experimental import pallas as pl
from jax.experimental.pallas import tpu as pltpu
from jax.sharding import Mesh, PartitionSpec as P

HEAD_WIDTH = 128
BLOCK_TOKENS = 64
EXTRA_DIAGONALS = 4
SLASH_SLOTS = 6
INTERPRET = False


def shifted(value, axis, by):
    size = lax.axis_size(axis)
    pairs = [(i, i + by) for i in range(size) if 0 <= i + by < size]
    return lax.ppermute(value, axis, pairs)


def attend_kernel(
    off_ref, q_ref, wk_ref, wv_ref, kv_ref, vv_ref, ms_ref, mv_ref, o_ref, *, group, scale, nbd
):
    g = pl.program_id(0)
    i = pl.program_id(1)
    rows = BLOCK_TOKENS * group
    picked_k, picked_v = [], []
    for j in range(EXTRA_DIAGONALS + 1):
        block = jnp.clip(nbd + i - off_ref[g, j], 0, 2 * nbd - 1)
        start = pl.multiple_of(block * BLOCK_TOKENS, BLOCK_TOKENS)
        picked_k.append(wk_ref[pl.ds(start, BLOCK_TOKENS), :])
        picked_v.append(wv_ref[pl.ds(start, BLOCK_TOKENS), :])
    pad = jnp.zeros(
        ((SLASH_SLOTS - EXTRA_DIAGONALS - 1) * BLOCK_TOKENS, HEAD_WIDTH), wk_ref.dtype
    )
    ks = jnp.concatenate(picked_k + [pad], 0)
    vs = jnp.concatenate(picked_v + [pad], 0)
    q = q_ref[...]
    q_stack = jnp.concatenate(
        [q[:, h * HEAD_WIDTH : (h + 1) * HEAD_WIDTH] for h in range(group)], axis=0
    )
    nt = (((1,), (1,)), ((), ()))
    s_slash = lax.dot_general(q_stack, ks, nt, preferred_element_type=jnp.float32) * scale
    s_vert = lax.dot_general(q_stack, kv_ref[0], nt, preferred_element_type=jnp.float32) * scale
    width = s_slash.shape[1]
    row = jnp.bitwise_and(lax.broadcasted_iota(jnp.int32, (rows, width), 0), BLOCK_TOKENS - 1)
    col = lax.broadcasted_iota(jnp.int32, (rows, width), 1)
    ok_slash = (ms_ref[0, 0] > 0) & ((col >= BLOCK_TOKENS) | (col <= row))
    s_slash = jnp.where(ok_slash, s_slash, -jnp.inf)
    s_vert = jnp.where(mv_ref[0, 0] > 0, s_vert, -jnp.inf)
    top = jnp.maximum(
        jnp.max(s_slash, axis=1, keepdims=True), jnp.max(s_vert, axis=1, keepdims=True)
    )
    w_slash = jnp.exp(s_slash - top)
    w_vert = jnp.exp(s_vert - top)
    total = jnp.sum(w_slash, axis=1, keepdims=True) + jnp.sum(w_vert, axis=1, keepdims=True)
    acc = jnp.dot(w_slash.astype(jnp.bfloat16), vs, preferred_element_type=jnp.float32)
    acc = acc + jnp.dot(
        w_vert.astype(jnp.bfloat16), vv_ref[0], preferred_element_type=jnp.float32
    )
    res = (acc / total).astype(o_ref.dtype)
    for h in range(group):
        o_ref[:, h * HEAD_WIDTH : (h + 1) * HEAD_WIDTH] = res[
            h * BLOCK_TOKENS : (h + 1) * BLOCK_TOKENS
        ]


def attend(offsets, q_all, win_k, win_v, kv, vv, ms, mv, group, scale):
    kv_local, nbd = ms.shape[0], ms.shape[1]
    slash_rows = ms.shape[3]
    vert_rows = kv.shape[1]
    window_rows = win_k.shape[0]
    cols = group * HEAD_WIDTH
    rows = BLOCK_TOKENS * group
    steps = kv_local * nbd
    flops = steps * 4 * rows * (slash_rows + vert_rows) * HEAD_WIDTH
    cost = pl.CostEstimate(
        flops=flops,
        transcendentals=steps * rows * (slash_rows + vert_rows),
        bytes_accessed=2 * (2 * q_all.size + win_k.size + win_v.size + kv.size + vv.size),
    )
    kernel = lambda *refs: attend_kernel(*refs, group=group, scale=scale, nbd=nbd)
    grid_spec = pltpu.PrefetchScalarGridSpec(
        num_scalar_prefetch=1,
        grid=(kv_local, nbd),
        in_specs=[
            pl.BlockSpec((BLOCK_TOKENS, cols), lambda g, i, off: (i, g)),
            pl.BlockSpec((window_rows, HEAD_WIDTH), lambda g, i, off: (0, g)),
            pl.BlockSpec((window_rows, HEAD_WIDTH), lambda g, i, off: (0, g)),
            pl.BlockSpec((1, vert_rows, HEAD_WIDTH), lambda g, i, off: (g, 0, 0)),
            pl.BlockSpec((1, vert_rows, HEAD_WIDTH), lambda g, i, off: (g, 0, 0)),
            pl.BlockSpec((1, 1, 1, slash_rows), lambda g, i, off: (g, i, 0, 0)),
            pl.BlockSpec((1, 1, 1, vert_rows), lambda g, i, off: (g, i, 0, 0)),
        ],
        out_specs=pl.BlockSpec((BLOCK_TOKENS, cols), lambda g, i, off: (i, g)),
    )
    return pl.pallas_call(
        kernel,
        grid_spec=grid_spec,
        out_shape=jax.ShapeDtypeStruct(q_all.shape, q_all.dtype),
        cost_estimate=cost,
        interpret=INTERPRET,
    )(offsets, q_all, win_k, win_v, kv, vv, ms, mv)


def local(queries, keys, values, slash, vertical):
    softmax_scale = HEAD_WIDTH ** (-0.5)
    core_index = lax.axis_index("core")
    seq_index = lax.axis_index("chip") * lax.axis_size("core") + core_index
    head_index = lax.axis_index("head")
    heads = lax.axis_size("head")
    tokens = keys.shape[0]
    joined = jnp.concatenate(
        [keys.reshape(tokens, heads, -1), values.reshape(tokens, heads, -1)], 2
    )
    joined = lax.all_to_all(joined, "head", split_axis=1, concat_axis=0, tiled=True)
    k_cols = keys.shape[1] // heads
    k_all = joined[:, 0, :k_cols]
    v_all = joined[:, 0, k_cols:]
    rows = k_all.shape[0]
    nbd = rows // BLOCK_TOKENS
    kv_local = k_all.shape[1] // HEAD_WIDTH
    query_group = queries.shape[1] // heads // HEAD_WIDTH // kv_local
    width = EXTRA_DIAGONALS + 1
    prev_k, prev_v = shifted((k_all, v_all), ("chip", "core"), 1)
    own_k = k_all.reshape(nbd, BLOCK_TOKENS, kv_local, HEAD_WIDTH)
    own_v = v_all.reshape(nbd, BLOCK_TOKENS, kv_local, HEAD_WIDTH)
    first_head = head_index * kv_local
    local_slash = lax.dynamic_slice_in_dim(slash, first_head, kv_local, 0) + 1
    diagonal_offsets = jnp.concatenate([jnp.zeros((kv_local, 1), jnp.int32), local_slash], 1)
    local_vert = lax.dynamic_slice_in_dim(vertical, first_head, kv_local, 0)
    owner = local_vert // nbd
    inner = local_vert % nbd
    listed = local_vert.shape[1]
    earlier = jnp.arange(listed)[None, :] < jnp.arange(listed)[:, None]
    same_owner = owner[:, :, None] == owner[:, None, :]
    rank = jnp.sum(same_owner & earlier[None], axis=2)
    slots = 2
    mine = (owner == seq_index)[:, None, :] & (rank[:, None, :] == jnp.arange(slots)[None, :, None])
    pick = jnp.sum(jnp.where(mine, inner[:, None, :], 0), axis=2)
    pieces = []
    for group_member in range(kv_local):
        pieces.append(
            jnp.stack(
                [
                    own_k[:, :, group_member][pick[group_member]],
                    own_v[:, :, group_member][pick[group_member]],
                ],
                1,
            )
        )
    pieces, queries = lax.optimization_barrier((jnp.stack(pieces, 0), queries))
    chips = lax.axis_size("chip")
    cores = lax.axis_size("core")
    side = int(round(chips ** 0.5))
    chip_index = lax.axis_index("chip")
    swap = [(c, cores - 1 - c) for c in range(cores)]
    mine = lax.dynamic_index_in_dim(pieces, core_index, 2, keepdims=False)
    sent = lax.dynamic_index_in_dim(pieces, cores - 1 - core_index, 2, keepdims=False)
    stage = jnp.stack([mine, lax.ppermute(sent, "core", swap)], 0)
    q_all = lax.all_to_all(queries, "head", split_axis=1, concat_axis=0, tiled=True)
    for stride in (1, side):
        moved = [stage]
        for step in range(1, side):
            pairs = []
            for chip in range(chips):
                row, col = chip // side, chip % side
                if stride == 1:
                    pairs.append((chip, row * side + (col + step) % side))
                else:
                    pairs.append((chip, ((row + step) % side) * side + col))
            moved.append(lax.ppermute(stage, "chip", pairs))
        stage = jnp.stack(moved, 0)
        if stride == 1:
            stage, q_all, prev_k, prev_v = lax.optimization_barrier((stage, q_all, prev_k, prev_v))
    owner_chip = owner // cores
    owner_core = owner % cores
    dy = (chip_index // side - owner_chip // side) % side
    dx = (chip_index % side - owner_chip % side) % side
    heads_idx = jnp.arange(kv_local)[:, None]
    part = stage[dy, dx, (owner_core + core_index) % cores, heads_idx, rank]
    part = part.reshape(kv_local, listed * BLOCK_TOKENS, HEAD_WIDTH)
    other = lax.ppermute(part, "core", swap)
    vert_keys = jnp.where(core_index == 0, part, other)
    vert_vals = jnp.where(core_index == 0, other, part)
    window_k = jnp.concatenate([prev_k, k_all], 0)
    window_v = jnp.concatenate([prev_v, v_all], 0)
    qblocks = seq_index * nbd + jnp.arange(nbd, dtype=jnp.int32)
    slash_ok, vert_ok = [], []
    for group_member in range(kv_local):
        offset = diagonal_offsets[group_member]
        block_ok = qblocks[:, None] - offset[None, :] >= 0
        block_ok = jnp.concatenate(
            [block_ok, jnp.zeros((nbd, SLASH_SLOTS - width), jnp.bool_)], 1
        )
        slash_ok.append(jnp.repeat(block_ok, BLOCK_TOKENS, axis=1))
        dist = qblocks[:, None] - local_vert[group_member][None, :]
        hit = jnp.any(dist[:, :, None] == offset[None, None, :], axis=2)
        ok = (dist > 0) & jnp.logical_not(hit)
        vert_ok.append(jnp.repeat(ok, BLOCK_TOKENS, axis=1))
    ms = jnp.stack(slash_ok, 0).astype(jnp.int32)[:, :, None, :]
    mv = jnp.stack(vert_ok, 0).astype(jnp.int32)[:, :, None, :]
    return attend(
        diagonal_offsets, q_all, window_k, window_v, vert_keys, vert_vals, ms, mv,
        query_group, softmax_scale,
    )


def solution(mesh):
    cores = 2
    devices = mesh.devices.reshape(mesh.shape["seq"] // cores, cores, mesh.shape["head"])
    split = Mesh(devices, ("chip", "core", "head"))
    return jax.shard_map(
        local,
        mesh=split,
        in_specs=(
            P(("chip", "core", "head"), None),
            P(("chip", "core", "head"), None),
            P(("chip", "core", "head"), None),
            P(),
            P(),
        ),
        out_specs=P(("chip", "core"), "head"),
        check_vma=False,
    )
```

```python
import jax
import jax.numpy as jnp
from jax import lax
from jax.experimental import pallas as pl
from jax.experimental.pallas import tpu as pltpu
from jax.sharding import Mesh, PartitionSpec as P

HEAD_WIDTH = 128
BLOCK_TOKENS = 64
EXTRA_DIAGONALS = 4
SLASH_SLOTS = 6
INTERPRET = False


def shifted(value, axis, by):
    size = lax.axis_size(axis)
    pairs = [(i, i + by) for i in range(size) if 0 <= i + by < size]
    return lax.ppermute(value, axis, pairs)


def attend_kernel(
    off_ref, q_ref, wk_ref, wv_ref, kv_ref, vv_ref, ms_ref, mv_ref, o_ref, *, group, scale, nbd
):
    g = pl.program_id(0)
    i = pl.program_id(1)
    rows = BLOCK_TOKENS * group
    picked_k, picked_v = [], []
    for j in range(EXTRA_DIAGONALS + 1):
        block = jnp.clip(nbd + i - off_ref[g, j], 0, 2 * nbd - 1)
        start = pl.multiple_of(block * BLOCK_TOKENS, BLOCK_TOKENS)
        picked_k.append(wk_ref[pl.ds(start, BLOCK_TOKENS), :])
        picked_v.append(wv_ref[pl.ds(start, BLOCK_TOKENS), :])
    pad = jnp.zeros(
        ((SLASH_SLOTS - EXTRA_DIAGONALS - 1) * BLOCK_TOKENS, HEAD_WIDTH), wk_ref.dtype
    )
    ks = jnp.concatenate(picked_k + [pad], 0)
    vs = jnp.concatenate(picked_v + [pad], 0)
    q = q_ref[...]
    q_stack = jnp.concatenate(
        [q[:, h * HEAD_WIDTH : (h + 1) * HEAD_WIDTH] for h in range(group)], axis=0
    )
    nt = (((1,), (1,)), ((), ()))
    s_slash = lax.dot_general(q_stack, ks, nt, preferred_element_type=jnp.float32) * scale
    s_vert = lax.dot_general(q_stack, kv_ref[0], nt, preferred_element_type=jnp.float32) * scale
    width = s_slash.shape[1]
    row = jnp.bitwise_and(lax.broadcasted_iota(jnp.int32, (rows, width), 0), BLOCK_TOKENS - 1)
    col = lax.broadcasted_iota(jnp.int32, (rows, width), 1)
    ok_slash = (ms_ref[0, 0] > 0) & ((col >= BLOCK_TOKENS) | (col <= row))
    s_slash = jnp.where(ok_slash, s_slash, -jnp.inf)
    s_vert = jnp.where(mv_ref[0, 0] > 0, s_vert, -jnp.inf)
    top = jnp.maximum(
        jnp.max(s_slash, axis=1, keepdims=True), jnp.max(s_vert, axis=1, keepdims=True)
    )
    w_slash = jnp.exp(s_slash - top)
    w_vert = jnp.exp(s_vert - top)
    total = jnp.sum(w_slash, axis=1, keepdims=True) + jnp.sum(w_vert, axis=1, keepdims=True)
    acc = jnp.dot(w_slash.astype(jnp.bfloat16), vs, preferred_element_type=jnp.float32)
    acc = acc + jnp.dot(
        w_vert.astype(jnp.bfloat16), vv_ref[0], preferred_element_type=jnp.float32
    )
    res = (acc / total).astype(o_ref.dtype)
    for h in range(group):
        o_ref[:, h * HEAD_WIDTH : (h + 1) * HEAD_WIDTH] = res[
            h * BLOCK_TOKENS : (h + 1) * BLOCK_TOKENS
        ]


def attend(offsets, q_all, win_k, win_v, kv, vv, ms, mv, group, scale):
    kv_local, nbd = ms.shape[0], ms.shape[1]
    slash_rows = ms.shape[3]
    vert_rows = kv.shape[1]
    window_rows = win_k.shape[0]
    cols = group * HEAD_WIDTH
    rows = BLOCK_TOKENS * group
    steps = kv_local * nbd
    flops = steps * 4 * rows * (slash_rows + vert_rows) * HEAD_WIDTH
    cost = pl.CostEstimate(
        flops=flops,
        transcendentals=steps * rows * (slash_rows + vert_rows),
        bytes_accessed=2 * (2 * q_all.size + win_k.size + win_v.size + kv.size + vv.size),
    )
    kernel = lambda *refs: attend_kernel(*refs, group=group, scale=scale, nbd=nbd)
    grid_spec = pltpu.PrefetchScalarGridSpec(
        num_scalar_prefetch=1,
        grid=(kv_local, nbd),
        in_specs=[
            pl.BlockSpec((BLOCK_TOKENS, cols), lambda g, i, off: (i, g)),
            pl.BlockSpec((window_rows, HEAD_WIDTH), lambda g, i, off: (0, g)),
            pl.BlockSpec((window_rows, HEAD_WIDTH), lambda g, i, off: (0, g)),
            pl.BlockSpec((1, vert_rows, HEAD_WIDTH), lambda g, i, off: (g, 0, 0)),
            pl.BlockSpec((1, vert_rows, HEAD_WIDTH), lambda g, i, off: (g, 0, 0)),
            pl.BlockSpec((1, 1, 1, slash_rows), lambda g, i, off: (g, i, 0, 0)),
            pl.BlockSpec((1, 1, 1, vert_rows), lambda g, i, off: (g, i, 0, 0)),
        ],
        out_specs=pl.BlockSpec((BLOCK_TOKENS, cols), lambda g, i, off: (i, g)),
    )
    return pl.pallas_call(
        kernel,
        grid_spec=grid_spec,
        out_shape=jax.ShapeDtypeStruct(q_all.shape, q_all.dtype),
        cost_estimate=cost,
        interpret=INTERPRET,
    )(offsets, q_all, win_k, win_v, kv, vv, ms, mv)


def side_inputs(prev_k, prev_v, k_all, v_all, diagonal_offsets, local_vert, seq_index, nbd):
    kv_local, width = diagonal_offsets.shape
    window_k = jnp.concatenate([prev_k, k_all], 0)
    window_v = jnp.concatenate([prev_v, v_all], 0)
    qblocks = seq_index * nbd + jnp.arange(nbd, dtype=jnp.int32)
    slash_ok, vert_ok = [], []
    for group_member in range(kv_local):
        offset = diagonal_offsets[group_member]
        block_ok = qblocks[:, None] - offset[None, :] >= 0
        block_ok = jnp.concatenate(
            [block_ok, jnp.zeros((nbd, SLASH_SLOTS - width), jnp.bool_)], 1
        )
        slash_ok.append(jnp.repeat(block_ok, BLOCK_TOKENS, axis=1))
        dist = qblocks[:, None] - local_vert[group_member][None, :]
        hit = jnp.any(dist[:, :, None] == offset[None, None, :], axis=2)
        ok = (dist > 0) & jnp.logical_not(hit)
        vert_ok.append(jnp.repeat(ok, BLOCK_TOKENS, axis=1))
    ms = jnp.stack(slash_ok, 0).astype(jnp.int32)[:, :, None, :]
    mv = jnp.stack(vert_ok, 0).astype(jnp.int32)[:, :, None, :]
    return window_k, window_v, ms, mv


def local(queries, keys, values, slash, vertical):
    softmax_scale = HEAD_WIDTH ** (-0.5)
    core_index = lax.axis_index("core")
    seq_index = lax.axis_index("chip") * lax.axis_size("core") + core_index
    head_index = lax.axis_index("head")
    heads = lax.axis_size("head")
    tokens = keys.shape[0]
    joined = jnp.concatenate(
        [keys.reshape(tokens, heads, -1), values.reshape(tokens, heads, -1)], 2
    )
    joined = lax.all_to_all(joined, "head", split_axis=1, concat_axis=0, tiled=True)
    k_cols = keys.shape[1] // heads
    k_all = joined[:, 0, :k_cols]
    v_all = joined[:, 0, k_cols:]
    rows = k_all.shape[0]
    nbd = rows // BLOCK_TOKENS
    kv_local = k_all.shape[1] // HEAD_WIDTH
    query_group = queries.shape[1] // heads // HEAD_WIDTH // kv_local
    width = EXTRA_DIAGONALS + 1
    prev_k, prev_v = shifted((k_all, v_all), ("chip", "core"), 1)
    own_k = k_all.reshape(nbd, BLOCK_TOKENS, kv_local, HEAD_WIDTH)
    own_v = v_all.reshape(nbd, BLOCK_TOKENS, kv_local, HEAD_WIDTH)
    first_head = head_index * kv_local
    local_slash = lax.dynamic_slice_in_dim(slash, first_head, kv_local, 0) + 1
    diagonal_offsets = jnp.concatenate([jnp.zeros((kv_local, 1), jnp.int32), local_slash], 1)
    local_vert = lax.dynamic_slice_in_dim(vertical, first_head, kv_local, 0)
    owner = local_vert // nbd
    inner = local_vert % nbd
    listed = local_vert.shape[1]
    earlier = jnp.arange(listed)[None, :] < jnp.arange(listed)[:, None]
    same_owner = owner[:, :, None] == owner[:, None, :]
    rank = jnp.sum(same_owner & earlier[None], axis=2)
    slots = 2
    mine = (owner == seq_index)[:, None, :] & (rank[:, None, :] == jnp.arange(slots)[None, :, None])
    pick = jnp.sum(jnp.where(mine, inner[:, None, :], 0), axis=2)
    pieces = []
    for group_member in range(kv_local):
        pieces.append(
            jnp.stack(
                [
                    own_k[:, :, group_member][pick[group_member]],
                    own_v[:, :, group_member][pick[group_member]],
                ],
                1,
            )
        )
    pieces, queries = lax.optimization_barrier((jnp.stack(pieces, 0), queries))
    chips = lax.axis_size("chip")
    cores = lax.axis_size("core")
    side = int(round(chips ** 0.5))
    chip_index = lax.axis_index("chip")
    swap = [(c, cores - 1 - c) for c in range(cores)]
    mine = lax.dynamic_index_in_dim(pieces, core_index, 2, keepdims=False)
    sent = lax.dynamic_index_in_dim(pieces, cores - 1 - core_index, 2, keepdims=False)
    stage = jnp.stack([mine, lax.ppermute(sent, "core", swap)], 0)
    q_all = lax.all_to_all(queries, "head", split_axis=1, concat_axis=0, tiled=True)
    for stride in (1, side):
        moved = [stage]
        for step in range(1, side):
            pairs = []
            for chip in range(chips):
                row, col = chip // side, chip % side
                if stride == 1:
                    pairs.append((chip, row * side + (col + step) % side))
                else:
                    pairs.append((chip, ((row + step) % side) * side + col))
            moved.append(lax.ppermute(stage, "chip", pairs))
        stage = jnp.stack(moved, 0)
        if stride == 1:
            stage, q_all, prev_k, prev_v, diagonal_offsets, local_vert = lax.optimization_barrier(
                (stage, q_all, prev_k, prev_v, diagonal_offsets, local_vert)
            )
            window_k, window_v, ms, mv = side_inputs(
                prev_k, prev_v, k_all, v_all, diagonal_offsets, local_vert, seq_index, nbd
            )
        else:
            stage, window_k, window_v, ms, mv = lax.optimization_barrier(
                (stage, window_k, window_v, ms, mv)
            )
    owner_chip = owner // cores
    owner_core = owner % cores
    dy = (chip_index // side - owner_chip // side) % side
    dx = (chip_index % side - owner_chip % side) % side
    heads_idx = jnp.arange(kv_local)[:, None]
    part = stage[dy, dx, (owner_core + core_index) % cores, heads_idx, rank]
    part = part.reshape(kv_local, listed * BLOCK_TOKENS, HEAD_WIDTH)
    other = lax.ppermute(part, "core", swap)
    vert_keys = jnp.where(core_index == 0, part, other)
    vert_vals = jnp.where(core_index == 0, other, part)
    return attend(
        diagonal_offsets, q_all, window_k, window_v, vert_keys, vert_vals, ms, mv,
        query_group, softmax_scale,
    )


def solution(mesh):
    cores = 2
    devices = mesh.devices.reshape(mesh.shape["seq"] // cores, cores, mesh.shape["head"])
    split = Mesh(devices, ("chip", "core", "head"))
    return jax.shard_map(
        local,
        mesh=split,
        in_specs=(
            P(("chip", "core", "head"), None),
            P(("chip", "core", "head"), None),
            P(("chip", "core", "head"), None),
            P(),
            P(),
        ),
        out_specs=P(("chip", "core"), "head"),
        check_vma=False,
    )
```

```python
import jax
import jax.numpy as jnp
from jax import lax
from jax.experimental import pallas as pl
from jax.experimental.pallas import tpu as pltpu
from jax.sharding import Mesh, PartitionSpec as P

HEAD_WIDTH = 128
BLOCK_TOKENS = 64
EXTRA_DIAGONALS = 4
SLASH_SLOTS = 6
INTERPRET = False


def shifted(value, axis, by):
    size = lax.axis_size(axis)
    pairs = [(i, i + by) for i in range(size) if 0 <= i + by < size]
    return lax.ppermute(value, axis, pairs)


def attend_kernel(
    off_ref, q_ref, wk_ref, wv_ref, kv_ref, vv_ref, ms_ref, mv_ref, o_ref, *, group, scale, nbd
):
    g = pl.program_id(0)
    i = pl.program_id(1)
    rows = BLOCK_TOKENS * group
    picked_k, picked_v = [], []
    for j in range(EXTRA_DIAGONALS + 1):
        block = jnp.clip(nbd + i - off_ref[g, j], 0, 2 * nbd - 1)
        start = pl.multiple_of(block * BLOCK_TOKENS, BLOCK_TOKENS)
        picked_k.append(wk_ref[pl.ds(start, BLOCK_TOKENS), :])
        picked_v.append(wv_ref[pl.ds(start, BLOCK_TOKENS), :])
    pad = jnp.zeros(
        ((SLASH_SLOTS - EXTRA_DIAGONALS - 1) * BLOCK_TOKENS, HEAD_WIDTH), wk_ref.dtype
    )
    ks = jnp.concatenate(picked_k + [pad], 0)
    vs = jnp.concatenate(picked_v + [pad], 0)
    q = q_ref[...]
    q_stack = jnp.concatenate(
        [q[:, h * HEAD_WIDTH : (h + 1) * HEAD_WIDTH] for h in range(group)], axis=0
    )
    nt = (((1,), (1,)), ((), ()))
    s_slash = lax.dot_general(q_stack, ks, nt, preferred_element_type=jnp.float32) * scale
    s_vert = lax.dot_general(q_stack, kv_ref[0], nt, preferred_element_type=jnp.float32) * scale
    width = s_slash.shape[1]
    row = jnp.bitwise_and(lax.broadcasted_iota(jnp.int32, (rows, width), 0), BLOCK_TOKENS - 1)
    col = lax.broadcasted_iota(jnp.int32, (rows, width), 1)
    ok_slash = (ms_ref[0, 0] > 0) & ((col >= BLOCK_TOKENS) | (col <= row))
    s_slash = jnp.where(ok_slash, s_slash, -jnp.inf)
    s_vert = jnp.where(mv_ref[0, 0] > 0, s_vert, -jnp.inf)
    top = jnp.maximum(
        jnp.max(s_slash, axis=1, keepdims=True), jnp.max(s_vert, axis=1, keepdims=True)
    )
    w_slash = jnp.exp(s_slash - top)
    w_vert = jnp.exp(s_vert - top)
    total = jnp.sum(w_slash, axis=1, keepdims=True) + jnp.sum(w_vert, axis=1, keepdims=True)
    acc = jnp.dot(w_slash.astype(jnp.bfloat16), vs, preferred_element_type=jnp.float32)
    acc = acc + jnp.dot(
        w_vert.astype(jnp.bfloat16), vv_ref[0], preferred_element_type=jnp.float32
    )
    res = (acc / total).astype(o_ref.dtype)
    for h in range(group):
        o_ref[:, h * HEAD_WIDTH : (h + 1) * HEAD_WIDTH] = res[
            h * BLOCK_TOKENS : (h + 1) * BLOCK_TOKENS
        ]


def attend(offsets, q_all, win_k, win_v, kv, vv, ms, mv, group, scale):
    kv_local, nbd = ms.shape[0], ms.shape[1]
    slash_rows = ms.shape[3]
    vert_rows = kv.shape[1]
    window_rows = win_k.shape[0]
    cols = group * HEAD_WIDTH
    rows = BLOCK_TOKENS * group
    steps = kv_local * nbd
    flops = steps * 4 * rows * (slash_rows + vert_rows) * HEAD_WIDTH
    cost = pl.CostEstimate(
        flops=flops,
        transcendentals=steps * rows * (slash_rows + vert_rows),
        bytes_accessed=2 * (2 * q_all.size + win_k.size + win_v.size + kv.size + vv.size),
    )
    kernel = lambda *refs: attend_kernel(*refs, group=group, scale=scale, nbd=nbd)
    grid_spec = pltpu.PrefetchScalarGridSpec(
        num_scalar_prefetch=1,
        grid=(kv_local, nbd),
        in_specs=[
            pl.BlockSpec((BLOCK_TOKENS, cols), lambda g, i, off: (i, g)),
            pl.BlockSpec((window_rows, HEAD_WIDTH), lambda g, i, off: (0, g)),
            pl.BlockSpec((window_rows, HEAD_WIDTH), lambda g, i, off: (0, g)),
            pl.BlockSpec((1, vert_rows, HEAD_WIDTH), lambda g, i, off: (g, 0, 0)),
            pl.BlockSpec((1, vert_rows, HEAD_WIDTH), lambda g, i, off: (g, 0, 0)),
            pl.BlockSpec((1, 1, 1, slash_rows), lambda g, i, off: (g, i, 0, 0)),
            pl.BlockSpec((1, 1, 1, vert_rows), lambda g, i, off: (g, i, 0, 0)),
        ],
        out_specs=pl.BlockSpec((BLOCK_TOKENS, cols), lambda g, i, off: (i, g)),
    )
    return pl.pallas_call(
        kernel,
        grid_spec=grid_spec,
        out_shape=jax.ShapeDtypeStruct(q_all.shape, q_all.dtype),
        cost_estimate=cost,
        interpret=INTERPRET,
    )(offsets, q_all, win_k, win_v, kv, vv, ms, mv)


def side_inputs(prev_k, prev_v, k_all, v_all, diagonal_offsets, local_vert, seq_index, nbd):
    kv_local, width = diagonal_offsets.shape
    window_k = jnp.concatenate([prev_k, k_all], 0)
    window_v = jnp.concatenate([prev_v, v_all], 0)
    qblocks = seq_index * nbd + jnp.arange(nbd, dtype=jnp.int32)
    slash_ok, vert_ok = [], []
    for group_member in range(kv_local):
        offset = diagonal_offsets[group_member]
        block_ok = qblocks[:, None] - offset[None, :] >= 0
        block_ok = jnp.concatenate(
            [block_ok, jnp.zeros((nbd, SLASH_SLOTS - width), jnp.bool_)], 1
        )
        slash_ok.append(jnp.repeat(block_ok, BLOCK_TOKENS, axis=1))
        dist = qblocks[:, None] - local_vert[group_member][None, :]
        hit = jnp.any(dist[:, :, None] == offset[None, None, :], axis=2)
        ok = (dist > 0) & jnp.logical_not(hit)
        vert_ok.append(jnp.repeat(ok, BLOCK_TOKENS, axis=1))
    ms = jnp.stack(slash_ok, 0).astype(jnp.int32)[:, :, None, :]
    mv = jnp.stack(vert_ok, 0).astype(jnp.int32)[:, :, None, :]
    return window_k, window_v, ms, mv


def local(queries, keys, values, slash, vertical):
    softmax_scale = HEAD_WIDTH ** (-0.5)
    core_index = lax.axis_index("core")
    seq_index = lax.axis_index("chip") * lax.axis_size("core") + core_index
    head_index = lax.axis_index("head")
    heads = lax.axis_size("head")
    tokens = keys.shape[0]
    joined = jnp.concatenate(
        [keys.reshape(tokens, heads, -1), values.reshape(tokens, heads, -1)], 2
    )
    joined = lax.all_to_all(joined, "head", split_axis=1, concat_axis=0, tiled=True)
    k_cols = keys.shape[1] // heads
    k_all = joined[:, 0, :k_cols]
    v_all = joined[:, 0, k_cols:]
    rows = k_all.shape[0]
    nbd = rows // BLOCK_TOKENS
    kv_local = k_all.shape[1] // HEAD_WIDTH
    query_group = queries.shape[1] // heads // HEAD_WIDTH // kv_local
    width = EXTRA_DIAGONALS + 1
    prev_k, prev_v = shifted((k_all, v_all), ("chip", "core"), 1)
    own_k = k_all.reshape(nbd, BLOCK_TOKENS, kv_local, HEAD_WIDTH)
    own_v = v_all.reshape(nbd, BLOCK_TOKENS, kv_local, HEAD_WIDTH)
    first_head = head_index * kv_local
    local_slash = lax.dynamic_slice_in_dim(slash, first_head, kv_local, 0) + 1
    diagonal_offsets = jnp.concatenate([jnp.zeros((kv_local, 1), jnp.int32), local_slash], 1)
    local_vert = lax.dynamic_slice_in_dim(vertical, first_head, kv_local, 0)
    owner = local_vert // nbd
    inner = local_vert % nbd
    listed = local_vert.shape[1]
    earlier = jnp.arange(listed)[None, :] < jnp.arange(listed)[:, None]
    same_owner = owner[:, :, None] == owner[:, None, :]
    rank = jnp.sum(same_owner & earlier[None], axis=2)
    slots = 2
    mine = (owner == seq_index)[:, None, :] & (rank[:, None, :] == jnp.arange(slots)[None, :, None])
    pick = jnp.sum(jnp.where(mine, inner[:, None, :], 0), axis=2)
    pieces = []
    for group_member in range(kv_local):
        pieces.append(
            jnp.stack(
                [
                    own_k[:, :, group_member][pick[group_member]],
                    own_v[:, :, group_member][pick[group_member]],
                ],
                1,
            )
        )
    pieces, queries = lax.optimization_barrier((jnp.stack(pieces, 0), queries))
    chips = lax.axis_size("chip")
    cores = lax.axis_size("core")
    side = int(round(chips ** 0.5))
    assert side == 4 and side * side == chips
    chip_index = lax.axis_index("chip")
    swap = [(c, cores - 1 - c) for c in range(cores)]
    mine = lax.dynamic_index_in_dim(pieces, core_index, 2, keepdims=False)
    sent = lax.dynamic_index_in_dim(pieces, cores - 1 - core_index, 2, keepdims=False)
    stage = jnp.stack([mine, lax.ppermute(sent, "core", swap)], 0)
    q_all = lax.all_to_all(queries, "head", split_axis=1, concat_axis=0, tiled=True)
    for stride in (1, side):
        def shift(value, step):
            pairs = []
            for chip in range(chips):
                row, col = chip // side, chip % side
                if stride == 1:
                    pairs.append((chip, row * side + (col + step) % side))
                else:
                    pairs.append((chip, ((row + step) % side) * side + col))
            return lax.ppermute(value, "chip", pairs)

        split = stage.ndim - 4
        ahead = shift(stage, 1)
        behind = shift(stage, side - 1)
        far = jnp.concatenate(
            [
                shift(lax.index_in_dim(ahead, 0, split), 1),
                shift(lax.index_in_dim(behind, 1, split), side - 1),
            ],
            split,
        )
        stage = jnp.stack([stage, ahead, far, behind], 0)
        if stride == 1:
            stage, q_all, prev_k, prev_v, diagonal_offsets, local_vert = lax.optimization_barrier(
                (stage, q_all, prev_k, prev_v, diagonal_offsets, local_vert)
            )
            window_k, window_v, ms, mv = side_inputs(
                prev_k, prev_v, k_all, v_all, diagonal_offsets, local_vert, seq_index, nbd
            )
        else:
            stage, window_k, window_v, ms, mv = lax.optimization_barrier(
                (stage, window_k, window_v, ms, mv)
            )
    owner_chip = owner // cores
    owner_core = owner % cores
    dy = (chip_index // side - owner_chip // side) % side
    dx = (chip_index % side - owner_chip % side) % side
    heads_idx = jnp.arange(kv_local)[:, None]
    part = stage[dy, dx, (owner_core + core_index) % cores, heads_idx, rank]
    part = part.reshape(kv_local, listed * BLOCK_TOKENS, HEAD_WIDTH)
    other = lax.ppermute(part, "core", swap)
    vert_keys = jnp.where(core_index == 0, part, other)
    vert_vals = jnp.where(core_index == 0, other, part)
    return attend(
        diagonal_offsets, q_all, window_k, window_v, vert_keys, vert_vals, ms, mv,
        query_group, softmax_scale,
    )


def solution(mesh):
    cores = 2
    devices = mesh.devices.reshape(mesh.shape["seq"] // cores, cores, mesh.shape["head"])
    split = Mesh(devices, ("chip", "core", "head"))
    return jax.shard_map(
        local,
        mesh=split,
        in_specs=(
            P(("chip", "core", "head"), None),
            P(("chip", "core", "head"), None),
            P(("chip", "core", "head"), None),
            P(),
            P(),
        ),
        out_specs=P(("chip", "core"), "head"),
        check_vma=False,
    )
```

```python
import jax
import jax.numpy as jnp
from jax import lax
from jax.experimental import pallas as pl
from jax.experimental.pallas import tpu as pltpu
from jax.sharding import Mesh, PartitionSpec as P

HEAD_WIDTH = 128
BLOCK_TOKENS = 64
EXTRA_DIAGONALS = 4
SLASH_SLOTS = 6
INTERPRET = False


def shifted(value, axis, by):
    size = lax.axis_size(axis)
    pairs = [(i, i + by) for i in range(size) if 0 <= i + by < size]
    return lax.ppermute(value, axis, pairs)


def attend_kernel(
    off_ref, q_ref, wk_ref, wv_ref, kv_ref, vv_ref, ms_ref, mv_ref, o_ref, *, group, scale, nbd
):
    g = pl.program_id(0)
    i = pl.program_id(1)
    rows = BLOCK_TOKENS * group
    picked_k, picked_v = [], []
    for j in range(EXTRA_DIAGONALS + 1):
        block = jnp.clip(nbd + i - off_ref[g, j], 0, 2 * nbd - 1)
        start = pl.multiple_of(block * BLOCK_TOKENS, BLOCK_TOKENS)
        picked_k.append(wk_ref[pl.ds(start, BLOCK_TOKENS), :])
        picked_v.append(wv_ref[pl.ds(start, BLOCK_TOKENS), :])
    pad = jnp.zeros(
        ((SLASH_SLOTS - EXTRA_DIAGONALS - 1) * BLOCK_TOKENS, HEAD_WIDTH), wk_ref.dtype
    )
    ks = jnp.concatenate(picked_k + [pad], 0)
    vs = jnp.concatenate(picked_v + [pad], 0)
    q = q_ref[...]
    q_stack = jnp.concatenate(
        [q[:, h * HEAD_WIDTH : (h + 1) * HEAD_WIDTH] for h in range(group)], axis=0
    )
    nt = (((1,), (1,)), ((), ()))
    s_slash = lax.dot_general(q_stack, ks, nt, preferred_element_type=jnp.float32) * scale
    s_vert = lax.dot_general(q_stack, kv_ref[0], nt, preferred_element_type=jnp.float32) * scale
    width = s_slash.shape[1]
    row = jnp.bitwise_and(lax.broadcasted_iota(jnp.int32, (rows, width), 0), BLOCK_TOKENS - 1)
    col = lax.broadcasted_iota(jnp.int32, (rows, width), 1)
    ok_slash = (ms_ref[0, 0] > 0) & ((col >= BLOCK_TOKENS) | (col <= row))
    s_slash = jnp.where(ok_slash, s_slash, -jnp.inf)
    s_vert = jnp.where(mv_ref[0, 0] > 0, s_vert, -jnp.inf)
    top = jnp.maximum(
        jnp.max(s_slash, axis=1, keepdims=True), jnp.max(s_vert, axis=1, keepdims=True)
    )
    w_slash = jnp.exp(s_slash - top)
    w_vert = jnp.exp(s_vert - top)
    total = jnp.sum(w_slash, axis=1, keepdims=True) + jnp.sum(w_vert, axis=1, keepdims=True)
    acc = jnp.dot(w_slash.astype(jnp.bfloat16), vs, preferred_element_type=jnp.float32)
    acc = acc + jnp.dot(
        w_vert.astype(jnp.bfloat16), vv_ref[0], preferred_element_type=jnp.float32
    )
    res = (acc / total).astype(o_ref.dtype)
    for h in range(group):
        o_ref[:, h * HEAD_WIDTH : (h + 1) * HEAD_WIDTH] = res[
            h * BLOCK_TOKENS : (h + 1) * BLOCK_TOKENS
        ]


def attend(offsets, q_all, win_k, win_v, kv, vv, ms, mv, group, scale):
    kv_local, nbd = ms.shape[0], ms.shape[1]
    slash_rows = ms.shape[3]
    vert_rows = kv.shape[1]
    window_rows = win_k.shape[0]
    cols = group * HEAD_WIDTH
    rows = BLOCK_TOKENS * group
    steps = kv_local * nbd
    flops = steps * 4 * rows * (slash_rows + vert_rows) * HEAD_WIDTH
    cost = pl.CostEstimate(
        flops=flops,
        transcendentals=steps * rows * (slash_rows + vert_rows),
        bytes_accessed=2 * (2 * q_all.size + win_k.size + win_v.size + kv.size + vv.size),
    )
    kernel = lambda *refs: attend_kernel(*refs, group=group, scale=scale, nbd=nbd)
    grid_spec = pltpu.PrefetchScalarGridSpec(
        num_scalar_prefetch=1,
        grid=(kv_local, nbd),
        in_specs=[
            pl.BlockSpec((BLOCK_TOKENS, cols), lambda g, i, off: (i, g)),
            pl.BlockSpec((window_rows, HEAD_WIDTH), lambda g, i, off: (0, g)),
            pl.BlockSpec((window_rows, HEAD_WIDTH), lambda g, i, off: (0, g)),
            pl.BlockSpec((1, vert_rows, HEAD_WIDTH), lambda g, i, off: (g, 0, 0)),
            pl.BlockSpec((1, vert_rows, HEAD_WIDTH), lambda g, i, off: (g, 0, 0)),
            pl.BlockSpec((1, 1, 1, slash_rows), lambda g, i, off: (g, i, 0, 0)),
            pl.BlockSpec((1, 1, 1, vert_rows), lambda g, i, off: (g, i, 0, 0)),
        ],
        out_specs=pl.BlockSpec((BLOCK_TOKENS, cols), lambda g, i, off: (i, g)),
    )
    return pl.pallas_call(
        kernel,
        grid_spec=grid_spec,
        out_shape=jax.ShapeDtypeStruct(q_all.shape, q_all.dtype),
        cost_estimate=cost,
        interpret=INTERPRET,
    )(offsets, q_all, win_k, win_v, kv, vv, ms, mv)


def side_inputs(prev_k, prev_v, k_all, v_all, diagonal_offsets, local_vert, seq_index, nbd):
    kv_local, width = diagonal_offsets.shape
    window_k = jnp.concatenate([prev_k, k_all], 0)
    window_v = jnp.concatenate([prev_v, v_all], 0)
    qblocks = seq_index * nbd + jnp.arange(nbd, dtype=jnp.int32)
    slash_ok, vert_ok = [], []
    for group_member in range(kv_local):
        offset = diagonal_offsets[group_member]
        block_ok = qblocks[:, None] - offset[None, :] >= 0
        block_ok = jnp.concatenate(
            [block_ok, jnp.zeros((nbd, SLASH_SLOTS - width), jnp.bool_)], 1
        )
        slash_ok.append(jnp.repeat(block_ok, BLOCK_TOKENS, axis=1))
        dist = qblocks[:, None] - local_vert[group_member][None, :]
        hit = jnp.any(dist[:, :, None] == offset[None, None, :], axis=2)
        ok = (dist > 0) & jnp.logical_not(hit)
        vert_ok.append(jnp.repeat(ok, BLOCK_TOKENS, axis=1))
    ms = jnp.stack(slash_ok, 0).astype(jnp.int32)[:, :, None, :]
    mv = jnp.stack(vert_ok, 0).astype(jnp.int32)[:, :, None, :]
    return window_k, window_v, ms, mv


def local(queries, keys, values, slash, vertical):
    softmax_scale = HEAD_WIDTH ** (-0.5)
    core_index = lax.axis_index("core")
    seq_index = lax.axis_index("chip") * lax.axis_size("core") + core_index
    head_index = lax.axis_index("head")
    heads = lax.axis_size("head")
    tokens = keys.shape[0]
    joined = jnp.concatenate(
        [keys.reshape(tokens, heads, -1), values.reshape(tokens, heads, -1)], 2
    )
    joined = lax.all_to_all(joined, "head", split_axis=1, concat_axis=0, tiled=True)
    k_cols = keys.shape[1] // heads
    k_all = joined[:, 0, :k_cols]
    v_all = joined[:, 0, k_cols:]
    rows = k_all.shape[0]
    nbd = rows // BLOCK_TOKENS
    kv_local = k_all.shape[1] // HEAD_WIDTH
    query_group = queries.shape[1] // heads // HEAD_WIDTH // kv_local
    width = EXTRA_DIAGONALS + 1
    prev_k, prev_v = shifted((k_all, v_all), ("chip", "core"), 1)
    own_k = k_all.reshape(nbd, BLOCK_TOKENS, kv_local, HEAD_WIDTH)
    own_v = v_all.reshape(nbd, BLOCK_TOKENS, kv_local, HEAD_WIDTH)
    first_head = head_index * kv_local
    local_slash = lax.dynamic_slice_in_dim(slash, first_head, kv_local, 0) + 1
    diagonal_offsets = jnp.concatenate([jnp.zeros((kv_local, 1), jnp.int32), local_slash], 1)
    local_vert = lax.dynamic_slice_in_dim(vertical, first_head, kv_local, 0)
    owner = local_vert // nbd
    inner = local_vert % nbd
    listed = local_vert.shape[1]
    earlier = jnp.arange(listed)[None, :] < jnp.arange(listed)[:, None]
    same_owner = owner[:, :, None] == owner[:, None, :]
    rank = jnp.sum(same_owner & earlier[None], axis=2)
    slots = 2
    mine = (owner == seq_index)[:, None, :] & (rank[:, None, :] == jnp.arange(slots)[None, :, None])
    pick = jnp.sum(jnp.where(mine, inner[:, None, :], 0), axis=2)
    pieces, queries = lax.optimization_barrier((pick, queries))
    chips = lax.axis_size("chip")
    cores = lax.axis_size("core")
    side = int(round(chips ** 0.5))
    chip_index = lax.axis_index("chip")
    swap = [(c, cores - 1 - c) for c in range(cores)]
    heads_col = jnp.arange(kv_local)[:, None]
    mine = jnp.where(core_index == 0, own_k, own_v)[pieces, :, heads_col]
    sent = jnp.where(core_index == 0, own_v, own_k)[pieces, :, heads_col]
    stage = jnp.stack([mine, lax.ppermute(sent, "core", swap)], 0)
    q_all = lax.all_to_all(queries, "head", split_axis=1, concat_axis=0, tiled=True)
    for stride in (1, side):
        moved = [stage]
        for step in range(1, side):
            pairs = []
            for chip in range(chips):
                row, col = chip // side, chip % side
                if stride == 1:
                    pairs.append((chip, row * side + (col + step) % side))
                else:
                    pairs.append((chip, ((row + step) % side) * side + col))
            moved.append(lax.ppermute(stage, "chip", pairs))
        stage = jnp.stack(moved, 0)
        if stride == 1:
            stage, q_all, prev_k, prev_v, diagonal_offsets, local_vert = lax.optimization_barrier(
                (stage, q_all, prev_k, prev_v, diagonal_offsets, local_vert)
            )
            window_k, window_v, ms, mv = side_inputs(
                prev_k, prev_v, k_all, v_all, diagonal_offsets, local_vert, seq_index, nbd
            )
        else:
            stage, window_k, window_v, ms, mv = lax.optimization_barrier(
                (stage, window_k, window_v, ms, mv)
            )
    owner_chip = owner // cores
    owner_core = owner % cores
    dy = (chip_index // side - owner_chip // side) % side
    dx = (chip_index % side - owner_chip % side) % side
    heads_idx = jnp.arange(kv_local)[:, None]
    part = stage[dy, dx, (owner_core + core_index) % cores, heads_idx, rank]
    part = part.reshape(kv_local, listed * BLOCK_TOKENS, HEAD_WIDTH)
    other = lax.ppermute(part, "core", swap)
    vert_keys = jnp.where(core_index == 0, part, other)
    vert_vals = jnp.where(core_index == 0, other, part)
    return attend(
        diagonal_offsets, q_all, window_k, window_v, vert_keys, vert_vals, ms, mv,
        query_group, softmax_scale,
    )


def solution(mesh):
    cores = 2
    devices = mesh.devices.reshape(mesh.shape["seq"] // cores, cores, mesh.shape["head"])
    split = Mesh(devices, ("chip", "core", "head"))
    return jax.shard_map(
        local,
        mesh=split,
        in_specs=(
            P(("chip", "core", "head"), None),
            P(("chip", "core", "head"), None),
            P(("chip", "core", "head"), None),
            P(),
            P(),
        ),
        out_specs=P(("chip", "core"), "head"),
        check_vma=False,
    )
```

```python
import jax
import jax.numpy as jnp
from jax import lax
from jax.experimental import pallas as pl
from jax.experimental.pallas import tpu as pltpu
from jax.sharding import Mesh, PartitionSpec as P

HEAD_WIDTH = 128
BLOCK_TOKENS = 64
EXTRA_DIAGONALS = 4
SLASH_SLOTS = 6
INTERPRET = False


def shifted(value, axis, by):
    size = lax.axis_size(axis)
    pairs = [(i, i + by) for i in range(size) if 0 <= i + by < size]
    return lax.ppermute(value, axis, pairs)


def attend_kernel(
    off_ref, q_ref, wk_ref, wv_ref, kv_ref, vv_ref, ms_ref, mv_ref, o_ref, *, group, scale, nbd
):
    g = pl.program_id(0)
    i = pl.program_id(1)
    rows = BLOCK_TOKENS * group
    picked_k, picked_v = [], []
    for j in range(EXTRA_DIAGONALS + 1):
        block = jnp.clip(nbd + i - off_ref[g, j], 0, 2 * nbd - 1)
        start = pl.multiple_of(block * BLOCK_TOKENS, BLOCK_TOKENS)
        picked_k.append(wk_ref[pl.ds(start, BLOCK_TOKENS), :])
        picked_v.append(wv_ref[pl.ds(start, BLOCK_TOKENS), :])
    pad = jnp.zeros(
        ((SLASH_SLOTS - EXTRA_DIAGONALS - 1) * BLOCK_TOKENS, HEAD_WIDTH), wk_ref.dtype
    )
    ks = jnp.concatenate(picked_k + [pad], 0)
    vs = jnp.concatenate(picked_v + [pad], 0)
    q = q_ref[...]
    q_stack = jnp.concatenate(
        [q[:, h * HEAD_WIDTH : (h + 1) * HEAD_WIDTH] for h in range(group)], axis=0
    )
    nt = (((1,), (1,)), ((), ()))
    s_slash = lax.dot_general(q_stack, ks, nt, preferred_element_type=jnp.float32) * scale
    s_vert = lax.dot_general(q_stack, kv_ref[0], nt, preferred_element_type=jnp.float32) * scale
    width = s_slash.shape[1]
    row = jnp.bitwise_and(lax.broadcasted_iota(jnp.int32, (rows, width), 0), BLOCK_TOKENS - 1)
    col = lax.broadcasted_iota(jnp.int32, (rows, width), 1)
    ok_slash = (ms_ref[0, 0] > 0) & ((col >= BLOCK_TOKENS) | (col <= row))
    s_slash = jnp.where(ok_slash, s_slash, -jnp.inf)
    s_vert = jnp.where(mv_ref[0, 0] > 0, s_vert, -jnp.inf)
    top = jnp.maximum(
        jnp.max(s_slash, axis=1, keepdims=True), jnp.max(s_vert, axis=1, keepdims=True)
    )
    w_slash = jnp.exp(s_slash - top)
    w_vert = jnp.exp(s_vert - top)
    total = jnp.sum(w_slash, axis=1, keepdims=True) + jnp.sum(w_vert, axis=1, keepdims=True)
    acc = jnp.dot(w_slash.astype(jnp.bfloat16), vs, preferred_element_type=jnp.float32)
    acc = acc + jnp.dot(
        w_vert.astype(jnp.bfloat16), vv_ref[0], preferred_element_type=jnp.float32
    )
    res = (acc / total).astype(o_ref.dtype)
    for h in range(group):
        o_ref[:, h * HEAD_WIDTH : (h + 1) * HEAD_WIDTH] = res[
            h * BLOCK_TOKENS : (h + 1) * BLOCK_TOKENS
        ]


def attend(offsets, q_all, win_k, win_v, kv, vv, ms, mv, group, scale):
    kv_local, nbd = ms.shape[0], ms.shape[1]
    slash_rows = ms.shape[3]
    vert_rows = kv.shape[1]
    window_rows = win_k.shape[0]
    cols = group * HEAD_WIDTH
    rows = BLOCK_TOKENS * group
    steps = kv_local * nbd
    flops = steps * 4 * rows * (slash_rows + vert_rows) * HEAD_WIDTH
    cost = pl.CostEstimate(
        flops=flops,
        transcendentals=steps * rows * (slash_rows + vert_rows),
        bytes_accessed=2 * (2 * q_all.size + win_k.size + win_v.size + kv.size + vv.size),
    )
    kernel = lambda *refs: attend_kernel(*refs, group=group, scale=scale, nbd=nbd)
    grid_spec = pltpu.PrefetchScalarGridSpec(
        num_scalar_prefetch=1,
        grid=(kv_local, nbd),
        in_specs=[
            pl.BlockSpec((BLOCK_TOKENS, cols), lambda g, i, off: (i, g)),
            pl.BlockSpec((window_rows, HEAD_WIDTH), lambda g, i, off: (0, g)),
            pl.BlockSpec((window_rows, HEAD_WIDTH), lambda g, i, off: (0, g)),
            pl.BlockSpec((1, vert_rows, HEAD_WIDTH), lambda g, i, off: (g, 0, 0)),
            pl.BlockSpec((1, vert_rows, HEAD_WIDTH), lambda g, i, off: (g, 0, 0)),
            pl.BlockSpec((1, 1, 1, slash_rows), lambda g, i, off: (g, i, 0, 0)),
            pl.BlockSpec((1, 1, 1, vert_rows), lambda g, i, off: (g, i, 0, 0)),
        ],
        out_specs=pl.BlockSpec((BLOCK_TOKENS, cols), lambda g, i, off: (i, g)),
    )
    return pl.pallas_call(
        kernel,
        grid_spec=grid_spec,
        out_shape=jax.ShapeDtypeStruct(q_all.shape, q_all.dtype),
        cost_estimate=cost,
        interpret=INTERPRET,
    )(offsets, q_all, win_k, win_v, kv, vv, ms, mv)


def side_inputs(prev_k, prev_v, k_all, v_all, diagonal_offsets, local_vert, seq_index, nbd):
    kv_local, width = diagonal_offsets.shape
    window_k = jnp.concatenate([prev_k, k_all], 0)
    window_v = jnp.concatenate([prev_v, v_all], 0)
    qblocks = seq_index * nbd + jnp.arange(nbd, dtype=jnp.int32)
    slash_ok, vert_ok = [], []
    for group_member in range(kv_local):
        offset = diagonal_offsets[group_member]
        block_ok = qblocks[:, None] - offset[None, :] >= 0
        block_ok = jnp.concatenate(
            [block_ok, jnp.zeros((nbd, SLASH_SLOTS - width), jnp.bool_)], 1
        )
        slash_ok.append(jnp.repeat(block_ok, BLOCK_TOKENS, axis=1))
        dist = qblocks[:, None] - local_vert[group_member][None, :]
        hit = jnp.any(dist[:, :, None] == offset[None, None, :], axis=2)
        ok = (dist > 0) & jnp.logical_not(hit)
        vert_ok.append(jnp.repeat(ok, BLOCK_TOKENS, axis=1))
    ms = jnp.stack(slash_ok, 0).astype(jnp.int32)[:, :, None, :]
    mv = jnp.stack(vert_ok, 0).astype(jnp.int32)[:, :, None, :]
    return window_k, window_v, ms, mv


def local(queries, keys, values, slash, vertical):
    softmax_scale = HEAD_WIDTH ** (-0.5)
    core_index = lax.axis_index("core")
    seq_index = lax.axis_index("chip") * lax.axis_size("core") + core_index
    head_index = lax.axis_index("head")
    heads = lax.axis_size("head")
    tokens = keys.shape[0]
    joined = jnp.concatenate(
        [keys.reshape(tokens, heads, -1), values.reshape(tokens, heads, -1)], 2
    )
    joined = lax.all_to_all(joined, "head", split_axis=1, concat_axis=0, tiled=True)
    k_cols = keys.shape[1] // heads
    k_all = joined[:, 0, :k_cols]
    v_all = joined[:, 0, k_cols:]
    rows = k_all.shape[0]
    nbd = rows // BLOCK_TOKENS
    kv_local = k_all.shape[1] // HEAD_WIDTH
    query_group = queries.shape[1] // heads // HEAD_WIDTH // kv_local
    width = EXTRA_DIAGONALS + 1
    prev_k, prev_v = shifted((k_all, v_all), ("chip", "core"), 1)
    own_k = k_all.reshape(nbd, BLOCK_TOKENS, kv_local, HEAD_WIDTH)
    own_v = v_all.reshape(nbd, BLOCK_TOKENS, kv_local, HEAD_WIDTH)
    first_head = head_index * kv_local
    local_slash = lax.dynamic_slice_in_dim(slash, first_head, kv_local, 0) + 1
    diagonal_offsets = jnp.concatenate([jnp.zeros((kv_local, 1), jnp.int32), local_slash], 1)
    local_vert = lax.dynamic_slice_in_dim(vertical, first_head, kv_local, 0)
    owner = local_vert // nbd
    inner = local_vert % nbd
    listed = local_vert.shape[1]
    earlier = jnp.arange(listed)[None, :] < jnp.arange(listed)[:, None]
    same_owner = owner[:, :, None] == owner[:, None, :]
    rank = jnp.sum(same_owner & earlier[None], axis=2)
    slots = 2
    mine = (owner == seq_index)[:, None, :] & (rank[:, None, :] == jnp.arange(slots)[None, :, None])
    pick = jnp.sum(jnp.where(mine, inner[:, None, :], 0), axis=2)
    pieces, queries = lax.optimization_barrier((pick, queries))
    chips = lax.axis_size("chip")
    cores = lax.axis_size("core")
    side = int(round(chips ** 0.5))
    chip_index = lax.axis_index("chip")
    swap = [(c, cores - 1 - c) for c in range(cores)]
    heads_col = jnp.arange(kv_local)[:, None]
    mine = jnp.where(core_index == 0, own_k, own_v)[pieces, :, heads_col]
    sent = jnp.where(core_index == 0, own_v, own_k)[pieces, :, heads_col]
    stage = jnp.stack([mine, lax.ppermute(sent, "core", swap)], 0)
    q_all = lax.all_to_all(queries, "head", split_axis=1, concat_axis=0, tiled=True)
    def shift(value, stride, step):
        pairs = []
        for chip in range(chips):
            row, col = chip // side, chip % side
            if stride == 1:
                pairs.append((chip, row * side + (col + step) % side))
            else:
                pairs.append((chip, ((row + step) % side) * side + col))
        return lax.ppermute(value, "chip", pairs)

    def ring(value, stride):
        return jnp.stack([value] + [shift(value, stride, s) for s in range(1, side)], 0)

    across = ring(lax.index_in_dim(stage, 0, 1), 1)
    down = ring(lax.index_in_dim(stage, 1, 1), side)
    across, down, q_all, prev_k, prev_v, diagonal_offsets, local_vert = lax.optimization_barrier(
        (across, down, q_all, prev_k, prev_v, diagonal_offsets, local_vert)
    )
    window_k, window_v, ms, mv = side_inputs(
        prev_k, prev_v, k_all, v_all, diagonal_offsets, local_vert, seq_index, nbd
    )
    across = ring(across, side)
    down = ring(down, 1)
    across, down, window_k, window_v, ms, mv = lax.optimization_barrier(
        (across, down, window_k, window_v, ms, mv)
    )
    owner_chip = owner // cores
    owner_core = owner % cores
    dy = (chip_index // side - owner_chip // side) % side
    dx = (chip_index % side - owner_chip % side) % side
    heads_idx = jnp.arange(kv_local)[:, None]
    dc = (owner_core + core_index) % cores
    part = jnp.stack(
        [
            across[dy[0], dx[0], dc[0], 0, rank[0]],
            down[dx[1], dy[1], dc[1], 0, rank[1]],
        ],
        0,
    )
    part = part.reshape(kv_local, listed * BLOCK_TOKENS, HEAD_WIDTH)
    other = lax.ppermute(part, "core", swap)
    vert_keys = jnp.where(core_index == 0, part, other)
    vert_vals = jnp.where(core_index == 0, other, part)
    return attend(
        diagonal_offsets, q_all, window_k, window_v, vert_keys, vert_vals, ms, mv,
        query_group, softmax_scale,
    )


def solution(mesh):
    cores = 2
    devices = mesh.devices.reshape(mesh.shape["seq"] // cores, cores, mesh.shape["head"])
    split = Mesh(devices, ("chip", "core", "head"))
    return jax.shard_map(
        local,
        mesh=split,
        in_specs=(
            P(("chip", "core", "head"), None),
            P(("chip", "core", "head"), None),
            P(("chip", "core", "head"), None),
            P(),
            P(),
        ),
        out_specs=P(("chip", "core"), "head"),
        check_vma=False,
    )
```

```python
import jax
import jax.numpy as jnp
from jax import lax
from jax.experimental import pallas as pl
from jax.experimental.pallas import tpu as pltpu
from jax.sharding import Mesh, PartitionSpec as P

HEAD_WIDTH = 128
BLOCK_TOKENS = 64
EXTRA_DIAGONALS = 4
SLASH_SLOTS = 6
INTERPRET = False


def shifted(value, axis, by):
    size = lax.axis_size(axis)
    pairs = [(i, i + by) for i in range(size) if 0 <= i + by < size]
    return lax.ppermute(value, axis, pairs)


def attend_kernel(
    off_ref, q_ref, wk_ref, wv_ref, kv_ref, vv_ref, ms_ref, mv_ref, o_ref, *, group, scale, nbd
):
    g = pl.program_id(0)
    i = pl.program_id(1)
    rows = BLOCK_TOKENS * group
    picked_k, picked_v = [], []
    for j in range(EXTRA_DIAGONALS + 1):
        block = jnp.clip(nbd + i - off_ref[g, j], 0, 2 * nbd - 1)
        start = pl.multiple_of(block * BLOCK_TOKENS, BLOCK_TOKENS)
        picked_k.append(wk_ref[pl.ds(start, BLOCK_TOKENS), :])
        picked_v.append(wv_ref[pl.ds(start, BLOCK_TOKENS), :])
    pad = jnp.zeros(
        ((SLASH_SLOTS - EXTRA_DIAGONALS - 1) * BLOCK_TOKENS, HEAD_WIDTH), wk_ref.dtype
    )
    ks = jnp.concatenate(picked_k + [pad], 0)
    vs = jnp.concatenate(picked_v + [pad], 0)
    q = q_ref[...]
    q_stack = jnp.concatenate(
        [q[:, h * HEAD_WIDTH : (h + 1) * HEAD_WIDTH] for h in range(group)], axis=0
    )
    nt = (((1,), (1,)), ((), ()))
    s_slash = lax.dot_general(q_stack, ks, nt, preferred_element_type=jnp.float32) * scale
    s_vert = lax.dot_general(q_stack, kv_ref[0], nt, preferred_element_type=jnp.float32) * scale
    width = s_slash.shape[1]
    row = jnp.bitwise_and(lax.broadcasted_iota(jnp.int32, (rows, width), 0), BLOCK_TOKENS - 1)
    col = lax.broadcasted_iota(jnp.int32, (rows, width), 1)
    ok_slash = (ms_ref[0, 0] > 0) & ((col >= BLOCK_TOKENS) | (col <= row))
    s_slash = jnp.where(ok_slash, s_slash, -jnp.inf)
    s_vert = jnp.where(mv_ref[0, 0] > 0, s_vert, -jnp.inf)
    top = jnp.maximum(
        jnp.max(s_slash, axis=1, keepdims=True), jnp.max(s_vert, axis=1, keepdims=True)
    )
    w_slash = jnp.exp(s_slash - top)
    w_vert = jnp.exp(s_vert - top)
    total = jnp.sum(w_slash, axis=1, keepdims=True) + jnp.sum(w_vert, axis=1, keepdims=True)
    acc = jnp.dot(w_slash.astype(jnp.bfloat16), vs, preferred_element_type=jnp.float32)
    acc = acc + jnp.dot(
        w_vert.astype(jnp.bfloat16), vv_ref[0], preferred_element_type=jnp.float32
    )
    res = (acc / total).astype(o_ref.dtype)
    for h in range(group):
        o_ref[:, h * HEAD_WIDTH : (h + 1) * HEAD_WIDTH] = res[
            h * BLOCK_TOKENS : (h + 1) * BLOCK_TOKENS
        ]


def attend(offsets, q_all, win_k, win_v, kv, vv, ms, mv, group, scale):
    kv_local, nbd = ms.shape[0], ms.shape[1]
    slash_rows = ms.shape[3]
    vert_rows = kv.shape[1]
    window_rows = win_k.shape[0]
    cols = group * HEAD_WIDTH
    rows = BLOCK_TOKENS * group
    steps = kv_local * nbd
    flops = steps * 4 * rows * (slash_rows + vert_rows) * HEAD_WIDTH
    cost = pl.CostEstimate(
        flops=flops,
        transcendentals=steps * rows * (slash_rows + vert_rows),
        bytes_accessed=2 * (2 * q_all.size + win_k.size + win_v.size + kv.size + vv.size),
    )
    kernel = lambda *refs: attend_kernel(*refs, group=group, scale=scale, nbd=nbd)
    grid_spec = pltpu.PrefetchScalarGridSpec(
        num_scalar_prefetch=1,
        grid=(kv_local, nbd),
        in_specs=[
            pl.BlockSpec((BLOCK_TOKENS, cols), lambda g, i, off: (i, g)),
            pl.BlockSpec((window_rows, HEAD_WIDTH), lambda g, i, off: (0, g)),
            pl.BlockSpec((window_rows, HEAD_WIDTH), lambda g, i, off: (0, g)),
            pl.BlockSpec((1, vert_rows, HEAD_WIDTH), lambda g, i, off: (g, 0, 0)),
            pl.BlockSpec((1, vert_rows, HEAD_WIDTH), lambda g, i, off: (g, 0, 0)),
            pl.BlockSpec((1, 1, 1, slash_rows), lambda g, i, off: (g, i, 0, 0)),
            pl.BlockSpec((1, 1, 1, vert_rows), lambda g, i, off: (g, i, 0, 0)),
        ],
        out_specs=pl.BlockSpec((BLOCK_TOKENS, cols), lambda g, i, off: (i, g)),
    )
    return pl.pallas_call(
        kernel,
        grid_spec=grid_spec,
        out_shape=jax.ShapeDtypeStruct(q_all.shape, q_all.dtype),
        cost_estimate=cost,
        interpret=INTERPRET,
    )(offsets, q_all, win_k, win_v, kv, vv, ms, mv)


def side_inputs(prev_k, prev_v, k_all, v_all, diagonal_offsets, local_vert, seq_index, nbd):
    kv_local, width = diagonal_offsets.shape
    window_k = jnp.concatenate([prev_k, k_all], 0)
    window_v = jnp.concatenate([prev_v, v_all], 0)
    qblocks = seq_index * nbd + jnp.arange(nbd, dtype=jnp.int32)
    slash_ok, vert_ok = [], []
    for group_member in range(kv_local):
        offset = diagonal_offsets[group_member]
        block_ok = qblocks[:, None] - offset[None, :] >= 0
        block_ok = jnp.concatenate(
            [block_ok, jnp.zeros((nbd, SLASH_SLOTS - width), jnp.bool_)], 1
        )
        slash_ok.append(jnp.repeat(block_ok, BLOCK_TOKENS, axis=1))
        dist = qblocks[:, None] - local_vert[group_member][None, :]
        hit = jnp.any(dist[:, :, None] == offset[None, None, :], axis=2)
        ok = (dist > 0) & jnp.logical_not(hit)
        vert_ok.append(jnp.repeat(ok, BLOCK_TOKENS, axis=1))
    ms = jnp.stack(slash_ok, 0).astype(jnp.int32)[:, :, None, :]
    mv = jnp.stack(vert_ok, 0).astype(jnp.int32)[:, :, None, :]
    return window_k, window_v, ms, mv


def local(queries, keys, values, slash, vertical):
    softmax_scale = HEAD_WIDTH ** (-0.5)
    core_index = lax.axis_index("core")
    seq_index = lax.axis_index("chip") * lax.axis_size("core") + core_index
    head_index = lax.axis_index("head")
    heads = lax.axis_size("head")
    tokens = keys.shape[0]
    joined = jnp.concatenate(
        [keys.reshape(tokens, heads, -1), values.reshape(tokens, heads, -1)], 2
    )
    joined = lax.all_to_all(joined, "head", split_axis=1, concat_axis=0, tiled=True)
    k_cols = keys.shape[1] // heads
    k_all = joined[:, 0, :k_cols]
    v_all = joined[:, 0, k_cols:]
    rows = k_all.shape[0]
    nbd = rows // BLOCK_TOKENS
    kv_local = k_all.shape[1] // HEAD_WIDTH
    query_group = queries.shape[1] // heads // HEAD_WIDTH // kv_local
    width = EXTRA_DIAGONALS + 1
    prev_k, prev_v = shifted((k_all, v_all), ("chip", "core"), 1)
    own_k = k_all.reshape(nbd, BLOCK_TOKENS, kv_local, HEAD_WIDTH)
    own_v = v_all.reshape(nbd, BLOCK_TOKENS, kv_local, HEAD_WIDTH)
    first_head = head_index * kv_local
    local_slash = lax.dynamic_slice_in_dim(slash, first_head, kv_local, 0) + 1
    diagonal_offsets = jnp.concatenate([jnp.zeros((kv_local, 1), jnp.int32), local_slash], 1)
    local_vert = lax.dynamic_slice_in_dim(vertical, first_head, kv_local, 0)
    owner = local_vert // nbd
    inner = local_vert % nbd
    listed = local_vert.shape[1]
    earlier = jnp.arange(listed)[None, :] < jnp.arange(listed)[:, None]
    same_owner = owner[:, :, None] == owner[:, None, :]
    rank = jnp.sum(same_owner & earlier[None], axis=2)
    slots = 2
    mine = (owner == seq_index)[:, None, :] & (rank[:, None, :] == jnp.arange(slots)[None, :, None])
    pick = jnp.sum(jnp.where(mine, inner[:, None, :], 0), axis=2)
    pieces, queries = lax.optimization_barrier((pick, queries))
    chips = lax.axis_size("chip")
    cores = lax.axis_size("core")
    side = int(round(chips ** 0.5))
    chip_index = lax.axis_index("chip")
    swap = [(c, cores - 1 - c) for c in range(cores)]
    heads_col = jnp.arange(kv_local)[:, None]
    mine = jnp.where(core_index == 0, own_k, own_v)[pieces, :, heads_col]
    sent = jnp.where(core_index == 0, own_v, own_k)[pieces, :, heads_col]
    stage = jnp.stack([mine, lax.ppermute(sent, "core", swap)], 0)
    def shift(value, stride, step):
        pairs = []
        for chip in range(chips):
            row, col = chip // side, chip % side
            if stride == 1:
                pairs.append((chip, row * side + (col + step) % side))
            else:
                pairs.append((chip, ((row + step) % side) * side + col))
        return lax.ppermute(value, "chip", pairs)

    def ring(value, stride):
        return jnp.stack([value] + [shift(value, stride, s) for s in range(1, side)], 0)

    across = ring(lax.index_in_dim(stage, 0, 1), 1)
    down = ring(lax.index_in_dim(stage, 1, 1), side)
    across, down, queries, prev_k, prev_v, diagonal_offsets, local_vert = lax.optimization_barrier(
        (across, down, queries, prev_k, prev_v, diagonal_offsets, local_vert)
    )
    q_all = lax.all_to_all(queries, "head", split_axis=1, concat_axis=0, tiled=True)
    window_k, window_v, ms, mv = side_inputs(
        prev_k, prev_v, k_all, v_all, diagonal_offsets, local_vert, seq_index, nbd
    )
    across = ring(across, side)
    down = ring(down, 1)
    across, down, window_k, window_v, ms, mv, q_all = lax.optimization_barrier(
        (across, down, window_k, window_v, ms, mv, q_all)
    )
    owner_chip = owner // cores
    owner_core = owner % cores
    dy = (chip_index // side - owner_chip // side) % side
    dx = (chip_index % side - owner_chip % side) % side
    heads_idx = jnp.arange(kv_local)[:, None]
    dc = (owner_core + core_index) % cores
    part = jnp.stack(
        [
            across[dy[0], dx[0], dc[0], 0, rank[0]],
            down[dx[1], dy[1], dc[1], 0, rank[1]],
        ],
        0,
    )
    part = part.reshape(kv_local, listed * BLOCK_TOKENS, HEAD_WIDTH)
    other = lax.ppermute(part, "core", swap)
    vert_keys = jnp.where(core_index == 0, part, other)
    vert_vals = jnp.where(core_index == 0, other, part)
    return attend(
        diagonal_offsets, q_all, window_k, window_v, vert_keys, vert_vals, ms, mv,
        query_group, softmax_scale,
    )


def solution(mesh):
    cores = 2
    devices = mesh.devices.reshape(mesh.shape["seq"] // cores, cores, mesh.shape["head"])
    split = Mesh(devices, ("chip", "core", "head"))
    return jax.shard_map(
        local,
        mesh=split,
        in_specs=(
            P(("chip", "core", "head"), None),
            P(("chip", "core", "head"), None),
            P(("chip", "core", "head"), None),
            P(),
            P(),
        ),
        out_specs=P(("chip", "core"), "head"),
        check_vma=False,
    )
```

```python
import jax
import jax.numpy as jnp
from jax import lax
from jax.experimental import pallas as pl
from jax.experimental.pallas import tpu as pltpu
from jax.sharding import Mesh, PartitionSpec as P

HEAD_WIDTH = 128
BLOCK_TOKENS = 64
EXTRA_DIAGONALS = 4
SLASH_SLOTS = 6
LOG2_E = 1.4426950408889634
INTERPRET = False


def shifted(value, axis, by):
    size = lax.axis_size(axis)
    pairs = [(i, i + by) for i in range(size) if 0 <= i + by < size]
    return lax.ppermute(value, axis, pairs)


def attend_kernel(
    off_ref, q_ref, wk_ref, wv_ref, kv_ref, vv_ref, ms_ref, mv_ref, o_ref, *, group, scale, nbd
):
    g = pl.program_id(0)
    i = pl.program_id(1)
    rows = BLOCK_TOKENS * group
    picked_k, picked_v = [], []
    for j in range(EXTRA_DIAGONALS + 1):
        block = jnp.clip(nbd + i - off_ref[g, j], 0, 2 * nbd - 1)
        start = pl.multiple_of(block * BLOCK_TOKENS, BLOCK_TOKENS)
        picked_k.append(wk_ref[pl.ds(start, BLOCK_TOKENS), :])
        picked_v.append(wv_ref[pl.ds(start, BLOCK_TOKENS), :])
    pad = jnp.zeros(
        ((SLASH_SLOTS - EXTRA_DIAGONALS - 1) * BLOCK_TOKENS, HEAD_WIDTH), wk_ref.dtype
    )
    ks = jnp.concatenate(picked_k + [pad], 0)
    vs = jnp.concatenate(picked_v + [pad], 0)
    q = q_ref[...]
    q_stack = jnp.concatenate(
        [q[:, h * HEAD_WIDTH : (h + 1) * HEAD_WIDTH] for h in range(group)], axis=0
    )
    nt = (((1,), (1,)), ((), ()))
    s_slash = lax.dot_general(q_stack, ks, nt, preferred_element_type=jnp.float32)
    s_vert = lax.dot_general(q_stack, kv_ref[0], nt, preferred_element_type=jnp.float32)
    width = s_slash.shape[1]
    row = jnp.bitwise_and(lax.broadcasted_iota(jnp.int32, (rows, width), 0), BLOCK_TOKENS - 1)
    col = lax.broadcasted_iota(jnp.int32, (rows, width), 1)
    ok_slash = (ms_ref[0, 0] > 0) & ((col >= BLOCK_TOKENS) | (col <= row))
    s_slash = jnp.where(ok_slash, s_slash, -jnp.inf)
    s_vert = jnp.where(mv_ref[0, 0] > 0, s_vert, -jnp.inf)
    top = jnp.maximum(
        jnp.max(s_slash, axis=1, keepdims=True), jnp.max(s_vert, axis=1, keepdims=True)
    )
    rate = scale * LOG2_E
    w_slash = jnp.exp2((s_slash - top) * rate)
    w_vert = jnp.exp2((s_vert - top) * rate)
    total = jnp.sum(w_slash, axis=1, keepdims=True) + jnp.sum(w_vert, axis=1, keepdims=True)
    acc = jnp.dot(w_slash.astype(jnp.bfloat16), vs, preferred_element_type=jnp.float32)
    acc = acc + jnp.dot(
        w_vert.astype(jnp.bfloat16), vv_ref[0], preferred_element_type=jnp.float32
    )
    res = (acc / total).astype(o_ref.dtype)
    for h in range(group):
        o_ref[:, h * HEAD_WIDTH : (h + 1) * HEAD_WIDTH] = res[
            h * BLOCK_TOKENS : (h + 1) * BLOCK_TOKENS
        ]


def attend(offsets, q_all, win_k, win_v, kv, vv, ms, mv, group, scale):
    kv_local, nbd = ms.shape[0], ms.shape[1]
    slash_rows = ms.shape[3]
    vert_rows = kv.shape[1]
    window_rows = win_k.shape[0]
    cols = group * HEAD_WIDTH
    rows = BLOCK_TOKENS * group
    steps = kv_local * nbd
    flops = steps * 4 * rows * (slash_rows + vert_rows) * HEAD_WIDTH
    cost = pl.CostEstimate(
        flops=flops,
        transcendentals=steps * rows * (slash_rows + vert_rows),
        bytes_accessed=2 * (2 * q_all.size + win_k.size + win_v.size + kv.size + vv.size),
    )
    kernel = lambda *refs: attend_kernel(*refs, group=group, scale=scale, nbd=nbd)
    grid_spec = pltpu.PrefetchScalarGridSpec(
        num_scalar_prefetch=1,
        grid=(kv_local, nbd),
        in_specs=[
            pl.BlockSpec((BLOCK_TOKENS, cols), lambda g, i, off: (i, g)),
            pl.BlockSpec((window_rows, HEAD_WIDTH), lambda g, i, off: (0, g)),
            pl.BlockSpec((window_rows, HEAD_WIDTH), lambda g, i, off: (0, g)),
            pl.BlockSpec((1, vert_rows, HEAD_WIDTH), lambda g, i, off: (g, 0, 0)),
            pl.BlockSpec((1, vert_rows, HEAD_WIDTH), lambda g, i, off: (g, 0, 0)),
            pl.BlockSpec((1, 1, 1, slash_rows), lambda g, i, off: (g, i, 0, 0)),
            pl.BlockSpec((1, 1, 1, vert_rows), lambda g, i, off: (g, i, 0, 0)),
        ],
        out_specs=pl.BlockSpec((BLOCK_TOKENS, cols), lambda g, i, off: (i, g)),
    )
    return pl.pallas_call(
        kernel,
        grid_spec=grid_spec,
        out_shape=jax.ShapeDtypeStruct(q_all.shape, q_all.dtype),
        cost_estimate=cost,
        interpret=INTERPRET,
    )(offsets, q_all, win_k, win_v, kv, vv, ms, mv)


def side_inputs(prev_k, prev_v, k_all, v_all, diagonal_offsets, local_vert, seq_index, nbd):
    kv_local, width = diagonal_offsets.shape
    window_k = jnp.concatenate([prev_k, k_all], 0)
    window_v = jnp.concatenate([prev_v, v_all], 0)
    qblocks = seq_index * nbd + jnp.arange(nbd, dtype=jnp.int32)
    slash_ok, vert_ok = [], []
    for group_member in range(kv_local):
        offset = diagonal_offsets[group_member]
        block_ok = qblocks[:, None] - offset[None, :] >= 0
        block_ok = jnp.concatenate(
            [block_ok, jnp.zeros((nbd, SLASH_SLOTS - width), jnp.bool_)], 1
        )
        slash_ok.append(jnp.repeat(block_ok, BLOCK_TOKENS, axis=1))
        dist = qblocks[:, None] - local_vert[group_member][None, :]
        hit = jnp.any(dist[:, :, None] == offset[None, None, :], axis=2)
        ok = (dist > 0) & jnp.logical_not(hit)
        vert_ok.append(jnp.repeat(ok, BLOCK_TOKENS, axis=1))
    ms = jnp.stack(slash_ok, 0).astype(jnp.int32)[:, :, None, :]
    mv = jnp.stack(vert_ok, 0).astype(jnp.int32)[:, :, None, :]
    return window_k, window_v, ms, mv


def local(queries, keys, values, slash, vertical):
    softmax_scale = HEAD_WIDTH ** (-0.5)
    core_index = lax.axis_index("core")
    seq_index = lax.axis_index("chip") * lax.axis_size("core") + core_index
    head_index = lax.axis_index("head")
    heads = lax.axis_size("head")
    tokens = keys.shape[0]
    joined = jnp.concatenate(
        [keys.reshape(tokens, heads, -1), values.reshape(tokens, heads, -1)], 2
    )
    joined = lax.all_to_all(joined, "head", split_axis=1, concat_axis=0, tiled=True)
    k_cols = keys.shape[1] // heads
    k_all = joined[:, 0, :k_cols]
    v_all = joined[:, 0, k_cols:]
    rows = k_all.shape[0]
    nbd = rows // BLOCK_TOKENS
    kv_local = k_all.shape[1] // HEAD_WIDTH
    query_group = queries.shape[1] // heads // HEAD_WIDTH // kv_local
    width = EXTRA_DIAGONALS + 1
    prev_k, prev_v = shifted((k_all, v_all), ("chip", "core"), 1)
    own_k = k_all.reshape(nbd, BLOCK_TOKENS, kv_local, HEAD_WIDTH)
    own_v = v_all.reshape(nbd, BLOCK_TOKENS, kv_local, HEAD_WIDTH)
    first_head = head_index * kv_local
    local_slash = lax.dynamic_slice_in_dim(slash, first_head, kv_local, 0) + 1
    diagonal_offsets = jnp.concatenate([jnp.zeros((kv_local, 1), jnp.int32), local_slash], 1)
    local_vert = lax.dynamic_slice_in_dim(vertical, first_head, kv_local, 0)
    owner = local_vert // nbd
    inner = local_vert % nbd
    listed = local_vert.shape[1]
    earlier = jnp.arange(listed)[None, :] < jnp.arange(listed)[:, None]
    same_owner = owner[:, :, None] == owner[:, None, :]
    rank = jnp.sum(same_owner & earlier[None], axis=2)
    slots = 2
    mine = (owner == seq_index)[:, None, :] & (rank[:, None, :] == jnp.arange(slots)[None, :, None])
    pick = jnp.sum(jnp.where(mine, inner[:, None, :], 0), axis=2)
    pieces, queries = lax.optimization_barrier((pick, queries))
    chips = lax.axis_size("chip")
    cores = lax.axis_size("core")
    side = int(round(chips ** 0.5))
    chip_index = lax.axis_index("chip")
    swap = [(c, cores - 1 - c) for c in range(cores)]
    heads_col = jnp.arange(kv_local)[:, None]
    mine = jnp.where(core_index == 0, own_k, own_v)[pieces, :, heads_col]
    sent = jnp.where(core_index == 0, own_v, own_k)[pieces, :, heads_col]
    stage = jnp.stack([mine, lax.ppermute(sent, "core", swap)], 0)
    q_all = lax.all_to_all(queries, "head", split_axis=1, concat_axis=0, tiled=True)
    def shift(value, stride, step):
        pairs = []
        for chip in range(chips):
            row, col = chip // side, chip % side
            if stride == 1:
                pairs.append((chip, row * side + (col + step) % side))
            else:
                pairs.append((chip, ((row + step) % side) * side + col))
        return lax.ppermute(value, "chip", pairs)

    def ring(value, stride):
        return jnp.stack([value] + [shift(value, stride, s) for s in range(1, side)], 0)

    across = ring(lax.index_in_dim(stage, 0, 1), 1)
    down = ring(lax.index_in_dim(stage, 1, 1), side)
    across, down, q_all, prev_k, prev_v, diagonal_offsets, local_vert = lax.optimization_barrier(
        (across, down, q_all, prev_k, prev_v, diagonal_offsets, local_vert)
    )
    window_k, window_v, ms, mv = side_inputs(
        prev_k, prev_v, k_all, v_all, diagonal_offsets, local_vert, seq_index, nbd
    )
    across = ring(across, side)
    down = ring(down, 1)
    across, down, window_k, window_v, ms, mv = lax.optimization_barrier(
        (across, down, window_k, window_v, ms, mv)
    )
    owner_chip = owner // cores
    owner_core = owner % cores
    dy = (chip_index // side - owner_chip // side) % side
    dx = (chip_index % side - owner_chip % side) % side
    heads_idx = jnp.arange(kv_local)[:, None]
    dc = (owner_core + core_index) % cores
    part = jnp.stack(
        [
            across[dy[0], dx[0], dc[0], 0, rank[0]],
            down[dx[1], dy[1], dc[1], 0, rank[1]],
        ],
        0,
    )
    part = part.reshape(kv_local, listed * BLOCK_TOKENS, HEAD_WIDTH)
    other = lax.ppermute(part, "core", swap)
    vert_keys = jnp.where(core_index == 0, part, other)
    vert_vals = jnp.where(core_index == 0, other, part)
    return attend(
        diagonal_offsets, q_all, window_k, window_v, vert_keys, vert_vals, ms, mv,
        query_group, softmax_scale,
    )


def solution(mesh):
    cores = 2
    devices = mesh.devices.reshape(mesh.shape["seq"] // cores, cores, mesh.shape["head"])
    split = Mesh(devices, ("chip", "core", "head"))
    return jax.shard_map(
        local,
        mesh=split,
        in_specs=(
            P(("chip", "core", "head"), None),
            P(("chip", "core", "head"), None),
            P(("chip", "core", "head"), None),
            P(),
            P(),
        ),
        out_specs=P(("chip", "core"), "head"),
        check_vma=False,
    )
```

```python
import jax
import jax.numpy as jnp
from jax import lax
from jax.experimental import pallas as pl
from jax.experimental.pallas import tpu as pltpu
from jax.sharding import Mesh, PartitionSpec as P

HEAD_WIDTH = 128
BLOCK_TOKENS = 64
EXTRA_DIAGONALS = 4
SLASH_SLOTS = 6
LOG2_E = 1.4426950408889634
INTERPRET = False


def shifted(value, axis, by):
    size = lax.axis_size(axis)
    pairs = [(i, i + by) for i in range(size) if 0 <= i + by < size]
    return lax.ppermute(value, axis, pairs)


def attend_kernel(
    off_ref, q_ref, wk_ref, wv_ref, kv_ref, vv_ref, ms_ref, mv_ref, *rest, group, scale, nbd, head
):
    o_ref = rest[-1]
    g = head
    i = pl.program_id(1)
    rows = BLOCK_TOKENS * group
    picked_k, picked_v = [], []
    for j in range(EXTRA_DIAGONALS + 1):
        block = jnp.clip(nbd + i - off_ref[g, j], 0, 2 * nbd - 1)
        start = pl.multiple_of(block * BLOCK_TOKENS, BLOCK_TOKENS)
        picked_k.append(wk_ref[pl.ds(start, BLOCK_TOKENS), :])
        picked_v.append(wv_ref[pl.ds(start, BLOCK_TOKENS), :])
    pad = jnp.zeros(
        ((SLASH_SLOTS - EXTRA_DIAGONALS - 1) * BLOCK_TOKENS, HEAD_WIDTH), wk_ref.dtype
    )
    ks = jnp.concatenate(picked_k + [pad], 0)
    vs = jnp.concatenate(picked_v + [pad], 0)
    q = q_ref[...]
    q_stack = jnp.concatenate(
        [q[:, h * HEAD_WIDTH : (h + 1) * HEAD_WIDTH] for h in range(group)], axis=0
    )
    nt = (((1,), (1,)), ((), ()))
    s_slash = lax.dot_general(q_stack, ks, nt, preferred_element_type=jnp.float32)
    s_vert = lax.dot_general(q_stack, kv_ref[0], nt, preferred_element_type=jnp.float32)
    width = s_slash.shape[1]
    row = jnp.bitwise_and(lax.broadcasted_iota(jnp.int32, (rows, width), 0), BLOCK_TOKENS - 1)
    col = lax.broadcasted_iota(jnp.int32, (rows, width), 1)
    ok_slash = (ms_ref[0, 0] > 0) & ((col >= BLOCK_TOKENS) | (col <= row))
    s_slash = jnp.where(ok_slash, s_slash, -jnp.inf)
    s_vert = jnp.where(mv_ref[0, 0] > 0, s_vert, -jnp.inf)
    top = jnp.maximum(
        jnp.max(s_slash, axis=1, keepdims=True), jnp.max(s_vert, axis=1, keepdims=True)
    )
    rate = scale * LOG2_E
    w_slash = jnp.exp2((s_slash - top) * rate)
    w_vert = jnp.exp2((s_vert - top) * rate)
    total = jnp.sum(w_slash, axis=1, keepdims=True) + jnp.sum(w_vert, axis=1, keepdims=True)
    acc = jnp.dot(w_slash.astype(jnp.bfloat16), vs, preferred_element_type=jnp.float32)
    acc = acc + jnp.dot(
        w_vert.astype(jnp.bfloat16), vv_ref[0], preferred_element_type=jnp.float32
    )
    res = (acc / total).astype(o_ref.dtype)
    for h in range(group):
        o_ref[:, h * HEAD_WIDTH : (h + 1) * HEAD_WIDTH] = res[
            h * BLOCK_TOKENS : (h + 1) * BLOCK_TOKENS
        ]


def attend(offsets, q_all, win_k, win_v, kv, vv, ms, mv, group, scale, head, prior):
    nbd = ms.shape[1]
    slash_rows = ms.shape[3]
    vert_rows = kv.shape[1]
    window_rows = win_k.shape[0]
    cols = group * HEAD_WIDTH
    rows = BLOCK_TOKENS * group
    flops = nbd * 4 * rows * (slash_rows + vert_rows) * HEAD_WIDTH
    cost = pl.CostEstimate(
        flops=flops,
        transcendentals=nbd * rows * (slash_rows + vert_rows),
        bytes_accessed=2 * (q_all.size + win_k.size // 2 + kv.size + vv.size),
    )
    kernel = lambda *refs: attend_kernel(*refs, group=group, scale=scale, nbd=nbd, head=head)
    in_specs = [
        pl.BlockSpec((BLOCK_TOKENS, cols), lambda g, i, off: (i, head)),
        pl.BlockSpec((window_rows, HEAD_WIDTH), lambda g, i, off: (0, head)),
        pl.BlockSpec((window_rows, HEAD_WIDTH), lambda g, i, off: (0, head)),
        pl.BlockSpec((1, vert_rows, HEAD_WIDTH), lambda g, i, off: (0, 0, 0)),
        pl.BlockSpec((1, vert_rows, HEAD_WIDTH), lambda g, i, off: (0, 0, 0)),
        pl.BlockSpec((1, 1, 1, slash_rows), lambda g, i, off: (head, i, 0, 0)),
        pl.BlockSpec((1, 1, 1, vert_rows), lambda g, i, off: (head, i, 0, 0)),
    ]
    operands = [offsets, q_all, win_k, win_v, kv, vv, ms, mv]
    aliases = {}
    if prior is not None:
        in_specs.append(pl.BlockSpec(memory_space=pl.ANY))
        aliases = {len(operands): 0}
        operands.append(prior)
    grid_spec = pltpu.PrefetchScalarGridSpec(
        num_scalar_prefetch=1,
        grid=(1, nbd),
        in_specs=in_specs,
        out_specs=pl.BlockSpec((BLOCK_TOKENS, cols), lambda g, i, off: (i, head)),
    )
    return pl.pallas_call(
        kernel,
        grid_spec=grid_spec,
        out_shape=jax.ShapeDtypeStruct(q_all.shape, q_all.dtype),
        cost_estimate=cost,
        input_output_aliases=aliases,
        interpret=INTERPRET,
    )(*operands)


def side_inputs(prev_k, prev_v, k_all, v_all, diagonal_offsets, local_vert, seq_index, nbd):
    kv_local, width = diagonal_offsets.shape
    window_k = jnp.concatenate([prev_k, k_all], 0)
    window_v = jnp.concatenate([prev_v, v_all], 0)
    qblocks = seq_index * nbd + jnp.arange(nbd, dtype=jnp.int32)
    slash_ok, vert_ok = [], []
    for group_member in range(kv_local):
        offset = diagonal_offsets[group_member]
        block_ok = qblocks[:, None] - offset[None, :] >= 0
        block_ok = jnp.concatenate(
            [block_ok, jnp.zeros((nbd, SLASH_SLOTS - width), jnp.bool_)], 1
        )
        slash_ok.append(jnp.repeat(block_ok, BLOCK_TOKENS, axis=1))
        dist = qblocks[:, None] - local_vert[group_member][None, :]
        hit = jnp.any(dist[:, :, None] == offset[None, None, :], axis=2)
        ok = (dist > 0) & jnp.logical_not(hit)
        vert_ok.append(jnp.repeat(ok, BLOCK_TOKENS, axis=1))
    ms = jnp.stack(slash_ok, 0).astype(jnp.int32)[:, :, None, :]
    mv = jnp.stack(vert_ok, 0).astype(jnp.int32)[:, :, None, :]
    return window_k, window_v, ms, mv


def local(queries, keys, values, slash, vertical):
    softmax_scale = HEAD_WIDTH ** (-0.5)
    core_index = lax.axis_index("core")
    seq_index = lax.axis_index("chip") * lax.axis_size("core") + core_index
    head_index = lax.axis_index("head")
    heads = lax.axis_size("head")
    tokens = keys.shape[0]
    joined = jnp.concatenate(
        [keys.reshape(tokens, heads, -1), values.reshape(tokens, heads, -1)], 2
    )
    joined = lax.all_to_all(joined, "head", split_axis=1, concat_axis=0, tiled=True)
    k_cols = keys.shape[1] // heads
    k_all = joined[:, 0, :k_cols]
    v_all = joined[:, 0, k_cols:]
    rows = k_all.shape[0]
    nbd = rows // BLOCK_TOKENS
    kv_local = k_all.shape[1] // HEAD_WIDTH
    query_group = queries.shape[1] // heads // HEAD_WIDTH // kv_local
    width = EXTRA_DIAGONALS + 1
    prev_k, prev_v = shifted((k_all, v_all), ("chip", "core"), 1)
    own_k = k_all.reshape(nbd, BLOCK_TOKENS, kv_local, HEAD_WIDTH)
    own_v = v_all.reshape(nbd, BLOCK_TOKENS, kv_local, HEAD_WIDTH)
    first_head = head_index * kv_local
    local_slash = lax.dynamic_slice_in_dim(slash, first_head, kv_local, 0) + 1
    diagonal_offsets = jnp.concatenate([jnp.zeros((kv_local, 1), jnp.int32), local_slash], 1)
    local_vert = lax.dynamic_slice_in_dim(vertical, first_head, kv_local, 0)
    owner = local_vert // nbd
    inner = local_vert % nbd
    listed = local_vert.shape[1]
    earlier = jnp.arange(listed)[None, :] < jnp.arange(listed)[:, None]
    same_owner = owner[:, :, None] == owner[:, None, :]
    rank = jnp.sum(same_owner & earlier[None], axis=2)
    slots = 2
    mine = (owner == seq_index)[:, None, :] & (rank[:, None, :] == jnp.arange(slots)[None, :, None])
    pick = jnp.sum(jnp.where(mine, inner[:, None, :], 0), axis=2)
    pieces, queries = lax.optimization_barrier((pick, queries))
    chips = lax.axis_size("chip")
    cores = lax.axis_size("core")
    side = int(round(chips ** 0.5))
    chip_index = lax.axis_index("chip")
    swap = [(c, cores - 1 - c) for c in range(cores)]
    heads_col = jnp.arange(kv_local)[:, None]
    mine = jnp.where(core_index == 0, own_k, own_v)[pieces, :, heads_col]
    sent = jnp.where(core_index == 0, own_v, own_k)[pieces, :, heads_col]
    stage = jnp.stack([mine, lax.ppermute(sent, "core", swap)], 0)
    q_all = lax.all_to_all(queries, "head", split_axis=1, concat_axis=0, tiled=True)
    def shift(value, stride, step):
        pairs = []
        for chip in range(chips):
            row, col = chip // side, chip % side
            if stride == 1:
                pairs.append((chip, row * side + (col + step) % side))
            else:
                pairs.append((chip, ((row + step) % side) * side + col))
        return lax.ppermute(value, "chip", pairs)

    def ring(value, stride):
        return jnp.stack([value] + [shift(value, stride, s) for s in range(1, side)], 0)

    across = ring(lax.index_in_dim(stage, 0, 1), 1)
    down = ring(lax.index_in_dim(stage, 1, 1), side)
    across, down, q_all, prev_k, prev_v, diagonal_offsets, local_vert = lax.optimization_barrier(
        (across, down, q_all, prev_k, prev_v, diagonal_offsets, local_vert)
    )
    window_k, window_v, ms, mv = side_inputs(
        prev_k, prev_v, k_all, v_all, diagonal_offsets, local_vert, seq_index, nbd
    )
    across = ring(across, side)
    down = ring(down, 1)
    across, down, window_k, window_v, ms, mv = lax.optimization_barrier(
        (across, down, window_k, window_v, ms, mv)
    )
    owner_chip = owner // cores
    owner_core = owner % cores
    dy = (chip_index // side - owner_chip // side) % side
    dx = (chip_index % side - owner_chip % side) % side
    heads_idx = jnp.arange(kv_local)[:, None]
    dc = (owner_core + core_index) % cores
    gathered = [
        across[dy[0], dx[0], dc[0], 0, rank[0]],
        down[dx[1], dy[1], dc[1], 0, rank[1]],
    ]
    result = None
    for head in range(kv_local):
        part = gathered[head].reshape(1, listed * BLOCK_TOKENS, HEAD_WIDTH)
        other = lax.ppermute(part, "core", swap)
        vert_keys = jnp.where(core_index == 0, part, other)
        vert_vals = jnp.where(core_index == 0, other, part)
        result = attend(
            diagonal_offsets, q_all, window_k, window_v, vert_keys, vert_vals, ms, mv,
            query_group, softmax_scale, head, result,
        )
    return result


def solution(mesh):
    cores = 2
    devices = mesh.devices.reshape(mesh.shape["seq"] // cores, cores, mesh.shape["head"])
    split = Mesh(devices, ("chip", "core", "head"))
    return jax.shard_map(
        local,
        mesh=split,
        in_specs=(
            P(("chip", "core", "head"), None),
            P(("chip", "core", "head"), None),
            P(("chip", "core", "head"), None),
            P(),
            P(),
        ),
        out_specs=P(("chip", "core"), "head"),
        check_vma=False,
    )
```

```python
import jax
import jax.numpy as jnp
from jax import lax
from jax.experimental import pallas as pl
from jax.experimental.pallas import tpu as pltpu
from jax.sharding import Mesh, PartitionSpec as P

HEAD_WIDTH = 128
BLOCK_TOKENS = 64
EXTRA_DIAGONALS = 4
SLASH_SLOTS = 6
LOG2_E = 1.4426950408889634
INTERPRET = False


def shifted(value, axis, by):
    size = lax.axis_size(axis)
    pairs = [(i, i + by) for i in range(size) if 0 <= i + by < size]
    return lax.ppermute(value, axis, pairs)


def attend_kernel(
    off_ref, head_ref, q_ref, wk_ref, wv_ref, kv_ref, vv_ref, ms_ref, mv_ref, *rest, group, scale, nbd
):
    o_ref = rest[-1]
    g = head_ref[0]
    i = pl.program_id(1)
    rows = BLOCK_TOKENS * group
    picked_k, picked_v = [], []
    for j in range(EXTRA_DIAGONALS + 1):
        block = jnp.clip(nbd + i - off_ref[g, j], 0, 2 * nbd - 1)
        start = pl.multiple_of(block * BLOCK_TOKENS, BLOCK_TOKENS)
        picked_k.append(wk_ref[pl.ds(start, BLOCK_TOKENS), :])
        picked_v.append(wv_ref[pl.ds(start, BLOCK_TOKENS), :])
    pad = jnp.zeros(
        ((SLASH_SLOTS - EXTRA_DIAGONALS - 1) * BLOCK_TOKENS, HEAD_WIDTH), wk_ref.dtype
    )
    ks = jnp.concatenate(picked_k + [pad], 0)
    vs = jnp.concatenate(picked_v + [pad], 0)
    q = q_ref[...]
    q_stack = jnp.concatenate(
        [q[:, h * HEAD_WIDTH : (h + 1) * HEAD_WIDTH] for h in range(group)], axis=0
    )
    nt = (((1,), (1,)), ((), ()))
    s_slash = lax.dot_general(q_stack, ks, nt, preferred_element_type=jnp.float32)
    s_vert = lax.dot_general(q_stack, kv_ref[0], nt, preferred_element_type=jnp.float32)
    width = s_slash.shape[1]
    row = jnp.bitwise_and(lax.broadcasted_iota(jnp.int32, (rows, width), 0), BLOCK_TOKENS - 1)
    col = lax.broadcasted_iota(jnp.int32, (rows, width), 1)
    ok_slash = (ms_ref[0, 0] > 0) & ((col >= BLOCK_TOKENS) | (col <= row))
    s_slash = jnp.where(ok_slash, s_slash, -jnp.inf)
    s_vert = jnp.where(mv_ref[0, 0] > 0, s_vert, -jnp.inf)
    top = jnp.maximum(
        jnp.max(s_slash, axis=1, keepdims=True), jnp.max(s_vert, axis=1, keepdims=True)
    )
    rate = scale * LOG2_E
    w_slash = jnp.exp2((s_slash - top) * rate)
    w_vert = jnp.exp2((s_vert - top) * rate)
    total = jnp.sum(w_slash, axis=1, keepdims=True) + jnp.sum(w_vert, axis=1, keepdims=True)
    acc = jnp.dot(w_slash.astype(jnp.bfloat16), vs, preferred_element_type=jnp.float32)
    acc = acc + jnp.dot(
        w_vert.astype(jnp.bfloat16), vv_ref[0], preferred_element_type=jnp.float32
    )
    res = (acc / total).astype(o_ref.dtype)
    for h in range(group):
        o_ref[:, h * HEAD_WIDTH : (h + 1) * HEAD_WIDTH] = res[
            h * BLOCK_TOKENS : (h + 1) * BLOCK_TOKENS
        ]


def attend(offsets, head, q_all, win_k, win_v, kv, vv, ms, mv, group, scale, prior):
    nbd = ms.shape[1]
    slash_rows = ms.shape[3]
    vert_rows = kv.shape[1]
    window_rows = win_k.shape[0]
    cols = group * HEAD_WIDTH
    rows = BLOCK_TOKENS * group
    flops = nbd * 4 * rows * (slash_rows + vert_rows) * HEAD_WIDTH
    cost = pl.CostEstimate(
        flops=flops,
        transcendentals=nbd * rows * (slash_rows + vert_rows),
        bytes_accessed=2 * (q_all.size + win_k.size // 2 + kv.size + vv.size),
    )
    kernel = lambda *refs: attend_kernel(*refs, group=group, scale=scale, nbd=nbd)
    in_specs = [
        pl.BlockSpec((BLOCK_TOKENS, cols), lambda g, i, off, hd: (i, hd[0])),
        pl.BlockSpec((window_rows, HEAD_WIDTH), lambda g, i, off, hd: (0, hd[0])),
        pl.BlockSpec((window_rows, HEAD_WIDTH), lambda g, i, off, hd: (0, hd[0])),
        pl.BlockSpec((1, vert_rows, HEAD_WIDTH), lambda g, i, off, hd: (0, 0, 0)),
        pl.BlockSpec((1, vert_rows, HEAD_WIDTH), lambda g, i, off, hd: (0, 0, 0)),
        pl.BlockSpec((1, 1, 1, slash_rows), lambda g, i, off, hd: (hd[0], i, 0, 0)),
        pl.BlockSpec((1, 1, 1, vert_rows), lambda g, i, off, hd: (hd[0], i, 0, 0)),
    ]
    operands = [offsets, head, q_all, win_k, win_v, kv, vv, ms, mv]
    aliases = {}
    if prior is not None:
        in_specs.append(pl.BlockSpec(memory_space=pl.ANY))
        aliases = {len(operands): 0}
        operands.append(prior)
    grid_spec = pltpu.PrefetchScalarGridSpec(
        num_scalar_prefetch=2,
        grid=(1, nbd),
        in_specs=in_specs,
        out_specs=pl.BlockSpec((BLOCK_TOKENS, cols), lambda g, i, off, hd: (i, hd[0])),
    )
    return pl.pallas_call(
        kernel,
        grid_spec=grid_spec,
        out_shape=jax.ShapeDtypeStruct(q_all.shape, q_all.dtype),
        cost_estimate=cost,
        input_output_aliases=aliases,
        interpret=INTERPRET,
    )(*operands)


def side_inputs(prev_k, prev_v, k_all, v_all, diagonal_offsets, local_vert, seq_index, nbd):
    kv_local, width = diagonal_offsets.shape
    window_k = jnp.concatenate([prev_k, k_all], 0)
    window_v = jnp.concatenate([prev_v, v_all], 0)
    qblocks = seq_index * nbd + jnp.arange(nbd, dtype=jnp.int32)
    slash_ok, vert_ok = [], []
    for group_member in range(kv_local):
        offset = diagonal_offsets[group_member]
        block_ok = qblocks[:, None] - offset[None, :] >= 0
        block_ok = jnp.concatenate(
            [block_ok, jnp.zeros((nbd, SLASH_SLOTS - width), jnp.bool_)], 1
        )
        slash_ok.append(jnp.repeat(block_ok, BLOCK_TOKENS, axis=1))
        dist = qblocks[:, None] - local_vert[group_member][None, :]
        hit = jnp.any(dist[:, :, None] == offset[None, None, :], axis=2)
        ok = (dist > 0) & jnp.logical_not(hit)
        vert_ok.append(jnp.repeat(ok, BLOCK_TOKENS, axis=1))
    ms = jnp.stack(slash_ok, 0).astype(jnp.int32)[:, :, None, :]
    mv = jnp.stack(vert_ok, 0).astype(jnp.int32)[:, :, None, :]
    return window_k, window_v, ms, mv


def local(queries, keys, values, slash, vertical):
    softmax_scale = HEAD_WIDTH ** (-0.5)
    core_index = lax.axis_index("core")
    seq_index = lax.axis_index("chip") * lax.axis_size("core") + core_index
    head_index = lax.axis_index("head")
    heads = lax.axis_size("head")
    tokens = keys.shape[0]
    joined = jnp.concatenate(
        [keys.reshape(tokens, heads, -1), values.reshape(tokens, heads, -1)], 2
    )
    joined = lax.all_to_all(joined, "head", split_axis=1, concat_axis=0, tiled=True)
    k_cols = keys.shape[1] // heads
    k_all = joined[:, 0, :k_cols]
    v_all = joined[:, 0, k_cols:]
    rows = k_all.shape[0]
    nbd = rows // BLOCK_TOKENS
    kv_local = k_all.shape[1] // HEAD_WIDTH
    query_group = queries.shape[1] // heads // HEAD_WIDTH // kv_local
    width = EXTRA_DIAGONALS + 1
    prev_k, prev_v = shifted((k_all, v_all), ("chip", "core"), 1)
    own_k = k_all.reshape(nbd, BLOCK_TOKENS, kv_local, HEAD_WIDTH)
    own_v = v_all.reshape(nbd, BLOCK_TOKENS, kv_local, HEAD_WIDTH)
    first_head = head_index * kv_local
    local_slash = lax.dynamic_slice_in_dim(slash, first_head, kv_local, 0) + 1
    diagonal_offsets = jnp.concatenate([jnp.zeros((kv_local, 1), jnp.int32), local_slash], 1)
    local_vert = lax.dynamic_slice_in_dim(vertical, first_head, kv_local, 0)
    owner = local_vert // nbd
    inner = local_vert % nbd
    listed = local_vert.shape[1]
    earlier = jnp.arange(listed)[None, :] < jnp.arange(listed)[:, None]
    same_owner = owner[:, :, None] == owner[:, None, :]
    rank = jnp.sum(same_owner & earlier[None], axis=2)
    slots = 2
    mine = (owner == seq_index)[:, None, :] & (rank[:, None, :] == jnp.arange(slots)[None, :, None])
    pick = jnp.sum(jnp.where(mine, inner[:, None, :], 0), axis=2)
    pieces, queries = lax.optimization_barrier((pick, queries))
    chips = lax.axis_size("chip")
    cores = lax.axis_size("core")
    side = int(round(chips ** 0.5))
    chip_index = lax.axis_index("chip")
    swap = [(c, cores - 1 - c) for c in range(cores)]
    heads_col = jnp.arange(kv_local)[:, None]
    both = jnp.stack([own_k[pieces, :, heads_col], own_v[pieces, :, heads_col]], 1)
    mine = lax.dynamic_index_in_dim(both, core_index, 0, keepdims=False)
    sent = lax.dynamic_index_in_dim(both, cores - 1 - core_index, 0, keepdims=False)
    stage = jnp.stack([mine, lax.ppermute(sent, "core", swap)], 0)
    q_all = lax.all_to_all(queries, "head", split_axis=1, concat_axis=0, tiled=True)
    def shift(value, stride, step):
        pairs = []
        for chip in range(chips):
            row, col = chip // side, chip % side
            if stride == 1:
                pairs.append((chip, row * side + (col + step) % side))
            else:
                pairs.append((chip, ((row + step) % side) * side + col))
        return lax.ppermute(value, "chip", pairs)

    def ring(value, stride):
        return jnp.stack([value] + [shift(value, stride, s) for s in range(1, side)], 0)

    across = ring(lax.index_in_dim(stage, 0, 1), 1)
    down = ring(lax.index_in_dim(stage, 1, 1), side)
    across, down, q_all, prev_k, prev_v, diagonal_offsets, local_vert = lax.optimization_barrier(
        (across, down, q_all, prev_k, prev_v, diagonal_offsets, local_vert)
    )
    window_k, window_v, ms, mv = side_inputs(
        prev_k, prev_v, k_all, v_all, diagonal_offsets, local_vert, seq_index, nbd
    )
    across = ring(across, side)
    down = ring(down, 1)
    across, down, window_k, window_v, ms, mv = lax.optimization_barrier(
        (across, down, window_k, window_v, ms, mv)
    )
    owner_chip = owner // cores
    owner_core = owner % cores
    dy = (chip_index // side - owner_chip // side) % side
    dx = (chip_index % side - owner_chip % side) % side
    heads_idx = jnp.arange(kv_local)[:, None]
    dc = (owner_core + core_index) % cores
    pick_head = lambda table: lax.dynamic_index_in_dim(table, core_index, 0, keepdims=False)
    dyc, dxc, dcc, rankc = pick_head(dy), pick_head(dx), pick_head(dc), pick_head(rank)
    shape = (1, listed * BLOCK_TOKENS, HEAD_WIDTH)
    own_keys = across[dyc, dxc, dcc, 0, rankc].reshape(shape)
    own_vals = down[dxc, dyc, dcc, 0, rankc].reshape(shape)
    other_keys, other_vals = lax.ppermute((own_keys, own_vals), "core", swap)
    first = jnp.reshape(core_index, (1,)).astype(jnp.int32)
    result = attend(
        diagonal_offsets, first, q_all, window_k, window_v, own_keys, own_vals, ms, mv,
        query_group, softmax_scale, None,
    )
    return attend(
        diagonal_offsets, cores - 1 - first, q_all, window_k, window_v, other_keys, other_vals,
        ms, mv, query_group, softmax_scale, result,
    )


def solution(mesh):
    cores = 2
    devices = mesh.devices.reshape(mesh.shape["seq"] // cores, cores, mesh.shape["head"])
    split = Mesh(devices, ("chip", "core", "head"))
    return jax.shard_map(
        local,
        mesh=split,
        in_specs=(
            P(("chip", "core", "head"), None),
            P(("chip", "core", "head"), None),
            P(("chip", "core", "head"), None),
            P(),
            P(),
        ),
        out_specs=P(("chip", "core"), "head"),
        check_vma=False,
    )
```
